32 devices in a mesh: ctx: 8 (over z, core), tp: 4 (over y, x).
Axes of the slice: x: 2, y: 2, z: 4, core: 2. Of those that a mesh axis runs over, the one named last changes fastest.
Arguments:
- x_in: bfloat16 [4096, 8192], P(('ctx', 'tp')), may hold values from -6 to 6
- bc_in: bfloat16 [4096, 2048], P(('ctx', 'tp')), may hold values from -6 to 6
- dt_in: bfloat16 [4096, 128], P(('ctx', 'tp')), may hold values from -3 to 3
- conv_x_weight: float32 [4, 8192], replicated, may hold values from -3 to 3
- conv_x_bias: float32 [8192], replicated, may hold values from -0.8 to -0.2
- conv_bc_weight: float32 [4, 2048], replicated, may hold values from -3 to 3
- conv_bc_bias: float32 [2048], replicated, may hold values from -0.8 to -0.2
- dt_bias: float32 [128], replicated, as said below
- a_log: float32 [128], replicated, as said below
- skip: float32 [128], replicated, may hold values from 0.5 to 1.5
Outputs:
- scan_out: bfloat16 [4096, 8192], P(('ctx', 'tp'))
The draws below stay inside these ranges and needn't reach their ends.
Inputs may be any that keep to these rules, and one draw needn't show every extreme that they name: `dt_bias`: one value for each head. `a_log`: one value for each head.
All inputs are finite; a program needn't handle non-finite values.
Results may differ from the reference program's by a relative error of at most 0.0051.
Values may be sent and summed in bfloat16 or wider, within the bound.
No kernel may reach another device: no remote copies, remote signals or barrier semaphores. Data moves between devices by JAX's collectives and lax.ppermute only.
A program may use at most 128 MiB of HBM per device.

```python
import jax
import jax.numpy as jnp
from jax import lax

H = 128
P_SIZE = 64
N = 256
G = 4
CONV = 4
BLOCK = 512
TOKENS = 4096


def head_law(key):
    share = 0.5
    pick = jax.random.uniform(jax.random.fold_in(key, 11), (H,))
    first = jax.random.uniform(jax.random.fold_in(key, 12), (H,))
    second = jax.random.uniform(jax.random.fold_in(key, 13), (H,))
    fast = pick < share
    length = jnp.float32(TOKENS)
    fast_rate = jnp.exp(jnp.log(1.0 / 50.0) + first * jnp.log(50.0 / 30.0))
    fast_dt = jnp.exp(jnp.log(0.07) + second * jnp.log(0.3 / 0.07))
    slow_total = jnp.exp(jnp.log(0.1) + first * jnp.log(10.0))
    slow_dt = jnp.exp(jnp.log(0.7) + second * jnp.log(2.0 / 0.7)) / jnp.sqrt(length)
    target = jnp.where(fast, fast_dt, slow_dt)
    magnitude = jnp.where(fast, fast_rate / fast_dt, slow_total / (slow_dt * length))
    return (jnp.log(magnitude).astype(jnp.float32), jnp.log(jnp.expm1(target)).astype(jnp.float32))


def draw_a_log(key, part):
    return head_law(key)[0]


def draw_dt_bias(key, part):
    return head_law(key)[1]


def level_of(own_key, extent, pieces, low, top_value):
    level, own = 1.0, jax.random.fold_in(own_key, 6)
    for position, parts in pieces:
        heights = jnp.exp(jax.random.uniform(jax.random.fold_in(own, position), (parts,), jnp.float32, low / len(pieces), top_value / len(pieces)))
        level = level * jnp.repeat(heights, extent[position] // parts).reshape([-1 if axis == position else 1 for axis in range(len(extent))])
    return level


def bell_draw(key, dims, deviation, reach, cuts=(), kind=jnp.bfloat16):
    values = jax.random.normal(key, dims, jnp.float32) * deviation
    if len(cuts) > 0:
        values = level_of(key, dims, cuts, -0.22, 0.18) * values
    return jnp.clip(values, min=-reach, max=reach).astype(kind)


def setup_inputs(seed: int = 0) -> dict:
    key_of = jax.random.split(jax.random.key(seed), 11)
    x_in = bell_draw(key_of[0], (TOKENS, H * P_SIZE), 1.0, 6.0, ((0, 32),))
    bc_in = bell_draw(key_of[1], (TOKENS, 2 * G * N), 1.0, 6.0, ((0, 32),))
    dt_in = bell_draw(key_of[2], (TOKENS, H), 0.7, 3.0, ((0, 32),))
    conv_x_weight = bell_draw(key_of[3], (CONV, H * P_SIZE), CONV ** -0.5, 3.0, (), jnp.float32)
    conv_x_bias = jnp.clip(jax.random.uniform(key_of[4], (H * P_SIZE,), jnp.float32, -0.8, -0.2), -0.8, -0.2)
    conv_bc_weight = bell_draw(key_of[5], (CONV, 2 * G * N), CONV ** -0.5, 3.0, (), jnp.float32)
    conv_bc_bias = jnp.clip(jax.random.uniform(key_of[6], (2 * G * N,), jnp.float32, -0.8, -0.2), -0.8, -0.2)
    dt_bias = draw_dt_bias(jax.random.fold_in(key_of[10], 71), 0)
    a_log = draw_a_log(jax.random.fold_in(key_of[10], 71), 0)
    skip = jnp.clip(jax.random.uniform(key_of[9], (H,), jnp.float32, 0.5, 1.5), 0.5, 1.5)
    return dict(x_in=x_in, bc_in=bc_in, dt_in=dt_in, conv_x_weight=conv_x_weight, conv_x_bias=conv_x_bias, conv_bc_weight=conv_bc_weight, conv_bc_bias=conv_bc_bias, dt_bias=dt_bias, a_log=a_log, skip=skip)


def conv_silu(raw, weight, bias):
    rows = raw.shape[0]
    prior = jnp.zeros((CONV - 1, raw.shape[1]), jnp.float32)
    full = jnp.concatenate([prior, raw.astype(jnp.float32)], axis=0)
    total = bias[None, :] + weight[0][None, :] * full[0:rows]
    for k in range(1, CONV):
        total = total + weight[k][None, :] * full[k:k + rows]
    return jax.nn.silu(total).astype(jnp.bfloat16)


def reference(x_in, bc_in, dt_in, conv_x_weight, conv_x_bias, conv_bc_weight, conv_bc_bias, dt_bias, a_log, skip):
    xc = conv_silu(x_in, conv_x_weight, conv_x_bias)
    bcc = conv_silu(bc_in, conv_bc_weight, conv_bc_bias)
    dt = jax.nn.softplus(dt_in.astype(jnp.float32) + dt_bias[None, :])
    log_decay = -dt * jnp.exp(a_log)[None, :]
    blocks = TOKENS // BLOCK
    per_group = H // G
    xs = xc.reshape(blocks, BLOCK, H, P_SIZE)
    bs = bcc[:, :G * N].reshape(blocks, BLOCK, G, N)
    cs = bcc[:, G * N:].reshape(blocks, BLOCK, G, N)
    dts = dt.reshape(blocks, BLOCK, H)
    logs = log_decay.reshape(blocks, BLOCK, H)
    mask = jnp.tril(jnp.ones((BLOCK, BLOCK), dtype=bool))

    def step(state, blk):
        xb, bb, cb, db, lb = blk
        cum = jnp.cumsum(lb, axis=0)
        scores = jnp.einsum('ign,jgn->gij', cb.astype(jnp.float32), bb.astype(jnp.float32))
        scores = jnp.repeat(scores, per_group, axis=0)
        ct = cum.T
        diff = ct[:, :, None] - ct[:, None, :]
        decay = jnp.where(mask[None], jnp.exp(jnp.where(mask[None], diff, 0.0)), 0.0)
        weights = (scores * decay * db.T[:, None, :]).astype(jnp.bfloat16)
        xf = xb.astype(jnp.float32)
        intra = jnp.einsum('hij,jhp->ihp', weights.astype(jnp.float32), xf)
        last = cum[-1]
        wx = ((jnp.exp(last[None, :] - cum) * db)[:, :, None] * xf).astype(jnp.bfloat16)
        bh = jnp.repeat(bb, per_group, axis=1).astype(jnp.float32)
        ch = jnp.repeat(cb, per_group, axis=1).astype(jnp.float32)
        local = jnp.einsum('jhn,jhp->hnp', bh, wx.astype(jnp.float32))
        inter = jnp.exp(cum)[:, :, None] * jnp.einsum('ihn,hnp->ihp', ch, state, precision=lax.Precision.HIGHEST)
        out = (intra + inter + skip[None, :, None] * xf).astype(jnp.bfloat16)
        new_state = jnp.exp(last)[:, None, None] * state + local
        return new_state, out

    start = jnp.zeros((H, N, P_SIZE), jnp.float32)
    final, outs = lax.scan(step, start, (xs, bs, cs, dts, logs))
    return outs.reshape(TOKENS, H * P_SIZE)
```

```python
import numpy as np
import jax
import jax.numpy as jnp
from jax import lax
from jax.sharding import PartitionSpec as P

H = 128
P_SIZE = 64
N = 256
G = 4
CONV = 4
BLOCK = 512


def from_behind(value, axis, steps):
    count = lax.axis_size(axis)
    initial, last = (max(0, -steps), min(count, count - steps))
    return lax.ppermute(value, axis, [(source, source + steps) for source in range(initial, last)])


def conv_silu(raw, prior, weight, bias):
    rows = raw.shape[0]
    full = jnp.concatenate([prior, raw], axis=0).astype(jnp.float32)
    total = bias[None, :] + weight[0][None, :] * full[0:rows]
    for k in range(1, CONV):
        total = total + weight[k][None, :] * full[k : k + rows]
    return jax.nn.silu(total).astype(jnp.bfloat16)


def head_columns(head_major):
    return jnp.repeat(head_major, P_SIZE, axis=-1)


def on_device(
    x_in,
    bc_in,
    dt_in,
    conv_x_weight,
    conv_x_bias,
    conv_bc_weight,
    conv_bc_bias,
    dt_bias,
    a_log,
    skip,
):
    n_tp = lax.axis_size("tp")
    tp_index = lax.axis_index("tp")
    n_ctx = lax.axis_size("ctx")
    ctx_index = lax.axis_index("ctx")
    rows = x_in.shape[0]
    local_heads = H // n_tp
    head_width = local_heads * P_SIZE
    per_group = H // G
    rim = CONV - 1

    prior_x, prior_bc = from_behind((x_in[rows - rim :], bc_in[rows - rim :]), ("ctx", "tp"), 1)
    x_part = conv_silu(x_in, prior_x, conv_x_weight, conv_x_bias)
    bc_part = conv_silu(bc_in, prior_bc, conv_bc_weight, conv_bc_bias)

    group_of = [(k * local_heads) // per_group for k in range(n_tp)]
    bc_groups = bc_part.reshape(rows, 2, G, N)
    if group_of != list(range(G)):
        bc_groups = jnp.take(bc_groups, np.array(group_of), axis=2)
    bc_groups = jnp.transpose(bc_groups, (2, 0, 1, 3))
    seg_bc = lax.all_to_all(bc_groups, "tp", split_axis=0, concat_axis=0, tiled=True)
    seg_bc = seg_bc.reshape(n_tp * rows, 2, N)
    seg_x = lax.all_to_all(x_part, "tp", split_axis=1, concat_axis=0, tiled=True)
    seg_dt = lax.all_to_all(dt_in, "tp", split_axis=1, concat_axis=0, tiled=True)
    seg_len = seg_x.shape[0]
    blocks = seg_len // BLOCK
    seg_b = seg_bc[:, 0].reshape(blocks, BLOCK, N)
    seg_c = seg_bc[:, 1].reshape(blocks, BLOCK, N)

    bias_local = lax.dynamic_slice_in_dim(dt_bias, tp_index * local_heads, local_heads, 0)
    rate_local = lax.dynamic_slice_in_dim(a_log, tp_index * local_heads, local_heads, 0)
    skip_local = lax.dynamic_slice_in_dim(skip, tp_index * local_heads, local_heads, 0)
    step_size = jax.nn.softplus(seg_dt.astype(jnp.float32) + bias_local[None, :])
    log_decay = -step_size * jnp.exp(rate_local)[None, :]

    dt_blk = step_size.reshape(blocks, BLOCK, local_heads)
    cum = jnp.cumsum(log_decay.reshape(blocks, BLOCK, local_heads), axis=1)
    last = cum[:, -1]
    x_blk = seg_x.reshape(blocks, BLOCK, head_width)
    x_float = x_blk.astype(jnp.float32)

    wx = (head_columns(jnp.exp(last[:, None, :] - cum) * dt_blk) * x_float).astype(jnp.bfloat16)
    fresh = jnp.einsum("bjn,bjk->bnk", seg_b, wx, preferred_element_type=jnp.float32)
    block_decay = jnp.exp(last)
    starts = [None]
    state = fresh[0]
    prefix = [jnp.ones((local_heads,), jnp.float32)]
    for b in range(1, blocks):
        starts.append(state)
        prefix.append(prefix[-1] * block_decay[b - 1])
        state = head_columns(block_decay[b])[None, :] * state + fresh[b]
    final = state
    segment_decay = prefix[-1] * block_decay[blocks - 1]

    core = ctx_index % 2
    chip = ctx_index // 2
    chips = n_ctx // 2
    half_width = head_width // 2
    half_heads = local_heads // 2
    decays = lax.all_gather(segment_decay, "ctx")
    mate_final = lax.ppermute(final, "ctx", [(i, i ^ 1) for i in range(n_ctx)])
    even_final = jnp.where(core == 0, final, mate_final)
    odd_final = jnp.where(core == 0, mate_final, final)
    odd_decay = lax.dynamic_index_in_dim(decays, chip * 2 + 1, 0, False)
    lo = core * half_width
    chip_half = head_columns(lax.dynamic_slice_in_dim(odd_decay, core * half_heads, half_heads, 0))[
        None, :
    ] * lax.dynamic_slice_in_dim(even_final, lo, half_width, 1) + lax.dynamic_slice_in_dim(
        odd_final, lo, half_width, 1
    )
    gathered = lax.all_gather(chip_half, "ctx")

    lower_mask = jnp.tril(jnp.ones((BLOCK, BLOCK), dtype=bool))
    cum_t = jnp.transpose(cum, (0, 2, 1))
    dt_t = jnp.transpose(dt_blk, (0, 2, 1))
    partials = []
    for b in range(blocks):
        scores = jnp.einsum("in,jn->ij", seg_c[b], seg_b[b], preferred_element_type=jnp.float32)
        gap_log = cum_t[b][:, :, None] - cum_t[b][:, None, :]
        decay = jnp.where(lower_mask[None], jnp.exp(jnp.where(lower_mask[None], gap_log, 0.0)), 0.0)
        weights = (scores[None] * decay * dt_t[b][:, None, :]).astype(jnp.bfloat16)
        intra = jnp.einsum(
            "hij,jhp->ihp",
            weights,
            x_blk[b].reshape(BLOCK, local_heads, P_SIZE),
            preferred_element_type=jnp.float32,
        ).reshape(BLOCK, head_width)
        partials.append(intra + head_columns(skip_local)[None, :] * x_float[b])

    seg_ids = jnp.arange(n_ctx)[None, :]
    chip_ids = jnp.arange(chips)[:, None]
    between = (seg_ids >= 2 * chip_ids + 2) & (seg_ids < ctx_index)
    chip_weight = jnp.prod(jnp.where(between[:, :, None], decays[None], 1.0), axis=1)
    chip_weight = jnp.where(chip_ids < chip, chip_weight, 0.0)
    halves = []
    for q in range(2):
        part = gathered[q::2]
        wq = head_columns(chip_weight[:, q * half_heads : (q + 1) * half_heads])
        halves.append(jnp.sum(wq[:, None, :] * part, axis=0))
    incoming = jnp.concatenate(halves, axis=1) + jnp.where(core == 1, 1.0, 0.0) * even_final

    results = []
    for b in range(blocks):
        carried_state = head_columns(prefix[b])[None, :] * incoming
        if starts[b] is not None:
            carried_state = starts[b] + carried_state
        inter = head_columns(jnp.exp(cum[b])) * jnp.dot(
            seg_c[b].astype(jnp.float32), carried_state, precision=lax.Precision.HIGHEST
        )
        results.append((partials[b] + inter).astype(jnp.bfloat16))
    result = jnp.concatenate(results, axis=0) if blocks > 1 else results[0]
    return lax.all_to_all(result, "tp", split_axis=0, concat_axis=1, tiled=True)


def solution(mesh):
    return jax.shard_map(
        on_device,
        mesh=mesh,
        in_specs=(
            P(("ctx", "tp"), None),
            P(("ctx", "tp"), None),
            P(("ctx", "tp"), None),
            P(),
            P(),
            P(),
            P(),
            P(),
            P(),
            P(),
        ),
        out_specs=P(("ctx", "tp"), None),
        check_vma=False,
    )
```

```python
import numpy as np
import jax
import jax.numpy as jnp
from jax import lax
from jax.sharding import PartitionSpec as P
from jax.experimental import pallas as pl
from jax.experimental.pallas import tpu as pltpu

H = 128
P_SIZE = 64
N = 256
G = 4
CONV = 4
BLOCK = 512


def from_behind(value, axis, steps):
    count = lax.axis_size(axis)
    initial, last = (max(0, -steps), min(count, count - steps))
    return lax.ppermute(value, axis, [(source, source + steps) for source in range(initial, last)])


def conv_rows(full, rows, weight, bias):
    total = bias[None, :] + weight[0][None, :] * full[0:rows]
    for k in range(1, CONV):
        total = total + weight[k][None, :] * full[k : k + rows]
    return jax.nn.silu(total).astype(jnp.bfloat16)


def conv_silu(raw, prior, weight, bias):
    rows = raw.shape[0]
    rim = CONV - 1
    zero_prior = jnp.zeros((rim, raw.shape[1]), jnp.float32)
    body = conv_rows(jnp.concatenate([zero_prior, raw.astype(jnp.float32)], axis=0), rows, weight, bias)
    edge = jnp.concatenate([prior, raw[:rim]], axis=0).astype(jnp.float32)
    return lax.dynamic_update_slice_in_dim(body, conv_rows(edge, rim, weight, bias), 0, 0)


def intra_kernel(x_ref, s_ref, cum_ref, cumt_ref, dtt_ref, skip_ref, o_ref):
    tiles = BLOCK // 128
    lane_head = lax.broadcasted_iota(jnp.int32, cum_ref.shape, 1)
    row_head = lax.broadcasted_iota(jnp.int32, cumt_ref.shape, 0)
    lane = lax.broadcasted_iota(jnp.int32, (128, 128), 1)

    def pair(p, carry):
        off = pl.multiple_of(p * 128, 128)
        xp = x_ref[:, pl.ds(off, 128)]
        cum_all = cum_ref[...]
        cumt_all = cumt_ref[...]
        dtt_all = dtt_ref[...]
        cols, rows, dts = [], [], []
        for k in range(2):
            h = 2 * p + k
            cols.append(jnp.sum(jnp.where(lane_head == h, cum_all, 0.0), axis=1, keepdims=True))
            rows.append(jnp.sum(jnp.where(row_head == h, cumt_all, 0.0), axis=0, keepdims=True))
            dts.append(jnp.sum(jnp.where(row_head == h, dtt_all, 0.0), axis=0, keepdims=True))
        skip_p = skip_ref[:, pl.ds(off, 128)]
        for r in range(tiles):
            width = (r + 1) * 128
            s_tile = s_ref[r * 128 : width, 0:width]
            lower = lax.broadcasted_iota(jnp.int32, (128, width), 1) <= (
                lax.broadcasted_iota(jnp.int32, (128, width), 0) + r * 128
            )
            res = []
            for k in range(2):
                gap = cols[k][r * 128 : width] - rows[k][:, 0:width]
                decay = jnp.where(lower, jnp.exp(jnp.where(lower, gap, 0.0)), 0.0)
                w = (s_tile * decay * dts[k][:, 0:width]).astype(jnp.bfloat16)
                res.append(jnp.dot(w, xp[0:width], preferred_element_type=jnp.float32))
            out = jnp.where(lane < P_SIZE, res[0], res[1])
            o_ref[r * 128 : width, pl.ds(off, 128)] = out + skip_p * xp[r * 128 : width].astype(jnp.float32)
        return carry

    lax.fori_loop(0, x_ref.shape[1] // 128, pair, 0)


def intra_block(x, scores, cum, dt, skip_cols):
    heads = cum.shape[1]
    width = x.shape[1]
    cum_lanes = jnp.pad(cum, ((0, 0), (0, 128 - heads)))
    pad_rows = (-heads) % 8
    cum_rows = jnp.pad(cum.T, ((0, pad_rows), (0, 0)))
    dt_rows = jnp.pad(dt.T, ((0, pad_rows), (0, 0)))
    vmem = pl.BlockSpec(memory_space=pltpu.VMEM)
    return pl.pallas_call(
        intra_kernel,
        out_shape=jax.ShapeDtypeStruct((BLOCK, width), jnp.float32),
        in_specs=[vmem] * 6,
        out_specs=vmem,
        name="ssd_intra",
        cost_estimate=pl.CostEstimate(
            flops=2 * BLOCK * BLOCK * width * 2,
            transcendentals=heads * BLOCK * BLOCK,
            bytes_accessed=BLOCK * width * 6 + BLOCK * BLOCK * 4,
        ),
    )(x, scores, cum_lanes, cum_rows, dt_rows, skip_cols[None, :])


def head_columns(head_major):
    return jnp.repeat(head_major, P_SIZE, axis=-1)


def on_device(
    x_in,
    bc_in,
    dt_in,
    conv_x_weight,
    conv_x_bias,
    conv_bc_weight,
    conv_bc_bias,
    dt_bias,
    a_log,
    skip,
):
    n_tp = lax.axis_size("tp")
    tp_index = lax.axis_index("tp")
    n_ctx = lax.axis_size("ctx")
    ctx_index = lax.axis_index("ctx")
    rows = x_in.shape[0]
    local_heads = H // n_tp
    head_width = local_heads * P_SIZE
    per_group = H // G
    rim = CONV - 1

    prior_x, prior_bc = from_behind((x_in[rows - rim :], bc_in[rows - rim :]), ("ctx", "tp"), 1)
    x_part = conv_silu(x_in, prior_x, conv_x_weight, conv_x_bias)
    bc_part = conv_silu(bc_in, prior_bc, conv_bc_weight, conv_bc_bias)

    group_of = [(k * local_heads) // per_group for k in range(n_tp)]
    bc_groups = bc_part.reshape(rows, 2, G, N)
    if group_of != list(range(G)):
        bc_groups = jnp.take(bc_groups, np.array(group_of), axis=2)
    bc_groups = jnp.transpose(bc_groups, (2, 0, 1, 3))
    seg_bc = lax.all_to_all(bc_groups, "tp", split_axis=0, concat_axis=0, tiled=True)
    seg_bc = seg_bc.reshape(n_tp * rows, 2, N)
    seg_x = lax.all_to_all(x_part, "tp", split_axis=1, concat_axis=0, tiled=True)
    seg_dt = lax.all_to_all(dt_in, "tp", split_axis=1, concat_axis=0, tiled=True)
    seg_len = seg_x.shape[0]
    blocks = seg_len // BLOCK
    seg_b = seg_bc[:, 0].reshape(blocks, BLOCK, N)
    seg_c = seg_bc[:, 1].reshape(blocks, BLOCK, N)

    bias_local = lax.dynamic_slice_in_dim(dt_bias, tp_index * local_heads, local_heads, 0)
    rate_local = lax.dynamic_slice_in_dim(a_log, tp_index * local_heads, local_heads, 0)
    skip_local = lax.dynamic_slice_in_dim(skip, tp_index * local_heads, local_heads, 0)
    step_size = jax.nn.softplus(seg_dt.astype(jnp.float32) + bias_local[None, :])
    log_decay = -step_size * jnp.exp(rate_local)[None, :]

    dt_blk = step_size.reshape(blocks, BLOCK, local_heads)
    cum = jnp.cumsum(log_decay.reshape(blocks, BLOCK, local_heads), axis=1)
    last = cum[:, -1]
    x_blk = seg_x.reshape(blocks, BLOCK, head_width)
    x_float = x_blk.astype(jnp.float32)

    wx = (head_columns(jnp.exp(last[:, None, :] - cum) * dt_blk) * x_float).astype(jnp.bfloat16)
    fresh = jnp.einsum("bjn,bjk->bnk", seg_b, wx, preferred_element_type=jnp.float32)
    block_decay = jnp.exp(last)
    starts = [None]
    state = fresh[0]
    prefix = [jnp.ones((local_heads,), jnp.float32)]
    for b in range(1, blocks):
        starts.append(state)
        prefix.append(prefix[-1] * block_decay[b - 1])
        state = head_columns(block_decay[b])[None, :] * state + fresh[b]
    final = state
    segment_decay = prefix[-1] * block_decay[blocks - 1]

    core = ctx_index % 2
    chip = ctx_index // 2
    chips = n_ctx // 2
    half_width = head_width // 2
    half_heads = local_heads // 2
    decay_slab = jnp.pad(segment_decay[None, :], ((0, 7), (0, head_width - local_heads)))
    mate = lax.ppermute(
        jnp.concatenate([final, decay_slab], axis=0), "ctx", [(i, i ^ 1) for i in range(n_ctx)]
    )
    mate_final = mate[:N]
    even_final = jnp.where(core == 0, final, mate_final)
    odd_final = jnp.where(core == 0, mate_final, final)
    odd_decay = jnp.where(core == 0, mate[N, :local_heads], segment_decay)
    lo = core * half_width
    chip_half = head_columns(lax.dynamic_slice_in_dim(odd_decay, core * half_heads, half_heads, 0))[
        None, :
    ] * lax.dynamic_slice_in_dim(even_final, lo, half_width, 1) + lax.dynamic_slice_in_dim(
        odd_final, lo, half_width, 1
    )
    gathered = lax.all_gather(
        jnp.concatenate([chip_half, decay_slab[:, :half_width]], axis=0), "ctx"
    )
    decays = gathered[:, N, :local_heads]

    skip_cols = head_columns(skip_local)
    partials = []
    for b in range(blocks):
        scores = jnp.einsum("in,jn->ij", seg_c[b], seg_b[b], preferred_element_type=jnp.float32)
        partials.append(intra_block(x_blk[b], scores, cum[b], dt_blk[b], skip_cols))

    seg_ids = jnp.arange(n_ctx)[None, :]
    chip_ids = jnp.arange(chips)[:, None]
    between = (seg_ids >= 2 * chip_ids + 2) & (seg_ids < ctx_index)
    chip_weight = jnp.prod(jnp.where(between[:, :, None], decays[None], 1.0), axis=1)
    chip_weight = jnp.where(chip_ids < chip, chip_weight, 0.0)
    halves = []
    for q in range(2):
        part = gathered[q::2, :N]
        wq = head_columns(chip_weight[:, q * half_heads : (q + 1) * half_heads])
        halves.append(jnp.sum(wq[:, None, :] * part, axis=0))
    incoming = jnp.concatenate(halves, axis=1) + jnp.where(core == 1, 1.0, 0.0) * even_final

    results = []
    for b in range(blocks):
        carried_state = head_columns(prefix[b])[None, :] * incoming
        if starts[b] is not None:
            carried_state = starts[b] + carried_state
        inter = head_columns(jnp.exp(cum[b])) * jnp.dot(
            seg_c[b].astype(jnp.float32), carried_state, precision=lax.Precision.HIGHEST
        )
        results.append((partials[b] + inter).astype(jnp.bfloat16))
    result = jnp.concatenate(results, axis=0) if blocks > 1 else results[0]
    return lax.all_to_all(result, "tp", split_axis=0, concat_axis=1, tiled=True)


def solution(mesh):
    return jax.shard_map(
        on_device,
        mesh=mesh,
        in_specs=(
            P(("ctx", "tp"), None),
            P(("ctx", "tp"), None),
            P(("ctx", "tp"), None),
            P(),
            P(),
            P(),
            P(),
            P(),
            P(),
            P(),
        ),
        out_specs=P(("ctx", "tp"), None),
        check_vma=False,
    )
```

```python
import numpy as np
import jax
import jax.numpy as jnp
from jax import lax
from jax.sharding import PartitionSpec as P
from jax.experimental import pallas as pl
from jax.experimental.pallas import tpu as pltpu

H = 128
P_SIZE = 64
N = 256
G = 4
CONV = 4
BLOCK = 512


def from_behind(value, axis, steps):
    count = lax.axis_size(axis)
    initial, last = (max(0, -steps), min(count, count - steps))
    return lax.ppermute(value, axis, [(source, source + steps) for source in range(initial, last)])


def conv_rows(full, rows, weight, bias):
    total = bias[None, :] + weight[0][None, :] * full[0:rows]
    for k in range(1, CONV):
        total = total + weight[k][None, :] * full[k : k + rows]
    return jax.nn.silu(total).astype(jnp.bfloat16)


def conv_silu(raw, prior, weight, bias):
    rows = raw.shape[0]
    rim = CONV - 1
    zero_prior = jnp.zeros((rim, raw.shape[1]), jnp.float32)
    body = conv_rows(jnp.concatenate([zero_prior, raw.astype(jnp.float32)], axis=0), rows, weight, bias)
    edge = jnp.concatenate([prior, raw[:rim]], axis=0).astype(jnp.float32)
    return lax.dynamic_update_slice_in_dim(body, conv_rows(edge, rim, weight, bias), 0, 0)


def intra_kernel(x_ref, s_ref, cum_ref, cumt_ref, dtt_ref, skip_ref, o_ref):
    tiles = BLOCK // 128
    lane_head = lax.broadcasted_iota(jnp.int32, cum_ref.shape, 1)
    row_head = lax.broadcasted_iota(jnp.int32, cumt_ref.shape, 0)
    lane = lax.broadcasted_iota(jnp.int32, (128, 128), 1)

    def pair(p, carry):
        off = pl.multiple_of(p * 128, 128)
        xp = x_ref[:, pl.ds(off, 128)]
        cum_all = cum_ref[...]
        cumt_all = cumt_ref[...]
        dtt_all = dtt_ref[...]
        cols, rows, dts = [], [], []
        for k in range(2):
            h = 2 * p + k
            cols.append(jnp.sum(jnp.where(lane_head == h, cum_all, 0.0), axis=1, keepdims=True))
            rows.append(jnp.sum(jnp.where(row_head == h, cumt_all, 0.0), axis=0, keepdims=True))
            dts.append(jnp.sum(jnp.where(row_head == h, dtt_all, 0.0), axis=0, keepdims=True))
        skip_p = skip_ref[:, pl.ds(off, 128)]
        for r in range(tiles):
            width = (r + 1) * 128
            s_tile = s_ref[r * 128 : width, 0:width]
            lower = lax.broadcasted_iota(jnp.int32, (128, width), 1) <= (
                lax.broadcasted_iota(jnp.int32, (128, width), 0) + r * 128
            )
            res = []
            for k in range(2):
                gap = cols[k][r * 128 : width] - rows[k][:, 0:width]
                decay = jnp.where(lower, jnp.exp(jnp.where(lower, gap, 0.0)), 0.0)
                w = (s_tile * decay * dts[k][:, 0:width]).astype(jnp.bfloat16)
                res.append(jnp.dot(w, xp[0:width], preferred_element_type=jnp.float32))
            out = jnp.where(lane < P_SIZE, res[0], res[1])
            o_ref[r * 128 : width, pl.ds(off, 128)] = out + skip_p * xp[r * 128 : width].astype(jnp.float32)
        return carry

    lax.fori_loop(0, x_ref.shape[1] // 128, pair, 0)


def intra_block(x, scores, cum, dt, skip_cols):
    heads = cum.shape[1]
    width = x.shape[1]
    cum_lanes = jnp.pad(cum, ((0, 0), (0, 128 - heads)))
    pad_rows = (-heads) % 8
    cum_rows = jnp.pad(cum.T, ((0, pad_rows), (0, 0)))
    dt_rows = jnp.pad(dt.T, ((0, pad_rows), (0, 0)))
    vmem = pl.BlockSpec(memory_space=pltpu.VMEM)
    return pl.pallas_call(
        intra_kernel,
        out_shape=jax.ShapeDtypeStruct((BLOCK, width), jnp.float32),
        in_specs=[vmem] * 6,
        out_specs=vmem,
        name="ssd_intra",
        cost_estimate=pl.CostEstimate(
            flops=2 * BLOCK * BLOCK * width * 2,
            transcendentals=heads * BLOCK * BLOCK,
            bytes_accessed=BLOCK * width * 6 + BLOCK * BLOCK * 4,
        ),
    )(x, scores, cum_lanes, cum_rows, dt_rows, skip_cols[None, :])


def fresh_kernel(x_ref, bt_ref, cum_ref, dtl_ref, o_ref):
    lane_head = lax.broadcasted_iota(jnp.int32, cum_ref.shape, 1)
    lane = lax.broadcasted_iota(jnp.int32, (BLOCK, 128), 1)

    def pair(p, carry):
        off = pl.multiple_of(p * 128, 128)
        xp = x_ref[:, pl.ds(off, 128)].astype(jnp.float32)
        cum_all = cum_ref[...]
        dt_all = dtl_ref[...]
        factors = []
        for k in range(2):
            h = 2 * p + k
            c = jnp.sum(jnp.where(lane_head == h, cum_all, 0.0), axis=1, keepdims=True)
            d = jnp.sum(jnp.where(lane_head == h, dt_all, 0.0), axis=1, keepdims=True)
            factors.append(jnp.exp(c[BLOCK - 1 : BLOCK] - c) * d)
        wx = (jnp.where(lane < P_SIZE, factors[0], factors[1]) * xp).astype(jnp.bfloat16)
        o_ref[:, pl.ds(off, 128)] = jnp.dot(bt_ref[...], wx, preferred_element_type=jnp.float32)
        return carry

    lax.fori_loop(0, x_ref.shape[1] // 128, pair, 0)


def fresh_block(x, b, cum, dt):
    heads = cum.shape[1]
    width = x.shape[1]
    cum_lanes = jnp.pad(cum, ((0, 0), (0, 128 - heads)))
    dt_lanes = jnp.pad(dt, ((0, 0), (0, 128 - heads)))
    vmem = pl.BlockSpec(memory_space=pltpu.VMEM)
    return pl.pallas_call(
        fresh_kernel,
        out_shape=jax.ShapeDtypeStruct((N, width), jnp.float32),
        in_specs=[vmem] * 4,
        out_specs=vmem,
        name="ssd_fresh",
        cost_estimate=pl.CostEstimate(
            flops=2 * BLOCK * N * width,
            transcendentals=heads * BLOCK,
            bytes_accessed=BLOCK * width * 2 + N * width * 4 + BLOCK * N * 2,
        ),
    )(x, b.T, cum_lanes, dt_lanes)


def head_columns(head_major):
    return jnp.repeat(head_major, P_SIZE, axis=-1)


def on_device(
    x_in,
    bc_in,
    dt_in,
    conv_x_weight,
    conv_x_bias,
    conv_bc_weight,
    conv_bc_bias,
    dt_bias,
    a_log,
    skip,
):
    n_tp = lax.axis_size("tp")
    tp_index = lax.axis_index("tp")
    n_ctx = lax.axis_size("ctx")
    ctx_index = lax.axis_index("ctx")
    rows = x_in.shape[0]
    local_heads = H // n_tp
    head_width = local_heads * P_SIZE
    per_group = H // G
    rim = CONV - 1

    prior_x, prior_bc = from_behind((x_in[rows - rim :], bc_in[rows - rim :]), ("ctx", "tp"), 1)
    x_part = conv_silu(x_in, prior_x, conv_x_weight, conv_x_bias)
    bc_part = conv_silu(bc_in, prior_bc, conv_bc_weight, conv_bc_bias)

    group_of = [(k * local_heads) // per_group for k in range(n_tp)]
    bc_groups = bc_part.reshape(rows, 2, G, N)
    if group_of != list(range(G)):
        bc_groups = jnp.take(bc_groups, np.array(group_of), axis=2)
    bc_groups = jnp.transpose(bc_groups, (2, 0, 1, 3))
    seg_bc = lax.all_to_all(bc_groups, "tp", split_axis=0, concat_axis=0, tiled=True)
    seg_bc = seg_bc.reshape(n_tp * rows, 2, N)
    seg_x = lax.all_to_all(x_part, "tp", split_axis=1, concat_axis=0, tiled=True)
    seg_dt = lax.all_to_all(dt_in, "tp", split_axis=1, concat_axis=0, tiled=True)
    seg_len = seg_x.shape[0]
    blocks = seg_len // BLOCK
    seg_b = seg_bc[:, 0].reshape(blocks, BLOCK, N)
    seg_c = seg_bc[:, 1].reshape(blocks, BLOCK, N)

    bias_local = lax.dynamic_slice_in_dim(dt_bias, tp_index * local_heads, local_heads, 0)
    rate_local = lax.dynamic_slice_in_dim(a_log, tp_index * local_heads, local_heads, 0)
    skip_local = lax.dynamic_slice_in_dim(skip, tp_index * local_heads, local_heads, 0)
    step_size = jax.nn.softplus(seg_dt.astype(jnp.float32) + bias_local[None, :])
    log_decay = -step_size * jnp.exp(rate_local)[None, :]

    dt_blk = step_size.reshape(blocks, BLOCK, local_heads)
    cum = jnp.cumsum(log_decay.reshape(blocks, BLOCK, local_heads), axis=1)
    last = cum[:, -1]
    x_blk = seg_x.reshape(blocks, BLOCK, head_width)

    fresh = [fresh_block(x_blk[b], seg_b[b], cum[b], dt_blk[b]) for b in range(blocks)]
    block_decay = jnp.exp(last)
    starts = [None]
    state = fresh[0]
    prefix = [jnp.ones((local_heads,), jnp.float32)]
    for b in range(1, blocks):
        starts.append(state)
        prefix.append(prefix[-1] * block_decay[b - 1])
        state = head_columns(block_decay[b])[None, :] * state + fresh[b]
    final = state
    segment_decay = prefix[-1] * block_decay[blocks - 1]

    core = ctx_index % 2
    chip = ctx_index // 2
    chips = n_ctx // 2
    half_width = head_width // 2
    half_heads = local_heads // 2
    decay_slab = jnp.pad(segment_decay[None, :], ((0, 7), (0, head_width - local_heads)))
    mate = lax.ppermute(
        jnp.concatenate([final, decay_slab], axis=0), "ctx", [(i, i ^ 1) for i in range(n_ctx)]
    )
    mate_final = mate[:N]
    even_final = jnp.where(core == 0, final, mate_final)
    odd_final = jnp.where(core == 0, mate_final, final)
    odd_decay = jnp.where(core == 0, mate[N, :local_heads], segment_decay)
    lo = core * half_width
    chip_half = head_columns(lax.dynamic_slice_in_dim(odd_decay, core * half_heads, half_heads, 0))[
        None, :
    ] * lax.dynamic_slice_in_dim(even_final, lo, half_width, 1) + lax.dynamic_slice_in_dim(
        odd_final, lo, half_width, 1
    )
    gathered = lax.all_gather(
        jnp.concatenate([chip_half, decay_slab[:, :half_width]], axis=0), "ctx"
    )
    decays = gathered[:, N, :local_heads]

    skip_cols = head_columns(skip_local)
    partials = []
    for b in range(blocks):
        scores = jnp.einsum("in,jn->ij", seg_c[b], seg_b[b], preferred_element_type=jnp.float32)
        partials.append(intra_block(x_blk[b], scores, cum[b], dt_blk[b], skip_cols))

    seg_ids = jnp.arange(n_ctx)[None, :]
    chip_ids = jnp.arange(chips)[:, None]
    between = (seg_ids >= 2 * chip_ids + 2) & (seg_ids < ctx_index)
    chip_weight = jnp.prod(jnp.where(between[:, :, None], decays[None], 1.0), axis=1)
    chip_weight = jnp.where(chip_ids < chip, chip_weight, 0.0)
    halves = []
    for q in range(2):
        part = gathered[q::2, :N]
        wq = head_columns(chip_weight[:, q * half_heads : (q + 1) * half_heads])
        halves.append(jnp.sum(wq[:, None, :] * part, axis=0))
    incoming = jnp.concatenate(halves, axis=1) + jnp.where(core == 1, 1.0, 0.0) * even_final

    results = []
    for b in range(blocks):
        carried_state = head_columns(prefix[b])[None, :] * incoming
        if starts[b] is not None:
            carried_state = starts[b] + carried_state
        inter = head_columns(jnp.exp(cum[b])) * jnp.dot(
            seg_c[b].astype(jnp.float32), carried_state, precision=lax.Precision.HIGHEST
        )
        results.append((partials[b] + inter).astype(jnp.bfloat16))
    result = jnp.concatenate(results, axis=0) if blocks > 1 else results[0]
    return lax.all_to_all(result, "tp", split_axis=0, concat_axis=1, tiled=True)


def solution(mesh):
    return jax.shard_map(
        on_device,
        mesh=mesh,
        in_specs=(
            P(("ctx", "tp"), None),
            P(("ctx", "tp"), None),
            P(("ctx", "tp"), None),
            P(),
            P(),
            P(),
            P(),
            P(),
            P(),
            P(),
        ),
        out_specs=P(("ctx", "tp"), None),
        check_vma=False,
    )
```

```python
import numpy as np
import jax
import jax.numpy as jnp
from jax import lax
from jax.sharding import PartitionSpec as P
from jax.experimental import pallas as pl
from jax.experimental.pallas import tpu as pltpu

H = 128
P_SIZE = 64
N = 256
G = 4
CONV = 4
BLOCK = 512


def from_behind(value, axis, steps):
    count = lax.axis_size(axis)
    initial, last = (max(0, -steps), min(count, count - steps))
    return lax.ppermute(value, axis, [(source, source + steps) for source in range(initial, last)])


def conv_rows(full, rows, weight, bias):
    total = bias[None, :] + weight[0][None, :] * full[0:rows]
    for k in range(1, CONV):
        total = total + weight[k][None, :] * full[k : k + rows]
    return jax.nn.silu(total).astype(jnp.bfloat16)


def conv_silu(raw, prior, weight, bias):
    rows = raw.shape[0]
    rim = CONV - 1
    zero_prior = jnp.zeros((rim, raw.shape[1]), jnp.float32)
    body = conv_rows(jnp.concatenate([zero_prior, raw.astype(jnp.float32)], axis=0), rows, weight, bias)
    edge = jnp.concatenate([prior, raw[:rim]], axis=0).astype(jnp.float32)
    return lax.dynamic_update_slice_in_dim(body, conv_rows(edge, rim, weight, bias), 0, 0)


def intra_kernel(x_ref, s_ref, cum_ref, cumt_ref, dtt_ref, skip_ref, o_ref):
    tiles = BLOCK // 128
    lane_head = lax.broadcasted_iota(jnp.int32, cum_ref.shape, 1)
    row_head = lax.broadcasted_iota(jnp.int32, cumt_ref.shape, 0)
    lane = lax.broadcasted_iota(jnp.int32, (128, 128), 1)

    def pair(p, carry):
        off = pl.multiple_of(p * 128, 128)
        xp = x_ref[:, pl.ds(off, 128)]
        cum_all = cum_ref[...]
        cumt_all = cumt_ref[...]
        dtt_all = dtt_ref[...]
        cols, rows, dts = [], [], []
        for k in range(2):
            h = 2 * p + k
            cols.append(jnp.sum(jnp.where(lane_head == h, cum_all, 0.0), axis=1, keepdims=True))
            rows.append(jnp.sum(jnp.where(row_head == h, cumt_all, 0.0), axis=0, keepdims=True))
            dts.append(jnp.sum(jnp.where(row_head == h, dtt_all, 0.0), axis=0, keepdims=True))
        skip_p = skip_ref[:, pl.ds(off, 128)]
        for r in range(tiles):
            width = (r + 1) * 128
            s_tile = s_ref[r * 128 : width, 0:width]
            lower = lax.broadcasted_iota(jnp.int32, (128, width), 1) <= (
                lax.broadcasted_iota(jnp.int32, (128, width), 0) + r * 128
            )
            res = []
            for k in range(2):
                gap = cols[k][r * 128 : width] - rows[k][:, 0:width]
                decay = jnp.where(lower, jnp.exp(jnp.where(lower, gap, 0.0)), 0.0)
                w = (s_tile * decay * dts[k][:, 0:width]).astype(jnp.bfloat16)
                res.append(jnp.dot(w, xp[0:width], preferred_element_type=jnp.float32))
            out = jnp.where(lane < P_SIZE, res[0], res[1])
            o_ref[r * 128 : width, pl.ds(off, 128)] = out + skip_p * xp[r * 128 : width].astype(jnp.float32)
        return carry

    lax.fori_loop(0, x_ref.shape[1] // 128, pair, 0)


def intra_block(x, scores, cum, dt, skip_cols):
    heads = cum.shape[1]
    width = x.shape[1]
    cum_lanes = jnp.pad(cum, ((0, 0), (0, 128 - heads)))
    pad_rows = (-heads) % 8
    cum_rows = jnp.pad(cum.T, ((0, pad_rows), (0, 0)))
    dt_rows = jnp.pad(dt.T, ((0, pad_rows), (0, 0)))
    vmem = pl.BlockSpec(memory_space=pltpu.VMEM)
    return pl.pallas_call(
        intra_kernel,
        out_shape=jax.ShapeDtypeStruct((BLOCK, width), jnp.float32),
        in_specs=[vmem] * 6,
        out_specs=vmem,
        name="ssd_intra",
        cost_estimate=pl.CostEstimate(
            flops=2 * BLOCK * BLOCK * width * 2,
            transcendentals=heads * BLOCK * BLOCK,
            bytes_accessed=BLOCK * width * 6 + BLOCK * BLOCK * 4,
        ),
    )(x, scores, cum_lanes, cum_rows, dt_rows, skip_cols[None, :])


def fresh_kernel(x_ref, bt_ref, cum_ref, dtl_ref, o_ref):
    lane_head = lax.broadcasted_iota(jnp.int32, cum_ref.shape, 1)
    lane = lax.broadcasted_iota(jnp.int32, (BLOCK, 128), 1)

    def pair(p, carry):
        off = pl.multiple_of(p * 128, 128)
        xp = x_ref[:, pl.ds(off, 128)].astype(jnp.float32)
        cum_all = cum_ref[...]
        dt_all = dtl_ref[...]
        factors = []
        for k in range(2):
            h = 2 * p + k
            c = jnp.sum(jnp.where(lane_head == h, cum_all, 0.0), axis=1, keepdims=True)
            d = jnp.sum(jnp.where(lane_head == h, dt_all, 0.0), axis=1, keepdims=True)
            factors.append(jnp.exp(c[BLOCK - 1 : BLOCK] - c) * d)
        wx = (jnp.where(lane < P_SIZE, factors[0], factors[1]) * xp).astype(jnp.bfloat16)
        o_ref[:, pl.ds(off, 128)] = jnp.dot(bt_ref[...], wx, preferred_element_type=jnp.float32)
        return carry

    lax.fori_loop(0, x_ref.shape[1] // 128, pair, 0)


def fresh_block(x, b, cum, dt):
    heads = cum.shape[1]
    width = x.shape[1]
    cum_lanes = jnp.pad(cum, ((0, 0), (0, 128 - heads)))
    dt_lanes = jnp.pad(dt, ((0, 0), (0, 128 - heads)))
    vmem = pl.BlockSpec(memory_space=pltpu.VMEM)
    return pl.pallas_call(
        fresh_kernel,
        out_shape=jax.ShapeDtypeStruct((N, width), jnp.float32),
        in_specs=[vmem] * 4,
        out_specs=vmem,
        name="ssd_fresh",
        cost_estimate=pl.CostEstimate(
            flops=2 * BLOCK * N * width,
            transcendentals=heads * BLOCK,
            bytes_accessed=BLOCK * width * 2 + N * width * 4 + BLOCK * N * 2,
        ),
    )(x, b.T, cum_lanes, dt_lanes)


def head_columns(head_major):
    return jnp.repeat(head_major, P_SIZE, axis=-1)


def on_device(
    x_in,
    bc_in,
    dt_in,
    conv_x_weight,
    conv_x_bias,
    conv_bc_weight,
    conv_bc_bias,
    dt_bias,
    a_log,
    skip,
):
    n_tp = lax.axis_size("tp")
    tp_index = lax.axis_index("tp")
    n_ctx = lax.axis_size("ctx")
    ctx_index = lax.axis_index("ctx")
    rows = x_in.shape[0]
    local_heads = H // n_tp
    head_width = local_heads * P_SIZE
    per_group = H // G
    rim = CONV - 1

    prior_x, prior_bc = from_behind((x_in[rows - rim :], bc_in[rows - rim :]), ("ctx", "tp"), 1)
    x_part = conv_silu(x_in, prior_x, conv_x_weight, conv_x_bias)
    bc_part = conv_silu(bc_in, prior_bc, conv_bc_weight, conv_bc_bias)

    group_of = [(k * local_heads) // per_group for k in range(n_tp)]
    bc_groups = bc_part.reshape(rows, 2, G, N)
    if group_of != list(range(G)):
        bc_groups = jnp.take(bc_groups, np.array(group_of), axis=2)
    bc_groups = jnp.transpose(bc_groups, (2, 0, 1, 3))
    seg_bc = lax.all_to_all(bc_groups, "tp", split_axis=0, concat_axis=0, tiled=True)
    seg_bc = seg_bc.reshape(n_tp * rows, 2, N)
    seg_x = lax.all_to_all(x_part, "tp", split_axis=1, concat_axis=0, tiled=True)
    seg_dt = lax.all_to_all(dt_in, "tp", split_axis=1, concat_axis=0, tiled=True)
    seg_len = seg_x.shape[0]
    blocks = seg_len // BLOCK
    seg_b = seg_bc[:, 0].reshape(blocks, BLOCK, N)
    seg_c = seg_bc[:, 1].reshape(blocks, BLOCK, N)

    bias_local = lax.dynamic_slice_in_dim(dt_bias, tp_index * local_heads, local_heads, 0)
    rate_local = lax.dynamic_slice_in_dim(a_log, tp_index * local_heads, local_heads, 0)
    skip_local = lax.dynamic_slice_in_dim(skip, tp_index * local_heads, local_heads, 0)
    step_size = jax.nn.softplus(seg_dt.astype(jnp.float32) + bias_local[None, :])
    log_decay = -step_size * jnp.exp(rate_local)[None, :]

    dt_blk = step_size.reshape(blocks, BLOCK, local_heads)
    cum = jnp.cumsum(log_decay.reshape(blocks, BLOCK, local_heads), axis=1)
    last = cum[:, -1]
    x_blk = seg_x.reshape(blocks, BLOCK, head_width)

    fresh = [fresh_block(x_blk[b], seg_b[b], cum[b], dt_blk[b]) for b in range(blocks)]
    block_decay = jnp.exp(last)
    starts = [None]
    state = fresh[0]
    prefix = [jnp.ones((local_heads,), jnp.float32)]
    for b in range(1, blocks):
        starts.append(state)
        prefix.append(prefix[-1] * block_decay[b - 1])
        state = head_columns(block_decay[b])[None, :] * state + fresh[b]
    final = state
    segment_decay = prefix[-1] * block_decay[blocks - 1]

    core = ctx_index % 2
    chip = ctx_index // 2
    chips = n_ctx // 2
    half_width = head_width // 2
    half_heads = local_heads // 2
    decay_slab = jnp.pad(segment_decay[None, :], ((0, 7), (0, head_width - local_heads)))
    mate = lax.ppermute(
        jnp.concatenate([final, decay_slab], axis=0), "ctx", [(i, i ^ 1) for i in range(n_ctx)]
    )
    mate_final = mate[:N]
    even_final = jnp.where(core == 0, final, mate_final)
    odd_final = jnp.where(core == 0, mate_final, final)
    odd_decay = jnp.where(core == 0, mate[N, :local_heads], segment_decay)
    lo = core * half_width
    chip_half = head_columns(lax.dynamic_slice_in_dim(odd_decay, core * half_heads, half_heads, 0))[
        None, :
    ] * lax.dynamic_slice_in_dim(even_final, lo, half_width, 1) + lax.dynamic_slice_in_dim(
        odd_final, lo, half_width, 1
    )
    skip_cols = head_columns(skip_local)
    partials = []
    for b in range(blocks):
        scores = jnp.einsum("in,jn->ij", seg_c[b], seg_b[b], preferred_element_type=jnp.float32)
        partials.append(intra_block(x_blk[b], scores, cum[b], dt_blk[b], skip_cols))

    mate_decay = mate[N, :local_heads]
    chip_decay = head_columns(
        lax.dynamic_slice_in_dim(segment_decay * mate_decay, core * half_heads, half_heads, 0)
    )[None, :]
    pieces = 4 if N % 32 == 0 else 1
    piece_rows = N // pieces
    acc = [jnp.zeros((piece_rows, half_width), jnp.float32) for _ in range(pieces)]
    for r in range(chips - 1):
        pairs = [(2 * r + q, 2 * r + 2 + q) for q in range(2)]
        for k in range(pieces):
            send = chip_decay * acc[k] + chip_half[k * piece_rows : (k + 1) * piece_rows]
            acc[k] = acc[k] + lax.ppermute(send, "ctx", pairs)
    prefix_half = jnp.concatenate(acc, axis=0) if pieces > 1 else acc[0]
    mate_prefix = lax.ppermute(prefix_half, "ctx", [(i, i ^ 1) for i in range(n_ctx)])
    chip_prefix = jnp.concatenate(
        [jnp.where(core == 0, prefix_half, mate_prefix), jnp.where(core == 0, mate_prefix, prefix_half)],
        axis=1,
    )
    incoming = jnp.where(
        core == 1, head_columns(mate_decay)[None, :] * chip_prefix + mate_final, chip_prefix
    )

    results = []
    for b in range(blocks):
        carried_state = head_columns(prefix[b])[None, :] * incoming
        if starts[b] is not None:
            carried_state = starts[b] + carried_state
        inter = head_columns(jnp.exp(cum[b])) * jnp.dot(
            seg_c[b].astype(jnp.float32), carried_state, precision=lax.Precision.HIGHEST
        )
        results.append((partials[b] + inter).astype(jnp.bfloat16))
    result = jnp.concatenate(results, axis=0) if blocks > 1 else results[0]
    return lax.all_to_all(result, "tp", split_axis=0, concat_axis=1, tiled=True)


def solution(mesh):
    return jax.shard_map(
        on_device,
        mesh=mesh,
        in_specs=(
            P(("ctx", "tp"), None),
            P(("ctx", "tp"), None),
            P(("ctx", "tp"), None),
            P(),
            P(),
            P(),
            P(),
            P(),
            P(),
            P(),
        ),
        out_specs=P(("ctx", "tp"), None),
        check_vma=False,
    )
```

```python
import numpy as np
import jax
import jax.numpy as jnp
from jax import lax
from jax.sharding import PartitionSpec as P
from jax.experimental import pallas as pl
from jax.experimental.pallas import tpu as pltpu

H = 128
P_SIZE = 64
N = 256
G = 4
CONV = 4
BLOCK = 512


def from_behind(value, axis, steps):
    count = lax.axis_size(axis)
    initial, last = (max(0, -steps), min(count, count - steps))
    return lax.ppermute(value, axis, [(source, source + steps) for source in range(initial, last)])


def conv_rows(full, rows, weight, bias):
    total = bias[None, :] + weight[0][None, :] * full[0:rows]
    for k in range(1, CONV):
        total = total + weight[k][None, :] * full[k : k + rows]
    return jax.nn.silu(total).astype(jnp.bfloat16)


def conv_silu(raw, prior, weight, bias):
    rows = raw.shape[0]
    rim = CONV - 1
    zero_prior = jnp.zeros((rim, raw.shape[1]), jnp.float32)
    body = conv_rows(jnp.concatenate([zero_prior, raw.astype(jnp.float32)], axis=0), rows, weight, bias)
    edge = jnp.concatenate([prior, raw[:rim]], axis=0).astype(jnp.float32)
    return lax.dynamic_update_slice_in_dim(body, conv_rows(edge, rim, weight, bias), 0, 0)


def intra_kernel(x_ref, s_ref, cum_ref, cumt_ref, dtt_ref, skip_ref, o_ref):
    tiles = BLOCK // 128
    lane_head = lax.broadcasted_iota(jnp.int32, cum_ref.shape, 1)
    row_head = lax.broadcasted_iota(jnp.int32, cumt_ref.shape, 0)
    lane = lax.broadcasted_iota(jnp.int32, (128, 128), 1)

    def pair(p, carry):
        off = pl.multiple_of(p * 128, 128)
        xp = x_ref[:, pl.ds(off, 128)]
        cum_all = cum_ref[...]
        cumt_all = cumt_ref[...]
        dtt_all = dtt_ref[...]
        cols, rows, dts = [], [], []
        for k in range(2):
            h = 2 * p + k
            cols.append(jnp.sum(jnp.where(lane_head == h, cum_all, 0.0), axis=1, keepdims=True))
            rows.append(jnp.sum(jnp.where(row_head == h, cumt_all, 0.0), axis=0, keepdims=True))
            dts.append(jnp.sum(jnp.where(row_head == h, dtt_all, 0.0), axis=0, keepdims=True))
        skip_p = skip_ref[:, pl.ds(off, 128)]
        for r in range(tiles):
            width = (r + 1) * 128
            s_tile = s_ref[r * 128 : width, 0:width]
            lower = lax.broadcasted_iota(jnp.int32, (128, width), 1) <= (
                lax.broadcasted_iota(jnp.int32, (128, width), 0) + r * 128
            )
            res = []
            for k in range(2):
                gap = cols[k][r * 128 : width] - rows[k][:, 0:width]
                decay = jnp.where(lower, jnp.exp(jnp.where(lower, gap, 0.0)), 0.0)
                w = (s_tile * decay * dts[k][:, 0:width]).astype(jnp.bfloat16)
                res.append(jnp.dot(w, xp[0:width], preferred_element_type=jnp.float32))
            out = jnp.where(lane < P_SIZE, res[0], res[1])
            o_ref[r * 128 : width, pl.ds(off, 128)] = out + skip_p * xp[r * 128 : width].astype(jnp.float32)
        return carry

    lax.fori_loop(0, x_ref.shape[1] // 128, pair, 0)


def intra_block(x, scores, cum, dt, skip_cols):
    heads = cum.shape[1]
    width = x.shape[1]
    cum_lanes = jnp.pad(cum, ((0, 0), (0, 128 - heads)))
    pad_rows = (-heads) % 8
    cum_rows = jnp.pad(cum.T, ((0, pad_rows), (0, 0)))
    dt_rows = jnp.pad(dt.T, ((0, pad_rows), (0, 0)))
    vmem = pl.BlockSpec(memory_space=pltpu.VMEM)
    return pl.pallas_call(
        intra_kernel,
        out_shape=jax.ShapeDtypeStruct((BLOCK, width), jnp.float32),
        in_specs=[vmem] * 6,
        out_specs=vmem,
        name="ssd_intra",
        cost_estimate=pl.CostEstimate(
            flops=2 * BLOCK * BLOCK * width * 2,
            transcendentals=heads * BLOCK * BLOCK,
            bytes_accessed=BLOCK * width * 6 + BLOCK * BLOCK * 4,
        ),
    )(x, scores, cum_lanes, cum_rows, dt_rows, skip_cols[None, :])


def fresh_kernel(x_ref, bt_ref, cum_ref, dtl_ref, o_ref):
    lane_head = lax.broadcasted_iota(jnp.int32, cum_ref.shape, 1)
    lane = lax.broadcasted_iota(jnp.int32, (BLOCK, 128), 1)

    def pair(p, carry):
        off = pl.multiple_of(p * 128, 128)
        xp = x_ref[:, pl.ds(off, 128)].astype(jnp.float32)
        cum_all = cum_ref[...]
        dt_all = dtl_ref[...]
        factors = []
        for k in range(2):
            h = 2 * p + k
            c = jnp.sum(jnp.where(lane_head == h, cum_all, 0.0), axis=1, keepdims=True)
            d = jnp.sum(jnp.where(lane_head == h, dt_all, 0.0), axis=1, keepdims=True)
            factors.append(jnp.exp(c[BLOCK - 1 : BLOCK] - c) * d)
        wx = (jnp.where(lane < P_SIZE, factors[0], factors[1]) * xp).astype(jnp.bfloat16)
        o_ref[:, pl.ds(off, 128)] = jnp.dot(bt_ref[...], wx, preferred_element_type=jnp.float32)
        return carry

    lax.fori_loop(0, x_ref.shape[1] // 128, pair, 0)


def fresh_block(x, b, cum, dt):
    heads = cum.shape[1]
    width = x.shape[1]
    cum_lanes = jnp.pad(cum, ((0, 0), (0, 128 - heads)))
    dt_lanes = jnp.pad(dt, ((0, 0), (0, 128 - heads)))
    vmem = pl.BlockSpec(memory_space=pltpu.VMEM)
    return pl.pallas_call(
        fresh_kernel,
        out_shape=jax.ShapeDtypeStruct((N, width), jnp.float32),
        in_specs=[vmem] * 4,
        out_specs=vmem,
        name="ssd_fresh",
        cost_estimate=pl.CostEstimate(
            flops=2 * BLOCK * N * width,
            transcendentals=heads * BLOCK,
            bytes_accessed=BLOCK * width * 2 + N * width * 4 + BLOCK * N * 2,
        ),
    )(x, b.T, cum_lanes, dt_lanes)


def head_columns(head_major):
    return jnp.repeat(head_major, P_SIZE, axis=-1)


def on_device(
    x_in,
    bc_in,
    dt_in,
    conv_x_weight,
    conv_x_bias,
    conv_bc_weight,
    conv_bc_bias,
    dt_bias,
    a_log,
    skip,
):
    n_tp = lax.axis_size("tp")
    tp_index = lax.axis_index("tp")
    n_ctx = lax.axis_size("ctx")
    ctx_index = lax.axis_index("ctx")
    rows = x_in.shape[0]
    local_heads = H // n_tp
    head_width = local_heads * P_SIZE
    per_group = H // G
    rim = CONV - 1

    prior_x, prior_bc = from_behind((x_in[rows - rim :], bc_in[rows - rim :]), ("ctx", "tp"), 1)
    x_part = conv_silu(x_in, prior_x, conv_x_weight, conv_x_bias)
    bc_part = conv_silu(bc_in, prior_bc, conv_bc_weight, conv_bc_bias)

    group_of = [(k * local_heads) // per_group for k in range(n_tp)]
    bc_groups = bc_part.reshape(rows, 2, G, N)
    if group_of != list(range(G)):
        bc_groups = jnp.take(bc_groups, np.array(group_of), axis=2)
    bc_groups = jnp.transpose(bc_groups, (2, 0, 1, 3))
    seg_bc = lax.all_to_all(bc_groups, "tp", split_axis=0, concat_axis=0, tiled=True)
    seg_bc = seg_bc.reshape(n_tp * rows, 2, N)
    seg_x = lax.all_to_all(x_part, "tp", split_axis=1, concat_axis=0, tiled=True)
    seg_dt = lax.all_to_all(dt_in, "tp", split_axis=1, concat_axis=0, tiled=True)
    seg_len = seg_x.shape[0]
    blocks = seg_len // BLOCK
    seg_b = seg_bc[:, 0].reshape(blocks, BLOCK, N)
    seg_c = seg_bc[:, 1].reshape(blocks, BLOCK, N)

    bias_local = lax.dynamic_slice_in_dim(dt_bias, tp_index * local_heads, local_heads, 0)
    rate_local = lax.dynamic_slice_in_dim(a_log, tp_index * local_heads, local_heads, 0)
    skip_local = lax.dynamic_slice_in_dim(skip, tp_index * local_heads, local_heads, 0)
    step_size = jax.nn.softplus(seg_dt.astype(jnp.float32) + bias_local[None, :])
    log_decay = -step_size * jnp.exp(rate_local)[None, :]

    dt_blk = step_size.reshape(blocks, BLOCK, local_heads)
    cum = jnp.cumsum(log_decay.reshape(blocks, BLOCK, local_heads), axis=1)
    last = cum[:, -1]
    x_blk = seg_x.reshape(blocks, BLOCK, head_width)

    fresh = [fresh_block(x_blk[b], seg_b[b], cum[b], dt_blk[b]) for b in range(blocks)]
    block_decay = jnp.exp(last)
    starts = [None]
    state = fresh[0]
    prefix = [jnp.ones((local_heads,), jnp.float32)]
    for b in range(1, blocks):
        starts.append(state)
        prefix.append(prefix[-1] * block_decay[b - 1])
        state = head_columns(block_decay[b])[None, :] * state + fresh[b]
    final = state
    segment_decay = prefix[-1] * block_decay[blocks - 1]

    core = ctx_index % 2
    chip = ctx_index // 2
    chips = n_ctx // 2
    half_width = head_width // 2
    half_heads = local_heads // 2
    decay_slab = jnp.pad(segment_decay[None, :], ((0, 7), (0, head_width - local_heads)))
    mate = lax.ppermute(
        jnp.concatenate([final, decay_slab], axis=0), "ctx", [(i, i ^ 1) for i in range(n_ctx)]
    )
    mate_final = mate[:N]
    even_final = jnp.where(core == 0, final, mate_final)
    odd_final = jnp.where(core == 0, mate_final, final)
    odd_decay = jnp.where(core == 0, mate[N, :local_heads], segment_decay)
    lo = core * half_width
    chip_half = head_columns(lax.dynamic_slice_in_dim(odd_decay, core * half_heads, half_heads, 0))[
        None, :
    ] * lax.dynamic_slice_in_dim(even_final, lo, half_width, 1) + lax.dynamic_slice_in_dim(
        odd_final, lo, half_width, 1
    )
    mate_decay = mate[N, :local_heads]
    chip_decay = head_columns(
        lax.dynamic_slice_in_dim(segment_decay * mate_decay, core * half_heads, half_heads, 0)
    )[None, :]
    pieces = 4 if N % 32 == 0 else 1
    piece_rows = N // pieces
    acc = [jnp.zeros((piece_rows, half_width), jnp.float32) for _ in range(pieces)]
    last_send = None
    for r in range(chips - 1):
        pairs = [(2 * r + q, 2 * r + 2 + q) for q in range(2)]
        for k in range(pieces):
            send = chip_decay * acc[k] + chip_half[k * piece_rows : (k + 1) * piece_rows]
            acc[k] = acc[k] + lax.ppermute(send, "ctx", pairs)
            last_send = send
    skip_cols = head_columns(skip_local)
    partials = []
    for b in range(blocks):
        scores = jnp.einsum("in,jn->ij", seg_c[b], seg_b[b], preferred_element_type=jnp.float32)
        operands = (x_blk[b], scores, cum[b], dt_blk[b])
        if last_send is not None:
            operands = lax.optimization_barrier(operands + (last_send,))[:4]
        partials.append(intra_block(*operands, skip_cols))

    prefix_half = jnp.concatenate(acc, axis=0) if pieces > 1 else acc[0]
    prefix_half = lax.optimization_barrier((prefix_half, partials))[0]
    mate_prefix = lax.ppermute(prefix_half, "ctx", [(i, i ^ 1) for i in range(n_ctx)])
    chip_prefix = jnp.concatenate(
        [jnp.where(core == 0, prefix_half, mate_prefix), jnp.where(core == 0, mate_prefix, prefix_half)],
        axis=1,
    )
    incoming = jnp.where(
        core == 1, head_columns(mate_decay)[None, :] * chip_prefix + mate_final, chip_prefix
    )

    results = []
    for b in range(blocks):
        carried_state = head_columns(prefix[b])[None, :] * incoming
        if starts[b] is not None:
            carried_state = starts[b] + carried_state
        state_hi = carried_state.astype(jnp.bfloat16)
        state_lo = (carried_state - state_hi.astype(jnp.float32)).astype(jnp.bfloat16)
        projected = jnp.dot(seg_c[b], state_hi, preferred_element_type=jnp.float32) + jnp.dot(
            seg_c[b], state_lo, preferred_element_type=jnp.float32
        )
        inter = head_columns(jnp.exp(cum[b])) * projected
        results.append((partials[b] + inter).astype(jnp.bfloat16))
    result = jnp.concatenate(results, axis=0) if blocks > 1 else results[0]
    return lax.all_to_all(result, "tp", split_axis=0, concat_axis=1, tiled=True)


def solution(mesh):
    return jax.shard_map(
        on_device,
        mesh=mesh,
        in_specs=(
            P(("ctx", "tp"), None),
            P(("ctx", "tp"), None),
            P(("ctx", "tp"), None),
            P(),
            P(),
            P(),
            P(),
            P(),
            P(),
            P(),
        ),
        out_specs=P(("ctx", "tp"), None),
        check_vma=False,
    )
```

```python
import numpy as np
import jax
import jax.numpy as jnp
from jax import lax
from jax.sharding import PartitionSpec as P
from jax.experimental import pallas as pl
from jax.experimental.pallas import tpu as pltpu

H = 128
P_SIZE = 64
N = 256
G = 4
CONV = 4
BLOCK = 512


def from_behind(value, axis, steps):
    count = lax.axis_size(axis)
    initial, last = (max(0, -steps), min(count, count - steps))
    return lax.ppermute(value, axis, [(source, source + steps) for source in range(initial, last)])


def conv_rows(full, rows, weight, bias):
    total = bias[None, :] + weight[0][None, :] * full[0:rows]
    for k in range(1, CONV):
        total = total + weight[k][None, :] * full[k : k + rows]
    return jax.nn.silu(total).astype(jnp.bfloat16)


def conv_silu(raw, prior, weight, bias):
    rows = raw.shape[0]
    rim = CONV - 1
    zero_prior = jnp.zeros((rim, raw.shape[1]), jnp.float32)
    body = conv_rows(jnp.concatenate([zero_prior, raw.astype(jnp.float32)], axis=0), rows, weight, bias)
    edge = jnp.concatenate([prior, raw[:rim]], axis=0).astype(jnp.float32)
    return lax.dynamic_update_slice_in_dim(body, conv_rows(edge, rim, weight, bias), 0, 0)


def intra_kernel(x_ref, s_ref, cum_ref, cumt_ref, dtt_ref, skip_ref, o_ref):
    tiles = BLOCK // 128
    lane_head = lax.broadcasted_iota(jnp.int32, cum_ref.shape, 1)
    row_head = lax.broadcasted_iota(jnp.int32, cumt_ref.shape, 0)
    lane = lax.broadcasted_iota(jnp.int32, (128, 128), 1)

    def pair(p, carry):
        off = pl.multiple_of(p * 128, 128)
        xp = x_ref[:, pl.ds(off, 128)]
        cum_all = cum_ref[...]
        cumt_all = cumt_ref[...]
        dtt_all = dtt_ref[...]
        cols, rows, dts = [], [], []
        for k in range(2):
            h = 2 * p + k
            cols.append(jnp.sum(jnp.where(lane_head == h, cum_all, 0.0), axis=1, keepdims=True))
            rows.append(jnp.sum(jnp.where(row_head == h, cumt_all, 0.0), axis=0, keepdims=True))
            dts.append(jnp.sum(jnp.where(row_head == h, dtt_all, 0.0), axis=0, keepdims=True))
        skip_p = skip_ref[:, pl.ds(off, 128)]
        for r in range(tiles):
            width = (r + 1) * 128
            s_tile = s_ref[r * 128 : width, 0:width]
            lower = lax.broadcasted_iota(jnp.int32, (128, width), 1) <= (
                lax.broadcasted_iota(jnp.int32, (128, width), 0) + r * 128
            )
            res = []
            for k in range(2):
                gap = cols[k][r * 128 : width] - rows[k][:, 0:width]
                decay = jnp.where(lower, jnp.exp(jnp.where(lower, gap, 0.0)), 0.0)
                w = (s_tile * decay * dts[k][:, 0:width]).astype(jnp.bfloat16)
                res.append(jnp.dot(w, xp[0:width], preferred_element_type=jnp.float32))
            out = jnp.where(lane < P_SIZE, res[0], res[1])
            o_ref[r * 128 : width, pl.ds(off, 128)] = out + skip_p * xp[r * 128 : width].astype(jnp.float32)
        return carry

    lax.fori_loop(0, x_ref.shape[1] // 128, pair, 0)


def intra_block(x, scores, cum, dt, skip_cols):
    heads = cum.shape[1]
    width = x.shape[1]
    cum_lanes = jnp.pad(cum, ((0, 0), (0, 128 - heads)))
    pad_rows = (-heads) % 8
    cum_rows = jnp.pad(cum.T, ((0, pad_rows), (0, 0)))
    dt_rows = jnp.pad(dt.T, ((0, pad_rows), (0, 0)))
    vmem = pl.BlockSpec(memory_space=pltpu.VMEM)
    return pl.pallas_call(
        intra_kernel,
        out_shape=jax.ShapeDtypeStruct((BLOCK, width), jnp.float32),
        in_specs=[vmem] * 6,
        out_specs=vmem,
        name="ssd_intra",
        cost_estimate=pl.CostEstimate(
            flops=2 * BLOCK * BLOCK * width * 2,
            transcendentals=heads * BLOCK * BLOCK,
            bytes_accessed=BLOCK * width * 6 + BLOCK * BLOCK * 4,
        ),
    )(x, scores, cum_lanes, cum_rows, dt_rows, skip_cols[None, :])


def fresh_kernel(x_ref, bt_ref, cum_ref, dtl_ref, o_ref):
    lane_head = lax.broadcasted_iota(jnp.int32, cum_ref.shape, 1)
    lane = lax.broadcasted_iota(jnp.int32, (BLOCK, 128), 1)

    def pair(p, carry):
        off = pl.multiple_of(p * 128, 128)
        xp = x_ref[:, pl.ds(off, 128)].astype(jnp.float32)
        cum_all = cum_ref[...]
        dt_all = dtl_ref[...]
        factors = []
        for k in range(2):
            h = 2 * p + k
            c = jnp.sum(jnp.where(lane_head == h, cum_all, 0.0), axis=1, keepdims=True)
            d = jnp.sum(jnp.where(lane_head == h, dt_all, 0.0), axis=1, keepdims=True)
            factors.append(jnp.exp(c[BLOCK - 1 : BLOCK] - c) * d)
        wx = (jnp.where(lane < P_SIZE, factors[0], factors[1]) * xp).astype(jnp.bfloat16)
        o_ref[:, pl.ds(off, 128)] = jnp.dot(bt_ref[...], wx, preferred_element_type=jnp.float32)
        return carry

    lax.fori_loop(0, x_ref.shape[1] // 128, pair, 0)


def fresh_block(x, b, cum, dt):
    heads = cum.shape[1]
    width = x.shape[1]
    cum_lanes = jnp.pad(cum, ((0, 0), (0, 128 - heads)))
    dt_lanes = jnp.pad(dt, ((0, 0), (0, 128 - heads)))
    vmem = pl.BlockSpec(memory_space=pltpu.VMEM)
    return pl.pallas_call(
        fresh_kernel,
        out_shape=jax.ShapeDtypeStruct((N, width), jnp.float32),
        in_specs=[vmem] * 4,
        out_specs=vmem,
        name="ssd_fresh",
        cost_estimate=pl.CostEstimate(
            flops=2 * BLOCK * N * width,
            transcendentals=heads * BLOCK,
            bytes_accessed=BLOCK * width * 2 + N * width * 4 + BLOCK * N * 2,
        ),
    )(x, b.T, cum_lanes, dt_lanes)


def head_columns(head_major):
    return jnp.repeat(head_major, P_SIZE, axis=-1)


def on_device(
    x_in,
    bc_in,
    dt_in,
    conv_x_weight,
    conv_x_bias,
    conv_bc_weight,
    conv_bc_bias,
    dt_bias,
    a_log,
    skip,
):
    n_tp = lax.axis_size("tp")
    tp_index = lax.axis_index("tp")
    n_ctx = lax.axis_size("ctx")
    ctx_index = lax.axis_index("ctx")
    rows = x_in.shape[0]
    local_heads = H // n_tp
    head_width = local_heads * P_SIZE
    per_group = H // G
    rim = CONV - 1

    prior_x, prior_bc = from_behind((x_in[rows - rim :], bc_in[rows - rim :]), ("ctx", "tp"), 1)
    x_part = conv_silu(x_in, prior_x, conv_x_weight, conv_x_bias)
    bc_part = conv_silu(bc_in, prior_bc, conv_bc_weight, conv_bc_bias)

    group_of = [(k * local_heads) // per_group for k in range(n_tp)]
    bc_groups = bc_part.reshape(rows, 2, G, N)
    if group_of != list(range(G)):
        bc_groups = jnp.take(bc_groups, np.array(group_of), axis=2)
    bc_groups = jnp.transpose(bc_groups, (2, 0, 1, 3))
    seg_bc = lax.all_to_all(bc_groups, "tp", split_axis=0, concat_axis=0, tiled=True)
    seg_bc = seg_bc.reshape(n_tp * rows, 2, N)
    seg_x = lax.all_to_all(x_part, "tp", split_axis=1, concat_axis=0, tiled=True)
    seg_dt = lax.all_to_all(dt_in, "tp", split_axis=1, concat_axis=0, tiled=True)
    seg_len = seg_x.shape[0]
    blocks = seg_len // BLOCK
    seg_b = seg_bc[:, 0].reshape(blocks, BLOCK, N)
    seg_c = seg_bc[:, 1].reshape(blocks, BLOCK, N)

    bias_local = lax.dynamic_slice_in_dim(dt_bias, tp_index * local_heads, local_heads, 0)
    rate_local = lax.dynamic_slice_in_dim(a_log, tp_index * local_heads, local_heads, 0)
    skip_local = lax.dynamic_slice_in_dim(skip, tp_index * local_heads, local_heads, 0)
    step_size = jax.nn.softplus(seg_dt.astype(jnp.float32) + bias_local[None, :])
    log_decay = -step_size * jnp.exp(rate_local)[None, :]

    dt_blk = step_size.reshape(blocks, BLOCK, local_heads)
    cum = jnp.cumsum(log_decay.reshape(blocks, BLOCK, local_heads), axis=1)
    last = cum[:, -1]
    x_blk = seg_x.reshape(blocks, BLOCK, head_width)

    fresh = [fresh_block(x_blk[b], seg_b[b], cum[b], dt_blk[b]) for b in range(blocks)]
    block_decay = jnp.exp(last)
    starts = [None]
    state = fresh[0]
    prefix = [jnp.ones((local_heads,), jnp.float32)]
    for b in range(1, blocks):
        starts.append(state)
        prefix.append(prefix[-1] * block_decay[b - 1])
        state = head_columns(block_decay[b])[None, :] * state + fresh[b]
    final = state
    segment_decay = prefix[-1] * block_decay[blocks - 1]

    core = ctx_index % 2
    chip = ctx_index // 2
    chips = n_ctx // 2
    half_width = head_width // 2
    half_heads = local_heads // 2
    decay_slab = jnp.pad(segment_decay[None, :], ((0, 7), (0, head_width - local_heads)))
    mate = lax.ppermute(
        jnp.concatenate([final, decay_slab], axis=0), "ctx", [(i, i ^ 1) for i in range(n_ctx)]
    )
    mate_final = mate[:N]
    even_final = jnp.where(core == 0, final, mate_final)
    odd_final = jnp.where(core == 0, mate_final, final)
    odd_decay = jnp.where(core == 0, mate[N, :local_heads], segment_decay)
    lo = core * half_width
    chip_half = head_columns(lax.dynamic_slice_in_dim(odd_decay, core * half_heads, half_heads, 0))[
        None, :
    ] * lax.dynamic_slice_in_dim(even_final, lo, half_width, 1) + lax.dynamic_slice_in_dim(
        odd_final, lo, half_width, 1
    )
    mate_decay = mate[N, :local_heads]
    chip_decay = head_columns(
        lax.dynamic_slice_in_dim(segment_decay * mate_decay, core * half_heads, half_heads, 0)
    )[None, :]
    pieces = 4 if N % 32 == 0 else 1
    piece_rows = N // pieces
    acc = [jnp.zeros((piece_rows, half_width), jnp.float32) for _ in range(pieces)]
    last_send = None
    for r in range(chips - 1):
        pairs = [(2 * r + q, 2 * r + 2 + q) for q in range(2)]
        for k in range(pieces):
            send = chip_decay * acc[k] + chip_half[k * piece_rows : (k + 1) * piece_rows]
            acc[k] = acc[k] + lax.ppermute(send, "ctx", pairs)
            last_send = send
    skip_cols = head_columns(skip_local)
    partials = []
    for b in range(blocks):
        scores = jnp.einsum("in,jn->ij", seg_c[b], seg_b[b], preferred_element_type=jnp.float32)
        operands = (x_blk[b], scores, cum[b], dt_blk[b])
        if last_send is not None:
            operands = lax.optimization_barrier(operands + (last_send,))[:4]
        partials.append(intra_block(*operands, skip_cols))

    prefix_half = jnp.concatenate(acc, axis=0) if pieces > 1 else acc[0]
    prefix_half = lax.optimization_barrier((prefix_half, partials))[0]
    mate_prefix = lax.ppermute(prefix_half, "ctx", [(i, i ^ 1) for i in range(n_ctx)])
    chip_prefix = jnp.concatenate(
        [jnp.where(core == 0, prefix_half, mate_prefix), jnp.where(core == 0, mate_prefix, prefix_half)],
        axis=1,
    )
    incoming = jnp.where(
        core == 1, head_columns(mate_decay)[None, :] * chip_prefix + mate_final, chip_prefix
    )

    results = []
    for b in range(blocks):
        carried_state = head_columns(prefix[b])[None, :] * incoming
        if starts[b] is not None:
            carried_state = starts[b] + carried_state
        state_hi = lax.reduce_precision(carried_state, exponent_bits=8, mantissa_bits=7)
        state_lo = (carried_state - state_hi).astype(jnp.bfloat16)
        projected = jnp.dot(
            seg_c[b], state_hi.astype(jnp.bfloat16), preferred_element_type=jnp.float32
        ) + jnp.dot(seg_c[b], state_lo, preferred_element_type=jnp.float32)
        inter = head_columns(jnp.exp(cum[b])) * projected
        results.append((partials[b] + inter).astype(jnp.bfloat16))
    result = jnp.concatenate(results, axis=0) if blocks > 1 else results[0]
    return lax.all_to_all(result, "tp", split_axis=0, concat_axis=1, tiled=True)


def solution(mesh):
    return jax.shard_map(
        on_device,
        mesh=mesh,
        in_specs=(
            P(("ctx", "tp"), None),
            P(("ctx", "tp"), None),
            P(("ctx", "tp"), None),
            P(),
            P(),
            P(),
            P(),
            P(),
            P(),
            P(),
        ),
        out_specs=P(("ctx", "tp"), None),
        check_vma=False,
    )
```

```python
import numpy as np
import jax
import jax.numpy as jnp
from jax import lax
from jax.sharding import PartitionSpec as P
from jax.experimental import pallas as pl
from jax.experimental.pallas import tpu as pltpu

H = 128
P_SIZE = 64
N = 256
G = 4
CONV = 4
BLOCK = 512


def from_behind(value, axis, steps):
    count = lax.axis_size(axis)
    initial, last = (max(0, -steps), min(count, count - steps))
    return lax.ppermute(value, axis, [(source, source + steps) for source in range(initial, last)])


def conv_rows(full, rows, weight, bias):
    total = bias[None, :] + weight[0][None, :] * full[0:rows]
    for k in range(1, CONV):
        total = total + weight[k][None, :] * full[k : k + rows]
    return jax.nn.silu(total).astype(jnp.bfloat16)


def conv_silu(raw, prior, weight, bias):
    rows = raw.shape[0]
    rim = CONV - 1
    zero_prior = jnp.zeros((rim, raw.shape[1]), jnp.float32)
    body = conv_rows(jnp.concatenate([zero_prior, raw.astype(jnp.float32)], axis=0), rows, weight, bias)
    edge = jnp.concatenate([prior, raw[:rim]], axis=0).astype(jnp.float32)
    return lax.dynamic_update_slice_in_dim(body, conv_rows(edge, rim, weight, bias), 0, 0)


def intra_kernel(x_ref, s_ref, cum_ref, cumt_ref, dtt_ref, skip_ref, o_ref):
    tiles = BLOCK // 128
    lane_head = lax.broadcasted_iota(jnp.int32, cum_ref.shape, 1)
    row_head = lax.broadcasted_iota(jnp.int32, cumt_ref.shape, 0)
    lane = lax.broadcasted_iota(jnp.int32, (128, 128), 1)

    def pair(p, carry):
        off = pl.multiple_of(p * 128, 128)
        xp = x_ref[:, pl.ds(off, 128)]
        cum_all = cum_ref[...]
        cumt_all = cumt_ref[...]
        dtt_all = dtt_ref[...]
        cols, rows, dts = [], [], []
        for k in range(2):
            h = 2 * p + k
            cols.append(jnp.sum(jnp.where(lane_head == h, cum_all, 0.0), axis=1, keepdims=True))
            rows.append(jnp.sum(jnp.where(row_head == h, cumt_all, 0.0), axis=0, keepdims=True))
            dts.append(jnp.sum(jnp.where(row_head == h, dtt_all, 0.0), axis=0, keepdims=True))
        skip_p = skip_ref[:, pl.ds(off, 128)]
        for r in range(tiles):
            width = (r + 1) * 128
            s_tile = s_ref[r * 128 : width, 0:width]
            lower = lax.broadcasted_iota(jnp.int32, (128, width), 1) <= (
                lax.broadcasted_iota(jnp.int32, (128, width), 0) + r * 128
            )
            res = []
            for k in range(2):
                gap = cols[k][r * 128 : width] - rows[k][:, 0:width]
                decay = jnp.where(lower, jnp.exp(jnp.where(lower, gap, 0.0)), 0.0)
                w = (s_tile * decay * dts[k][:, 0:width]).astype(jnp.bfloat16)
                res.append(jnp.dot(w, xp[0:width], preferred_element_type=jnp.float32))
            out = jnp.where(lane < P_SIZE, res[0], res[1])
            o_ref[r * 128 : width, pl.ds(off, 128)] = out + skip_p * xp[r * 128 : width].astype(jnp.float32)
        return carry

    lax.fori_loop(0, x_ref.shape[1] // 128, pair, 0)


def intra_block(x, scores, cum, dt, skip_cols):
    heads = cum.shape[1]
    width = x.shape[1]
    cum_lanes = jnp.pad(cum, ((0, 0), (0, 128 - heads)))
    pad_rows = (-heads) % 8
    cum_rows = jnp.pad(cum.T, ((0, pad_rows), (0, 0)))
    dt_rows = jnp.pad(dt.T, ((0, pad_rows), (0, 0)))
    vmem = pl.BlockSpec(memory_space=pltpu.VMEM)
    return pl.pallas_call(
        intra_kernel,
        out_shape=jax.ShapeDtypeStruct((BLOCK, width), jnp.float32),
        in_specs=[vmem] * 6,
        out_specs=vmem,
        name="ssd_intra",
        cost_estimate=pl.CostEstimate(
            flops=2 * BLOCK * BLOCK * width * 2,
            transcendentals=heads * BLOCK * BLOCK,
            bytes_accessed=BLOCK * width * 6 + BLOCK * BLOCK * 4,
        ),
    )(x, scores, cum_lanes, cum_rows, dt_rows, skip_cols[None, :])


def fresh_kernel(x_ref, bt_ref, cum_ref, dtl_ref, o_ref):
    lane_head = lax.broadcasted_iota(jnp.int32, cum_ref.shape, 1)
    lane = lax.broadcasted_iota(jnp.int32, (BLOCK, 128), 1)

    def pair(p, carry):
        off = pl.multiple_of(p * 128, 128)
        xp = x_ref[:, pl.ds(off, 128)].astype(jnp.float32)
        cum_all = cum_ref[...]
        dt_all = dtl_ref[...]
        factors = []
        for k in range(2):
            h = 2 * p + k
            c = jnp.sum(jnp.where(lane_head == h, cum_all, 0.0), axis=1, keepdims=True)
            d = jnp.sum(jnp.where(lane_head == h, dt_all, 0.0), axis=1, keepdims=True)
            factors.append(jnp.exp(c[BLOCK - 1 : BLOCK] - c) * d)
        wx = (jnp.where(lane < P_SIZE, factors[0], factors[1]) * xp).astype(jnp.bfloat16)
        o_ref[:, pl.ds(off, 128)] = jnp.dot(bt_ref[...], wx, preferred_element_type=jnp.float32)
        return carry

    lax.fori_loop(0, x_ref.shape[1] // 128, pair, 0)


def fresh_block(x, b, cum, dt):
    heads = cum.shape[1]
    width = x.shape[1]
    cum_lanes = jnp.pad(cum, ((0, 0), (0, 128 - heads)))
    dt_lanes = jnp.pad(dt, ((0, 0), (0, 128 - heads)))
    vmem = pl.BlockSpec(memory_space=pltpu.VMEM)
    return pl.pallas_call(
        fresh_kernel,
        out_shape=jax.ShapeDtypeStruct((N, width), jnp.float32),
        in_specs=[vmem] * 4,
        out_specs=vmem,
        name="ssd_fresh",
        cost_estimate=pl.CostEstimate(
            flops=2 * BLOCK * N * width,
            transcendentals=heads * BLOCK,
            bytes_accessed=BLOCK * width * 2 + N * width * 4 + BLOCK * N * 2,
        ),
    )(x, b.T, cum_lanes, dt_lanes)


def head_columns(head_major):
    return jnp.repeat(head_major, P_SIZE, axis=-1)


def on_device(
    x_in,
    bc_in,
    dt_in,
    conv_x_weight,
    conv_x_bias,
    conv_bc_weight,
    conv_bc_bias,
    dt_bias,
    a_log,
    skip,
):
    n_tp = lax.axis_size("tp")
    tp_index = lax.axis_index("tp")
    n_ctx = lax.axis_size("ctx")
    ctx_index = lax.axis_index("ctx")
    rows = x_in.shape[0]
    local_heads = H // n_tp
    head_width = local_heads * P_SIZE
    per_group = H // G
    rim = CONV - 1

    prior_x, prior_bc = from_behind((x_in[rows - rim :], bc_in[rows - rim :]), ("ctx", "tp"), 1)
    x_part = conv_silu(x_in, prior_x, conv_x_weight, conv_x_bias)
    bc_part = conv_silu(bc_in, prior_bc, conv_bc_weight, conv_bc_bias)

    group_of = [(k * local_heads) // per_group for k in range(n_tp)]
    bc_groups = bc_part.reshape(rows, 2, G, N)
    if group_of != list(range(G)):
        bc_groups = jnp.take(bc_groups, np.array(group_of), axis=2)
    bc_groups = jnp.transpose(bc_groups, (2, 0, 1, 3))
    seg_bc = lax.all_to_all(bc_groups, "tp", split_axis=0, concat_axis=0, tiled=True)
    seg_bc = seg_bc.reshape(n_tp * rows, 2, N)
    seg_x = lax.all_to_all(x_part, "tp", split_axis=1, concat_axis=0, tiled=True)
    seg_dt = lax.all_to_all(dt_in, "tp", split_axis=1, concat_axis=0, tiled=True)
    seg_len = seg_x.shape[0]
    blocks = seg_len // BLOCK
    seg_b = seg_bc[:, 0].reshape(blocks, BLOCK, N)
    seg_c = seg_bc[:, 1].reshape(blocks, BLOCK, N)

    bias_local = lax.dynamic_slice_in_dim(dt_bias, tp_index * local_heads, local_heads, 0)
    rate_local = lax.dynamic_slice_in_dim(a_log, tp_index * local_heads, local_heads, 0)
    skip_local = lax.dynamic_slice_in_dim(skip, tp_index * local_heads, local_heads, 0)
    step_size = jax.nn.softplus(seg_dt.astype(jnp.float32) + bias_local[None, :])
    log_decay = -step_size * jnp.exp(rate_local)[None, :]

    dt_blk = step_size.reshape(blocks, BLOCK, local_heads)
    cum = jnp.cumsum(log_decay.reshape(blocks, BLOCK, local_heads), axis=1)
    last = cum[:, -1]
    x_blk = seg_x.reshape(blocks, BLOCK, head_width)

    fresh = [fresh_block(x_blk[b], seg_b[b], cum[b], dt_blk[b]) for b in range(blocks)]
    block_decay = jnp.exp(last)
    starts = [None]
    state = fresh[0]
    prefix = [jnp.ones((local_heads,), jnp.float32)]
    for b in range(1, blocks):
        starts.append(state)
        prefix.append(prefix[-1] * block_decay[b - 1])
        state = head_columns(block_decay[b])[None, :] * state + fresh[b]
    final = state
    segment_decay = prefix[-1] * block_decay[blocks - 1]

    core = ctx_index % 2
    chip = ctx_index // 2
    chips = n_ctx // 2
    half_width = head_width // 2
    half_heads = local_heads // 2
    decay_slab = jnp.pad(segment_decay[None, :], ((0, 7), (0, head_width - local_heads)))
    mate = lax.ppermute(
        jnp.concatenate([final, decay_slab], axis=0), "ctx", [(i, i ^ 1) for i in range(n_ctx)]
    )
    mate_final = mate[:N]
    even_final = jnp.where(core == 0, final, mate_final)
    odd_final = jnp.where(core == 0, mate_final, final)
    odd_decay = jnp.where(core == 0, mate[N, :local_heads], segment_decay)
    lo = core * half_width
    chip_half = head_columns(lax.dynamic_slice_in_dim(odd_decay, core * half_heads, half_heads, 0))[
        None, :
    ] * lax.dynamic_slice_in_dim(even_final, lo, half_width, 1) + lax.dynamic_slice_in_dim(
        odd_final, lo, half_width, 1
    )
    mate_decay = mate[N, :local_heads]
    chip_decay = head_columns(
        lax.dynamic_slice_in_dim(segment_decay * mate_decay, core * half_heads, half_heads, 0)
    )[None, :]
    pieces = 4 if N % 32 == 0 else 1
    piece_rows = N // pieces
    own_pieces = chip_half.reshape(pieces, piece_rows, half_width)

    skip_cols = head_columns(skip_local)
    scores = [
        jnp.einsum("in,jn->ij", seg_c[b], seg_b[b], preferred_element_type=jnp.float32)
        for b in range(blocks)
    ]

    def run_intra(_):
        return [intra_block(x_blk[b], scores[b], cum[b], dt_blk[b], skip_cols) for b in range(blocks)]

    def no_intra(_):
        return [jnp.zeros((BLOCK, head_width), jnp.float32) for _ in range(blocks)]

    early = chip >= 2
    ahead = lax.cond(early, run_intra, no_intra, 0)
    own_pieces = lax.optimization_barrier((own_pieces, ahead))[0]

    acc = jnp.zeros((pieces, piece_rows, half_width), jnp.float32)
    for s in range(chips - 2 + pieces):
        pairs = [
            (2 * r + q, 2 * r + 2 + q) for r in range(chips - 1) if 0 <= s - r < pieces for q in range(2)
        ]
        send_piece = jnp.clip(s - chip, 0, pieces - 1)
        send = chip_decay * lax.dynamic_index_in_dim(acc, send_piece, 0, False) + lax.dynamic_index_in_dim(
            own_pieces, send_piece, 0, False
        )
        got = lax.ppermute(send, "ctx", pairs)
        recv_piece = jnp.clip(s - chip + 1, 0, pieces - 1)
        acc = lax.dynamic_update_index_in_dim(
            acc, lax.dynamic_index_in_dim(acc, recv_piece, 0, False) + got, recv_piece, 0
        )
    acc, ahead = lax.optimization_barrier((acc, ahead))
    partials = lax.cond(early, lambda a: a, run_intra, ahead)
    prefix_half = acc.reshape(N, half_width)
    mate_prefix = lax.ppermute(prefix_half, "ctx", [(i, i ^ 1) for i in range(n_ctx)])
    chip_prefix = jnp.concatenate(
        [jnp.where(core == 0, prefix_half, mate_prefix), jnp.where(core == 0, mate_prefix, prefix_half)],
        axis=1,
    )
    incoming = jnp.where(
        core == 1, head_columns(mate_decay)[None, :] * chip_prefix + mate_final, chip_prefix
    )

    results = []
    for b in range(blocks):
        carried_state = head_columns(prefix[b])[None, :] * incoming
        if starts[b] is not None:
            carried_state = starts[b] + carried_state
        state_hi = lax.reduce_precision(carried_state, exponent_bits=8, mantissa_bits=7)
        state_lo = (carried_state - state_hi).astype(jnp.bfloat16)
        projected = jnp.dot(
            seg_c[b], state_hi.astype(jnp.bfloat16), preferred_element_type=jnp.float32
        ) + jnp.dot(seg_c[b], state_lo, preferred_element_type=jnp.float32)
        inter = head_columns(jnp.exp(cum[b])) * projected
        results.append((partials[b] + inter).astype(jnp.bfloat16))
    result = jnp.concatenate(results, axis=0) if blocks > 1 else results[0]
    return lax.all_to_all(result, "tp", split_axis=0, concat_axis=1, tiled=True)


def solution(mesh):
    return jax.shard_map(
        on_device,
        mesh=mesh,
        in_specs=(
            P(("ctx", "tp"), None),
            P(("ctx", "tp"), None),
            P(("ctx", "tp"), None),
            P(),
            P(),
            P(),
            P(),
            P(),
            P(),
            P(),
        ),
        out_specs=P(("ctx", "tp"), None),
        check_vma=False,
    )
```

```python
import numpy as np
import jax
import jax.numpy as jnp
from jax import lax
from jax.sharding import PartitionSpec as P
from jax.experimental import pallas as pl
from jax.experimental.pallas import tpu as pltpu

H = 128
P_SIZE = 64
N = 256
G = 4
CONV = 4
BLOCK = 512


def from_behind(value, axis, steps):
    count = lax.axis_size(axis)
    initial, last = (max(0, -steps), min(count, count - steps))
    return lax.ppermute(value, axis, [(source, source + steps) for source in range(initial, last)])


def conv_rows(full, rows, weight, bias):
    total = bias[None, :] + weight[0][None, :] * full[0:rows]
    for k in range(1, CONV):
        total = total + weight[k][None, :] * full[k : k + rows]
    return jax.nn.silu(total).astype(jnp.bfloat16)


def conv_silu(raw, prior, weight, bias):
    rows = raw.shape[0]
    rim = CONV - 1
    zero_prior = jnp.zeros((rim, raw.shape[1]), jnp.float32)
    body = conv_rows(jnp.concatenate([zero_prior, raw.astype(jnp.float32)], axis=0), rows, weight, bias)
    edge = jnp.concatenate([prior, raw[:rim]], axis=0).astype(jnp.float32)
    return lax.dynamic_update_slice_in_dim(body, conv_rows(edge, rim, weight, bias), 0, 0)


def intra_kernel(x_ref, s_ref, cum_ref, cumt_ref, dtt_ref, skip_ref, o_ref):
    tiles = BLOCK // 128
    lane_head = lax.broadcasted_iota(jnp.int32, cum_ref.shape, 1)
    row_head = lax.broadcasted_iota(jnp.int32, cumt_ref.shape, 0)
    lane = lax.broadcasted_iota(jnp.int32, (128, 128), 1)

    def pair(p, carry):
        off = pl.multiple_of(p * 128, 128)
        xp = x_ref[:, pl.ds(off, 128)]
        cum_all = cum_ref[...]
        cumt_all = cumt_ref[...]
        dtt_all = dtt_ref[...]
        cols, rows, dts = [], [], []
        for k in range(2):
            h = 2 * p + k
            cols.append(jnp.sum(jnp.where(lane_head == h, cum_all, 0.0), axis=1, keepdims=True))
            rows.append(jnp.sum(jnp.where(row_head == h, cumt_all, 0.0), axis=0, keepdims=True))
            dts.append(jnp.sum(jnp.where(row_head == h, dtt_all, 0.0), axis=0, keepdims=True))
        skip_p = skip_ref[:, pl.ds(off, 128)]
        for r in range(tiles):
            width = (r + 1) * 128
            s_tile = s_ref[r * 128 : width, 0:width]
            lower = lax.broadcasted_iota(jnp.int32, (128, width), 1) <= (
                lax.broadcasted_iota(jnp.int32, (128, width), 0) + r * 128
            )
            res = []
            for k in range(2):
                gap = cols[k][r * 128 : width] - rows[k][:, 0:width]
                decay = jnp.where(lower, jnp.exp(jnp.where(lower, gap, 0.0)), 0.0)
                w = (s_tile * decay * dts[k][:, 0:width]).astype(jnp.bfloat16)
                res.append(jnp.dot(w, xp[0:width], preferred_element_type=jnp.float32))
            out = jnp.where(lane < P_SIZE, res[0], res[1])
            o_ref[r * 128 : width, pl.ds(off, 128)] = out + skip_p * xp[r * 128 : width].astype(jnp.float32)
        return carry

    lax.fori_loop(0, x_ref.shape[1] // 128, pair, 0)


def intra_block(x, scores, cum, dt, skip_cols):
    heads = cum.shape[1]
    width = x.shape[1]
    cum_lanes = jnp.pad(cum, ((0, 0), (0, 128 - heads)))
    pad_rows = (-heads) % 8
    cum_rows = jnp.pad(cum.T, ((0, pad_rows), (0, 0)))
    dt_rows = jnp.pad(dt.T, ((0, pad_rows), (0, 0)))
    vmem = pl.BlockSpec(memory_space=pltpu.VMEM)
    return pl.pallas_call(
        intra_kernel,
        out_shape=jax.ShapeDtypeStruct((BLOCK, width), jnp.float32),
        in_specs=[vmem] * 6,
        out_specs=vmem,
        name="ssd_intra",
        cost_estimate=pl.CostEstimate(
            flops=2 * BLOCK * BLOCK * width * 2,
            transcendentals=heads * BLOCK * BLOCK,
            bytes_accessed=BLOCK * width * 6 + BLOCK * BLOCK * 4,
        ),
    )(x, scores, cum_lanes, cum_rows, dt_rows, skip_cols[None, :])


def fresh_kernel(x_ref, bt_ref, fac_ref, o_ref):
    def pair(p, carry):
        off = pl.multiple_of(p * 128, 128)
        xp = x_ref[:, pl.ds(off, 128)].astype(jnp.float32)
        wx = (fac_ref[:, pl.ds(off, 128)] * xp).astype(jnp.bfloat16)
        o_ref[:, pl.ds(off, 128)] = jnp.dot(bt_ref[...], wx, preferred_element_type=jnp.float32)
        return carry

    lax.fori_loop(0, x_ref.shape[1] // 128, pair, 0)


def fresh_block(x, b, cum, dt):
    heads = cum.shape[1]
    width = x.shape[1]
    factors = head_columns(jnp.exp(cum[BLOCK - 1 :] - cum) * dt)
    vmem = pl.BlockSpec(memory_space=pltpu.VMEM)
    return pl.pallas_call(
        fresh_kernel,
        out_shape=jax.ShapeDtypeStruct((N, width), jnp.float32),
        in_specs=[vmem] * 3,
        out_specs=vmem,
        name="ssd_fresh",
        cost_estimate=pl.CostEstimate(
            flops=2 * BLOCK * N * width,
            transcendentals=0,
            bytes_accessed=BLOCK * width * 6 + N * width * 4 + BLOCK * N * 2,
        ),
    )(x, b.T, factors)


def head_columns(head_major):
    return jnp.repeat(head_major, P_SIZE, axis=-1)


def on_device(
    x_in,
    bc_in,
    dt_in,
    conv_x_weight,
    conv_x_bias,
    conv_bc_weight,
    conv_bc_bias,
    dt_bias,
    a_log,
    skip,
):
    n_tp = lax.axis_size("tp")
    tp_index = lax.axis_index("tp")
    n_ctx = lax.axis_size("ctx")
    ctx_index = lax.axis_index("ctx")
    rows = x_in.shape[0]
    local_heads = H // n_tp
    head_width = local_heads * P_SIZE
    per_group = H // G
    rim = CONV - 1

    prior_x, prior_bc = from_behind((x_in[rows - rim :], bc_in[rows - rim :]), ("ctx", "tp"), 1)
    x_part = conv_silu(x_in, prior_x, conv_x_weight, conv_x_bias)
    bc_part = conv_silu(bc_in, prior_bc, conv_bc_weight, conv_bc_bias)

    group_of = [(k * local_heads) // per_group for k in range(n_tp)]
    bc_groups = bc_part.reshape(rows, 2, G, N)
    if group_of != list(range(G)):
        bc_groups = jnp.take(bc_groups, np.array(group_of), axis=2)
    bc_groups = jnp.transpose(bc_groups, (2, 0, 1, 3))
    seg_bc = lax.all_to_all(bc_groups, "tp", split_axis=0, concat_axis=0, tiled=True)
    seg_bc = seg_bc.reshape(n_tp * rows, 2, N)
    seg_x = lax.all_to_all(x_part, "tp", split_axis=1, concat_axis=0, tiled=True)
    seg_dt = lax.all_to_all(dt_in, "tp", split_axis=1, concat_axis=0, tiled=True)
    seg_len = seg_x.shape[0]
    blocks = seg_len // BLOCK
    seg_b = seg_bc[:, 0].reshape(blocks, BLOCK, N)
    seg_c = seg_bc[:, 1].reshape(blocks, BLOCK, N)

    bias_local = lax.dynamic_slice_in_dim(dt_bias, tp_index * local_heads, local_heads, 0)
    rate_local = lax.dynamic_slice_in_dim(a_log, tp_index * local_heads, local_heads, 0)
    skip_local = lax.dynamic_slice_in_dim(skip, tp_index * local_heads, local_heads, 0)
    step_size = jax.nn.softplus(seg_dt.astype(jnp.float32) + bias_local[None, :])
    log_decay = -step_size * jnp.exp(rate_local)[None, :]

    dt_blk = step_size.reshape(blocks, BLOCK, local_heads)
    cum = jnp.cumsum(log_decay.reshape(blocks, BLOCK, local_heads), axis=1)
    last = cum[:, -1]
    x_blk = seg_x.reshape(blocks, BLOCK, head_width)

    fresh = [fresh_block(x_blk[b], seg_b[b], cum[b], dt_blk[b]) for b in range(blocks)]
    block_decay = jnp.exp(last)
    starts = [None]
    state = fresh[0]
    prefix = [jnp.ones((local_heads,), jnp.float32)]
    for b in range(1, blocks):
        starts.append(state)
        prefix.append(prefix[-1] * block_decay[b - 1])
        state = head_columns(block_decay[b])[None, :] * state + fresh[b]
    final = state
    segment_decay = prefix[-1] * block_decay[blocks - 1]

    core = ctx_index % 2
    chip = ctx_index // 2
    chips = n_ctx // 2
    half_width = head_width // 2
    half_heads = local_heads // 2
    decay_slab = jnp.pad(segment_decay[None, :], ((0, 7), (0, head_width - local_heads)))
    mate = lax.ppermute(
        jnp.concatenate([final, decay_slab], axis=0), "ctx", [(i, i ^ 1) for i in range(n_ctx)]
    )
    mate_final = mate[:N]
    even_final = jnp.where(core == 0, final, mate_final)
    odd_final = jnp.where(core == 0, mate_final, final)
    odd_decay = jnp.where(core == 0, mate[N, :local_heads], segment_decay)
    lo = core * half_width
    chip_half = head_columns(lax.dynamic_slice_in_dim(odd_decay, core * half_heads, half_heads, 0))[
        None, :
    ] * lax.dynamic_slice_in_dim(even_final, lo, half_width, 1) + lax.dynamic_slice_in_dim(
        odd_final, lo, half_width, 1
    )
    mate_decay = mate[N, :local_heads]
    chip_decay = head_columns(
        lax.dynamic_slice_in_dim(segment_decay * mate_decay, core * half_heads, half_heads, 0)
    )[None, :]
    pieces = 4 if N % 32 == 0 else 1
    piece_rows = N // pieces
    acc = [jnp.zeros((piece_rows, half_width), jnp.float32) for _ in range(pieces)]
    skip_cols = head_columns(skip_local)
    scores = [
        jnp.einsum("in,jn->ij", seg_c[b], seg_b[b], preferred_element_type=jnp.float32)
        for b in range(blocks)
    ]

    def intra_after(tie):
        parts = []
        for b in range(blocks):
            operands = (x_blk[b], scores[b], cum[b], dt_blk[b])
            if tie is not None:
                operands = lax.optimization_barrier(operands + (tie,))[:4]
            parts.append(intra_block(*operands, skip_cols))
        return parts

    partials = None
    last_send = None
    for r in range(chips - 1):
        if r == chips - 2 and r >= 1:
            partials = intra_after(last_send)
            acc = list(lax.optimization_barrier((tuple(acc), partials))[0])
        pairs = [(2 * r + q, 2 * r + 2 + q) for q in range(2)]
        for k in range(pieces):
            send = chip_decay * acc[k] + chip_half[k * piece_rows : (k + 1) * piece_rows]
            acc[k] = acc[k] + lax.ppermute(send, "ctx", pairs)
            last_send = send
    if partials is None:
        partials = intra_after(last_send)
    prefix_half = jnp.concatenate(acc, axis=0) if pieces > 1 else acc[0]
    mate_prefix = lax.ppermute(prefix_half, "ctx", [(i, i ^ 1) for i in range(n_ctx)])
    chip_prefix = jnp.concatenate(
        [jnp.where(core == 0, prefix_half, mate_prefix), jnp.where(core == 0, mate_prefix, prefix_half)],
        axis=1,
    )
    incoming = jnp.where(
        core == 1, head_columns(mate_decay)[None, :] * chip_prefix + mate_final, chip_prefix
    )

    results = []
    for b in range(blocks):
        carried_state = head_columns(prefix[b])[None, :] * incoming
        if starts[b] is not None:
            carried_state = starts[b] + carried_state
        state_hi = lax.reduce_precision(carried_state, exponent_bits=8, mantissa_bits=7)
        state_lo = (carried_state - state_hi).astype(jnp.bfloat16)
        projected = jnp.dot(
            seg_c[b], state_hi.astype(jnp.bfloat16), preferred_element_type=jnp.float32
        ) + jnp.dot(seg_c[b], state_lo, preferred_element_type=jnp.float32)
        inter = head_columns(jnp.exp(cum[b])) * projected
        results.append((partials[b] + inter).astype(jnp.bfloat16))
    result = jnp.concatenate(results, axis=0) if blocks > 1 else results[0]
    return lax.all_to_all(result, "tp", split_axis=0, concat_axis=1, tiled=True)


def solution(mesh):
    return jax.shard_map(
        on_device,
        mesh=mesh,
        in_specs=(
            P(("ctx", "tp"), None),
            P(("ctx", "tp"), None),
            P(("ctx", "tp"), None),
            P(),
            P(),
            P(),
            P(),
            P(),
            P(),
            P(),
        ),
        out_specs=P(("ctx", "tp"), None),
        check_vma=False,
    )
```

```python
import numpy as np
import jax
import jax.numpy as jnp
from jax import lax
from jax.sharding import PartitionSpec as P
from jax.experimental import pallas as pl
from jax.experimental.pallas import tpu as pltpu

H = 128
P_SIZE = 64
N = 256
G = 4
CONV = 4
BLOCK = 512


def from_behind(value, axis, steps):
    count = lax.axis_size(axis)
    initial, last = (max(0, -steps), min(count, count - steps))
    return lax.ppermute(value, axis, [(source, source + steps) for source in range(initial, last)])


def conv_rows(full, rows, weight, bias):
    total = bias[None, :] + weight[0][None, :] * full[0:rows]
    for k in range(1, CONV):
        total = total + weight[k][None, :] * full[k : k + rows]
    return jax.nn.silu(total).astype(jnp.bfloat16)


def conv_silu(raw, prior, weight, bias):
    rows = raw.shape[0]
    rim = CONV - 1
    zero_prior = jnp.zeros((rim, raw.shape[1]), jnp.float32)
    body = conv_rows(jnp.concatenate([zero_prior, raw.astype(jnp.float32)], axis=0), rows, weight, bias)
    edge = jnp.concatenate([prior, raw[:rim]], axis=0).astype(jnp.float32)
    return lax.dynamic_update_slice_in_dim(body, conv_rows(edge, rim, weight, bias), 0, 0)


def intra_kernel(x_ref, s_ref, cum_ref, cumt_ref, dtt_ref, skip_ref, o_ref):
    tiles = BLOCK // 128
    lane_head = lax.broadcasted_iota(jnp.int32, cum_ref.shape, 1)
    row_head = lax.broadcasted_iota(jnp.int32, cumt_ref.shape, 0)
    lane = lax.broadcasted_iota(jnp.int32, (128, 128), 1)

    def pair(p, carry):
        off = pl.multiple_of(p * 128, 128)
        xp = x_ref[:, pl.ds(off, 128)]
        cum_all = cum_ref[...]
        cumt_all = cumt_ref[...]
        dtt_all = dtt_ref[...]
        cols, rows, dts = [], [], []
        for k in range(2):
            h = 2 * p + k
            cols.append(jnp.sum(jnp.where(lane_head == h, cum_all, 0.0), axis=1, keepdims=True))
            rows.append(jnp.sum(jnp.where(row_head == h, cumt_all, 0.0), axis=0, keepdims=True))
            dts.append(jnp.sum(jnp.where(row_head == h, dtt_all, 0.0), axis=0, keepdims=True))
        skip_p = skip_ref[:, pl.ds(off, 128)]
        for r in range(tiles):
            width = (r + 1) * 128
            s_tile = s_ref[r * 128 : width, 0:width]
            lower = lax.broadcasted_iota(jnp.int32, (128, width), 1) <= (
                lax.broadcasted_iota(jnp.int32, (128, width), 0) + r * 128
            )
            res = []
            for k in range(2):
                gap = cols[k][r * 128 : width] - rows[k][:, 0:width]
                decay = jnp.where(lower, jnp.exp(jnp.where(lower, gap, 0.0)), 0.0)
                w = (s_tile * decay * dts[k][:, 0:width]).astype(jnp.bfloat16)
                res.append(jnp.dot(w, xp[0:width], preferred_element_type=jnp.float32))
            out = jnp.where(lane < P_SIZE, res[0], res[1])
            o_ref[r * 128 : width, pl.ds(off, 128)] = out + skip_p * xp[r * 128 : width].astype(jnp.float32)
        return carry

    lax.fori_loop(0, x_ref.shape[1] // 128, pair, 0)


def intra_block(x, scores, cum, dt, skip_cols):
    heads = cum.shape[1]
    width = x.shape[1]
    cum_lanes = jnp.pad(cum, ((0, 0), (0, 128 - heads)))
    pad_rows = (-heads) % 8
    cum_rows = jnp.pad(cum.T, ((0, pad_rows), (0, 0)))
    dt_rows = jnp.pad(dt.T, ((0, pad_rows), (0, 0)))
    vmem = pl.BlockSpec(memory_space=pltpu.VMEM)
    return pl.pallas_call(
        intra_kernel,
        out_shape=jax.ShapeDtypeStruct((BLOCK, width), jnp.float32),
        in_specs=[vmem] * 6,
        out_specs=vmem,
        name="ssd_intra",
        cost_estimate=pl.CostEstimate(
            flops=2 * BLOCK * BLOCK * width * 2,
            transcendentals=heads * BLOCK * BLOCK,
            bytes_accessed=BLOCK * width * 6 + BLOCK * BLOCK * 4,
        ),
    )(x, scores, cum_lanes, cum_rows, dt_rows, skip_cols[None, :])


def fresh_kernel(x_ref, bt_ref, fac_ref, o_ref):
    def pair(p, carry):
        off = pl.multiple_of(p * 128, 128)
        xp = x_ref[:, pl.ds(off, 128)].astype(jnp.float32)
        wx = (fac_ref[:, pl.ds(off, 128)] * xp).astype(jnp.bfloat16)
        o_ref[:, pl.ds(off, 128)] = jnp.dot(bt_ref[...], wx, preferred_element_type=jnp.float32)
        return carry

    lax.fori_loop(0, x_ref.shape[1] // 128, pair, 0)


def fresh_block(x, b, cum, dt):
    heads = cum.shape[1]
    width = x.shape[1]
    factors = head_columns(jnp.exp(cum[BLOCK - 1 :] - cum) * dt)
    vmem = pl.BlockSpec(memory_space=pltpu.VMEM)
    return pl.pallas_call(
        fresh_kernel,
        out_shape=jax.ShapeDtypeStruct((N, width), jnp.float32),
        in_specs=[vmem] * 3,
        out_specs=vmem,
        name="ssd_fresh",
        cost_estimate=pl.CostEstimate(
            flops=2 * BLOCK * N * width,
            transcendentals=0,
            bytes_accessed=BLOCK * width * 6 + N * width * 4 + BLOCK * N * 2,
        ),
    )(x, b.T, factors)


def head_columns(head_major):
    return jnp.repeat(head_major, P_SIZE, axis=-1)


def on_device(
    x_in,
    bc_in,
    dt_in,
    conv_x_weight,
    conv_x_bias,
    conv_bc_weight,
    conv_bc_bias,
    dt_bias,
    a_log,
    skip,
):
    n_tp = lax.axis_size("tp")
    tp_index = lax.axis_index("tp")
    n_ctx = lax.axis_size("ctx")
    ctx_index = lax.axis_index("ctx")
    rows = x_in.shape[0]
    local_heads = H // n_tp
    head_width = local_heads * P_SIZE
    per_group = H // G
    rim = CONV - 1

    prior_x, prior_bc = from_behind((x_in[rows - rim :], bc_in[rows - rim :]), ("ctx", "tp"), 1)
    x_part = conv_silu(x_in, prior_x, conv_x_weight, conv_x_bias)
    bc_part = conv_silu(bc_in, prior_bc, conv_bc_weight, conv_bc_bias)

    group_of = [(k * local_heads) // per_group for k in range(n_tp)]
    bc_groups = bc_part.reshape(rows, 2, G, N)
    if group_of != list(range(G)):
        bc_groups = jnp.take(bc_groups, np.array(group_of), axis=2)
    bc_groups = jnp.transpose(bc_groups, (2, 0, 1, 3))
    seg_bc = lax.all_to_all(bc_groups, "tp", split_axis=0, concat_axis=0, tiled=True)
    seg_bc = seg_bc.reshape(n_tp * rows, 2, N)
    seg_x = lax.all_to_all(x_part, "tp", split_axis=1, concat_axis=0, tiled=True)
    seg_dt = lax.all_to_all(dt_in, "tp", split_axis=1, concat_axis=0, tiled=True)
    seg_len = seg_x.shape[0]
    blocks = seg_len // BLOCK
    seg_b = seg_bc[:, 0].reshape(blocks, BLOCK, N)
    seg_c = seg_bc[:, 1].reshape(blocks, BLOCK, N)

    bias_local = lax.dynamic_slice_in_dim(dt_bias, tp_index * local_heads, local_heads, 0)
    rate_local = lax.dynamic_slice_in_dim(a_log, tp_index * local_heads, local_heads, 0)
    skip_local = lax.dynamic_slice_in_dim(skip, tp_index * local_heads, local_heads, 0)
    step_size = jax.nn.softplus(seg_dt.astype(jnp.float32) + bias_local[None, :])
    log_decay = -step_size * jnp.exp(rate_local)[None, :]

    dt_blk = step_size.reshape(blocks, BLOCK, local_heads)
    cum = jnp.cumsum(log_decay.reshape(blocks, BLOCK, local_heads), axis=1)
    last = cum[:, -1]
    x_blk = seg_x.reshape(blocks, BLOCK, head_width)

    fresh = [fresh_block(x_blk[b], seg_b[b], cum[b], dt_blk[b]) for b in range(blocks)]
    block_decay = jnp.exp(last)
    starts = [None]
    state = fresh[0]
    prefix = [jnp.ones((local_heads,), jnp.float32)]
    for b in range(1, blocks):
        starts.append(state)
        prefix.append(prefix[-1] * block_decay[b - 1])
        state = head_columns(block_decay[b])[None, :] * state + fresh[b]
    final = state
    segment_decay = prefix[-1] * block_decay[blocks - 1]

    core = ctx_index % 2
    chip = ctx_index // 2
    chips = n_ctx // 2
    half_width = head_width // 2
    half_heads = local_heads // 2
    decay_slab = jnp.pad(segment_decay[None, :], ((0, 7), (0, head_width - local_heads)))
    mate = lax.ppermute(
        jnp.concatenate([final, decay_slab], axis=0), "ctx", [(i, i ^ 1) for i in range(n_ctx)]
    )
    mate_final = mate[:N]
    even_final = jnp.where(core == 0, final, mate_final)
    odd_final = jnp.where(core == 0, mate_final, final)
    odd_decay = jnp.where(core == 0, mate[N, :local_heads], segment_decay)
    lo = core * half_width
    chip_half = head_columns(lax.dynamic_slice_in_dim(odd_decay, core * half_heads, half_heads, 0))[
        None, :
    ] * lax.dynamic_slice_in_dim(even_final, lo, half_width, 1) + lax.dynamic_slice_in_dim(
        odd_final, lo, half_width, 1
    )
    mate_decay = mate[N, :local_heads]
    chip_decay = head_columns(
        lax.dynamic_slice_in_dim(segment_decay * mate_decay, core * half_heads, half_heads, 0)
    )[None, :]
    pieces = 4 if N % 32 == 0 else 1
    piece_rows = N // pieces
    acc = [jnp.zeros((piece_rows, half_width), jnp.float32) for _ in range(pieces)]
    skip_cols = head_columns(skip_local)
    scores = [
        jnp.einsum("in,jn->ij", seg_c[b], seg_b[b], preferred_element_type=jnp.float32)
        for b in range(blocks)
    ]

    def intra_after(tie):
        parts, reach = [], []
        for b in range(blocks):
            operands = (x_blk[b], scores[b], cum[b], dt_blk[b], head_columns(jnp.exp(cum[b])))
            if tie is not None:
                operands = lax.optimization_barrier(operands + (tie,))[:5]
            parts.append(intra_block(*operands[:4], skip_cols))
            reach.append(operands[4])
        return parts, reach

    partials = None
    last_send = None
    for r in range(chips - 1):
        if r == chips - 2 and r >= 1:
            partials, reach = intra_after(last_send)
            acc = list(lax.optimization_barrier((tuple(acc), partials, reach))[0])
        pairs = [(2 * r + q, 2 * r + 2 + q) for q in range(2)]
        for k in range(pieces):
            send = chip_decay * acc[k] + chip_half[k * piece_rows : (k + 1) * piece_rows]
            acc[k] = acc[k] + lax.ppermute(send, "ctx", pairs)
            last_send = send
    if partials is None:
        partials, reach = intra_after(last_send)
    prefix_half = jnp.concatenate(acc, axis=0) if pieces > 1 else acc[0]
    mate_prefix = lax.ppermute(prefix_half, "ctx", [(i, i ^ 1) for i in range(n_ctx)])
    chip_prefix = jnp.concatenate(
        [jnp.where(core == 0, prefix_half, mate_prefix), jnp.where(core == 0, mate_prefix, prefix_half)],
        axis=1,
    )
    incoming = jnp.where(
        core == 1, head_columns(mate_decay)[None, :] * chip_prefix + mate_final, chip_prefix
    )

    results = []
    for b in range(blocks):
        carried_state = head_columns(prefix[b])[None, :] * incoming
        if starts[b] is not None:
            carried_state = starts[b] + carried_state
        state_hi = lax.reduce_precision(carried_state, exponent_bits=8, mantissa_bits=7)
        state_lo = (carried_state - state_hi).astype(jnp.bfloat16)
        projected = jnp.dot(
            seg_c[b], state_hi.astype(jnp.bfloat16), preferred_element_type=jnp.float32
        ) + jnp.dot(seg_c[b], state_lo, preferred_element_type=jnp.float32)
        inter = reach[b] * projected
        results.append((partials[b] + inter).astype(jnp.bfloat16))
    result = jnp.concatenate(results, axis=0) if blocks > 1 else results[0]
    return lax.all_to_all(result, "tp", split_axis=0, concat_axis=1, tiled=True)


def solution(mesh):
    return jax.shard_map(
        on_device,
        mesh=mesh,
        in_specs=(
            P(("ctx", "tp"), None),
            P(("ctx", "tp"), None),
            P(("ctx", "tp"), None),
            P(),
            P(),
            P(),
            P(),
            P(),
            P(),
            P(),
        ),
        out_specs=P(("ctx", "tp"), None),
        check_vma=False,
    )
```

```python
import numpy as np
import jax
import jax.numpy as jnp
from jax import lax
from jax.sharding import PartitionSpec as P
from jax.experimental import pallas as pl
from jax.experimental.pallas import tpu as pltpu

H = 128
P_SIZE = 64
N = 256
G = 4
CONV = 4
BLOCK = 512


def from_behind(value, axis, steps):
    count = lax.axis_size(axis)
    initial, last = (max(0, -steps), min(count, count - steps))
    return lax.ppermute(value, axis, [(source, source + steps) for source in range(initial, last)])


def conv_rows(full, rows, weight, bias):
    total = bias[None, :] + weight[0][None, :] * full[0:rows]
    for k in range(1, CONV):
        total = total + weight[k][None, :] * full[k : k + rows]
    return jax.nn.silu(total).astype(jnp.bfloat16)


def conv_silu(raw, prior, weight, bias):
    rows = raw.shape[0]
    rim = CONV - 1
    zero_prior = jnp.zeros((rim, raw.shape[1]), jnp.float32)
    body = conv_rows(jnp.concatenate([zero_prior, raw.astype(jnp.float32)], axis=0), rows, weight, bias)
    edge = jnp.concatenate([prior, raw[:rim]], axis=0).astype(jnp.float32)
    return lax.dynamic_update_slice_in_dim(body, conv_rows(edge, rim, weight, bias), 0, 0)


def intra_kernel(x_ref, s_ref, cum_ref, cumt_ref, dtt_ref, skip_ref, o_ref, reach_ref):
    tiles = BLOCK // 128
    lane_head = lax.broadcasted_iota(jnp.int32, cum_ref.shape, 1)
    row_head = lax.broadcasted_iota(jnp.int32, cumt_ref.shape, 0)
    lane = lax.broadcasted_iota(jnp.int32, (128, 128), 1)

    def pair(p, carry):
        off = pl.multiple_of(p * 128, 128)
        xp = x_ref[:, pl.ds(off, 128)]
        cum_all = cum_ref[...]
        cumt_all = cumt_ref[...]
        dtt_all = dtt_ref[...]
        cols, rows, dts = [], [], []
        for k in range(2):
            h = 2 * p + k
            cols.append(jnp.sum(jnp.where(lane_head == h, cum_all, 0.0), axis=1, keepdims=True))
            rows.append(jnp.sum(jnp.where(row_head == h, cumt_all, 0.0), axis=0, keepdims=True))
            dts.append(jnp.sum(jnp.where(row_head == h, dtt_all, 0.0), axis=0, keepdims=True))
        skip_p = skip_ref[:, pl.ds(off, 128)]
        pair_lane = lax.broadcasted_iota(jnp.int32, (BLOCK, 128), 1)
        reach_ref[:, pl.ds(off, 128)] = jnp.where(pair_lane < P_SIZE, jnp.exp(cols[0]), jnp.exp(cols[1]))
        for r in range(tiles):
            width = (r + 1) * 128
            s_tile = s_ref[r * 128 : width, 0:width]
            lower = lax.broadcasted_iota(jnp.int32, (128, width), 1) <= (
                lax.broadcasted_iota(jnp.int32, (128, width), 0) + r * 128
            )
            res = []
            for k in range(2):
                gap = cols[k][r * 128 : width] - rows[k][:, 0:width]
                decay = jnp.where(lower, jnp.exp(jnp.where(lower, gap, 0.0)), 0.0)
                w = (s_tile * decay * dts[k][:, 0:width]).astype(jnp.bfloat16)
                res.append(jnp.dot(w, xp[0:width], preferred_element_type=jnp.float32))
            out = jnp.where(lane < P_SIZE, res[0], res[1])
            o_ref[r * 128 : width, pl.ds(off, 128)] = out + skip_p * xp[r * 128 : width].astype(jnp.float32)
        return carry

    lax.fori_loop(0, x_ref.shape[1] // 128, pair, 0)


def intra_block(x, scores, cum, dt, skip_cols):
    heads = cum.shape[1]
    width = x.shape[1]
    cum_lanes = jnp.pad(cum, ((0, 0), (0, 128 - heads)))
    pad_rows = (-heads) % 8
    cum_rows = jnp.pad(cum.T, ((0, pad_rows), (0, 0)))
    dt_rows = jnp.pad(dt.T, ((0, pad_rows), (0, 0)))
    vmem = pl.BlockSpec(memory_space=pltpu.VMEM)
    return pl.pallas_call(
        intra_kernel,
        out_shape=(
            jax.ShapeDtypeStruct((BLOCK, width), jnp.float32),
            jax.ShapeDtypeStruct((BLOCK, width), jnp.float32),
        ),
        in_specs=[vmem] * 6,
        out_specs=(vmem, vmem),
        name="ssd_intra",
        cost_estimate=pl.CostEstimate(
            flops=2 * BLOCK * BLOCK * width * 2,
            transcendentals=heads * BLOCK * BLOCK,
            bytes_accessed=BLOCK * width * 6 + BLOCK * BLOCK * 4,
        ),
    )(x, scores, cum_lanes, cum_rows, dt_rows, skip_cols[None, :])


def fresh_kernel(x_ref, bt_ref, fac_ref, o_ref):
    def pair(p, carry):
        off = pl.multiple_of(p * 128, 128)
        xp = x_ref[:, pl.ds(off, 128)].astype(jnp.float32)
        wx = (fac_ref[:, pl.ds(off, 128)] * xp).astype(jnp.bfloat16)
        o_ref[:, pl.ds(off, 128)] = jnp.dot(bt_ref[...], wx, preferred_element_type=jnp.float32)
        return carry

    lax.fori_loop(0, x_ref.shape[1] // 128, pair, 0)


def fresh_block(x, b, cum, dt):
    heads = cum.shape[1]
    width = x.shape[1]
    factors = head_columns(jnp.exp(cum[BLOCK - 1 :] - cum) * dt)
    vmem = pl.BlockSpec(memory_space=pltpu.VMEM)
    return pl.pallas_call(
        fresh_kernel,
        out_shape=jax.ShapeDtypeStruct((N, width), jnp.float32),
        in_specs=[vmem] * 3,
        out_specs=vmem,
        name="ssd_fresh",
        cost_estimate=pl.CostEstimate(
            flops=2 * BLOCK * N * width,
            transcendentals=0,
            bytes_accessed=BLOCK * width * 6 + N * width * 4 + BLOCK * N * 2,
        ),
    )(x, b.T, factors)


def head_columns(head_major):
    return jnp.repeat(head_major, P_SIZE, axis=-1)


def on_device(
    x_in,
    bc_in,
    dt_in,
    conv_x_weight,
    conv_x_bias,
    conv_bc_weight,
    conv_bc_bias,
    dt_bias,
    a_log,
    skip,
):
    n_tp = lax.axis_size("tp")
    tp_index = lax.axis_index("tp")
    n_ctx = lax.axis_size("ctx")
    ctx_index = lax.axis_index("ctx")
    rows = x_in.shape[0]
    local_heads = H // n_tp
    head_width = local_heads * P_SIZE
    per_group = H // G
    rim = CONV - 1

    prior_x, prior_bc = from_behind((x_in[rows - rim :], bc_in[rows - rim :]), ("ctx", "tp"), 1)
    x_part = conv_silu(x_in, prior_x, conv_x_weight, conv_x_bias)
    bc_part = conv_silu(bc_in, prior_bc, conv_bc_weight, conv_bc_bias)

    group_of = [(k * local_heads) // per_group for k in range(n_tp)]
    bc_groups = bc_part.reshape(rows, 2, G, N)
    if group_of != list(range(G)):
        bc_groups = jnp.take(bc_groups, np.array(group_of), axis=2)
    bc_groups = jnp.transpose(bc_groups, (2, 0, 1, 3))
    seg_bc = lax.all_to_all(bc_groups, "tp", split_axis=0, concat_axis=0, tiled=True)
    seg_bc = seg_bc.reshape(n_tp * rows, 2, N)
    seg_x = lax.all_to_all(x_part, "tp", split_axis=1, concat_axis=0, tiled=True)
    seg_dt = lax.all_to_all(dt_in, "tp", split_axis=1, concat_axis=0, tiled=True)
    seg_len = seg_x.shape[0]
    blocks = seg_len // BLOCK
    seg_b = seg_bc[:, 0].reshape(blocks, BLOCK, N)
    seg_c = seg_bc[:, 1].reshape(blocks, BLOCK, N)

    bias_local = lax.dynamic_slice_in_dim(dt_bias, tp_index * local_heads, local_heads, 0)
    rate_local = lax.dynamic_slice_in_dim(a_log, tp_index * local_heads, local_heads, 0)
    skip_local = lax.dynamic_slice_in_dim(skip, tp_index * local_heads, local_heads, 0)
    step_size = jax.nn.softplus(seg_dt.astype(jnp.float32) + bias_local[None, :])
    log_decay = -step_size * jnp.exp(rate_local)[None, :]

    dt_blk = step_size.reshape(blocks, BLOCK, local_heads)
    cum = jnp.cumsum(log_decay.reshape(blocks, BLOCK, local_heads), axis=1)
    last = cum[:, -1]
    x_blk = seg_x.reshape(blocks, BLOCK, head_width)

    fresh = [fresh_block(x_blk[b], seg_b[b], cum[b], dt_blk[b]) for b in range(blocks)]
    block_decay = jnp.exp(last)
    starts = [None]
    state = fresh[0]
    prefix = [jnp.ones((local_heads,), jnp.float32)]
    for b in range(1, blocks):
        starts.append(state)
        prefix.append(prefix[-1] * block_decay[b - 1])
        state = head_columns(block_decay[b])[None, :] * state + fresh[b]
    final = state
    segment_decay = prefix[-1] * block_decay[blocks - 1]

    core = ctx_index % 2
    chip = ctx_index // 2
    chips = n_ctx // 2
    half_width = head_width // 2
    half_heads = local_heads // 2
    decay_slab = jnp.pad(segment_decay[None, :], ((0, 7), (0, head_width - local_heads)))
    mate = lax.ppermute(
        jnp.concatenate([final, decay_slab], axis=0), "ctx", [(i, i ^ 1) for i in range(n_ctx)]
    )
    mate_final = mate[:N]
    even_final = jnp.where(core == 0, final, mate_final)
    odd_final = jnp.where(core == 0, mate_final, final)
    odd_decay = jnp.where(core == 0, mate[N, :local_heads], segment_decay)
    lo = core * half_width
    chip_half = head_columns(lax.dynamic_slice_in_dim(odd_decay, core * half_heads, half_heads, 0))[
        None, :
    ] * lax.dynamic_slice_in_dim(even_final, lo, half_width, 1) + lax.dynamic_slice_in_dim(
        odd_final, lo, half_width, 1
    )
    mate_decay = mate[N, :local_heads]
    chip_decay = head_columns(
        lax.dynamic_slice_in_dim(segment_decay * mate_decay, core * half_heads, half_heads, 0)
    )[None, :]
    pieces = 4 if N % 32 == 0 else 1
    piece_rows = N // pieces
    acc = [jnp.zeros((piece_rows, half_width), jnp.float32) for _ in range(pieces)]
    skip_cols = head_columns(skip_local)
    scores = [
        jnp.einsum("in,jn->ij", seg_c[b], seg_b[b], preferred_element_type=jnp.float32)
        for b in range(blocks)
    ]

    def intra_after(tie):
        parts, reach = [], []
        for b in range(blocks):
            operands = (x_blk[b], scores[b], cum[b], dt_blk[b])
            if tie is not None:
                operands = lax.optimization_barrier(operands + (tie,))[:4]
            part, spread = intra_block(*operands, skip_cols)
            parts.append(part)
            reach.append(spread)
        return parts, reach

    partials = None
    last_send = None
    for r in range(chips - 1):
        if r == chips - 2 and r >= 1:
            partials, reach = intra_after(last_send)
            acc = list(lax.optimization_barrier((tuple(acc), partials, reach))[0])
        pairs = [(2 * r + q, 2 * r + 2 + q) for q in range(2)]
        for k in range(pieces):
            send = chip_decay * acc[k] + chip_half[k * piece_rows : (k + 1) * piece_rows]
            acc[k] = acc[k] + lax.ppermute(send, "ctx", pairs)
            last_send = send
    if partials is None:
        partials, reach = intra_after(last_send)
    prefix_half = jnp.concatenate(acc, axis=0) if pieces > 1 else acc[0]
    mate_prefix = lax.ppermute(prefix_half, "ctx", [(i, i ^ 1) for i in range(n_ctx)])
    chip_prefix = jnp.concatenate(
        [jnp.where(core == 0, prefix_half, mate_prefix), jnp.where(core == 0, mate_prefix, prefix_half)],
        axis=1,
    )
    incoming = jnp.where(
        core == 1, head_columns(mate_decay)[None, :] * chip_prefix + mate_final, chip_prefix
    )

    results = []
    for b in range(blocks):
        carried_state = head_columns(prefix[b])[None, :] * incoming
        if starts[b] is not None:
            carried_state = starts[b] + carried_state
        state_hi = lax.reduce_precision(carried_state, exponent_bits=8, mantissa_bits=7)
        state_lo = (carried_state - state_hi).astype(jnp.bfloat16)
        projected = jnp.dot(
            seg_c[b], state_hi.astype(jnp.bfloat16), preferred_element_type=jnp.float32
        ) + jnp.dot(seg_c[b], state_lo, preferred_element_type=jnp.float32)
        inter = reach[b] * projected
        results.append((partials[b] + inter).astype(jnp.bfloat16))
    result = jnp.concatenate(results, axis=0) if blocks > 1 else results[0]
    return lax.all_to_all(result, "tp", split_axis=0, concat_axis=1, tiled=True)


def solution(mesh):
    return jax.shard_map(
        on_device,
        mesh=mesh,
        in_specs=(
            P(("ctx", "tp"), None),
            P(("ctx", "tp"), None),
            P(("ctx", "tp"), None),
            P(),
            P(),
            P(),
            P(),
            P(),
            P(),
            P(),
        ),
        out_specs=P(("ctx", "tp"), None),
        check_vma=False,
    )
```

```python
import numpy as np
import jax
import jax.numpy as jnp
from jax import lax
from jax.sharding import PartitionSpec as P
from jax.experimental import pallas as pl
from jax.experimental.pallas import tpu as pltpu

H = 128
P_SIZE = 64
N = 256
G = 4
CONV = 4
BLOCK = 512


def from_behind(value, axis, steps):
    count = lax.axis_size(axis)
    initial, last = (max(0, -steps), min(count, count - steps))
    return lax.ppermute(value, axis, [(source, source + steps) for source in range(initial, last)])


def conv_rows(full, rows, weight, bias):
    total = bias[None, :] + weight[0][None, :] * full[0:rows]
    for k in range(1, CONV):
        total = total + weight[k][None, :] * full[k : k + rows]
    return jax.nn.silu(total).astype(jnp.bfloat16)


def conv_silu(raw, prior, weight, bias):
    rows = raw.shape[0]
    rim = CONV - 1
    zero_prior = jnp.zeros((rim, raw.shape[1]), jnp.float32)
    body = conv_rows(jnp.concatenate([zero_prior, raw.astype(jnp.float32)], axis=0), rows, weight, bias)
    edge = jnp.concatenate([prior, raw[:rim]], axis=0).astype(jnp.float32)
    return lax.dynamic_update_slice_in_dim(body, conv_rows(edge, rim, weight, bias), 0, 0)


def intra_kernel(x_ref, s_ref, cum_ref, cumt_ref, dtt_ref, skip_ref, o_ref, reach_ref):
    tiles = BLOCK // 128
    lane_head = lax.broadcasted_iota(jnp.int32, cum_ref.shape, 1)
    row_head = lax.broadcasted_iota(jnp.int32, cumt_ref.shape, 0)
    lane = lax.broadcasted_iota(jnp.int32, (128, 128), 1)

    def pair(p, carry):
        off = pl.multiple_of(p * 128, 128)
        xp = x_ref[:, pl.ds(off, 128)]
        cum_all = cum_ref[...]
        cumt_all = cumt_ref[...]
        dtt_all = dtt_ref[...]
        cols, rows, dts = [], [], []
        for k in range(2):
            h = 2 * p + k
            cols.append(jnp.sum(jnp.where(lane_head == h, cum_all, 0.0), axis=1, keepdims=True))
            rows.append(jnp.sum(jnp.where(row_head == h, cumt_all, 0.0), axis=0, keepdims=True))
            dts.append(jnp.sum(jnp.where(row_head == h, dtt_all, 0.0), axis=0, keepdims=True))
        skip_p = skip_ref[:, pl.ds(off, 128)]
        pair_lane = lax.broadcasted_iota(jnp.int32, (BLOCK, 128), 1)
        reach_ref[:, pl.ds(off, 128)] = jnp.where(pair_lane < P_SIZE, jnp.exp(cols[0]), jnp.exp(cols[1]))
        for r in range(tiles):
            width = (r + 1) * 128
            s_tile = s_ref[r * 128 : width, 0:width]
            lower = lax.broadcasted_iota(jnp.int32, (128, width), 1) <= (
                lax.broadcasted_iota(jnp.int32, (128, width), 0) + r * 128
            )
            res = []
            for k in range(2):
                gap = cols[k][r * 128 : width] - rows[k][:, 0:width]
                decay = jnp.where(lower, jnp.exp(jnp.where(lower, gap, 0.0)), 0.0)
                w = (s_tile * decay * dts[k][:, 0:width]).astype(jnp.bfloat16)
                res.append(jnp.dot(w, xp[0:width], preferred_element_type=jnp.float32))
            out = jnp.where(lane < P_SIZE, res[0], res[1])
            o_ref[r * 128 : width, pl.ds(off, 128)] = out + skip_p * xp[r * 128 : width].astype(jnp.float32)
        return carry

    lax.fori_loop(0, x_ref.shape[1] // 128, pair, 0)


def intra_block(x, scores, cum, dt, skip_cols):
    heads = cum.shape[1]
    width = x.shape[1]
    cum_lanes = jnp.pad(cum, ((0, 0), (0, 128 - heads)))
    pad_rows = (-heads) % 8
    cum_rows = jnp.pad(cum.T, ((0, pad_rows), (0, 0)))
    dt_rows = jnp.pad(dt.T, ((0, pad_rows), (0, 0)))
    vmem = pl.BlockSpec(memory_space=pltpu.VMEM)
    return pl.pallas_call(
        intra_kernel,
        out_shape=(
            jax.ShapeDtypeStruct((BLOCK, width), jnp.float32),
            jax.ShapeDtypeStruct((BLOCK, width), jnp.float32),
        ),
        in_specs=[vmem] * 6,
        out_specs=(vmem, vmem),
        name="ssd_intra",
        cost_estimate=pl.CostEstimate(
            flops=2 * BLOCK * BLOCK * width * 2,
            transcendentals=heads * BLOCK * BLOCK,
            bytes_accessed=BLOCK * width * 6 + BLOCK * BLOCK * 4,
        ),
    )(x, scores, cum_lanes, cum_rows, dt_rows, skip_cols[None, :])


def fresh_kernel(x_ref, bt_ref, fac_ref, o_ref):
    wx = (fac_ref[...] * x_ref[...].astype(jnp.float32)).astype(jnp.bfloat16)
    o_ref[...] = jnp.dot(bt_ref[...], wx, preferred_element_type=jnp.float32)


def fresh_block(x, b, cum, dt):
    heads = cum.shape[1]
    width = x.shape[1]
    factors = head_columns(jnp.exp(cum[BLOCK - 1 :] - cum) * dt)
    return pl.pallas_call(
        fresh_kernel,
        out_shape=jax.ShapeDtypeStruct((N, width), jnp.float32),
        grid=(width // 128,),
        in_specs=[
            pl.BlockSpec((BLOCK, 128), lambda p: (0, p)),
            pl.BlockSpec((N, BLOCK), lambda p: (0, 0)),
            pl.BlockSpec((BLOCK, 128), lambda p: (0, p)),
        ],
        out_specs=pl.BlockSpec((N, 128), lambda p: (0, p)),
        name="ssd_fresh",
        cost_estimate=pl.CostEstimate(
            flops=2 * BLOCK * N * width,
            transcendentals=0,
            bytes_accessed=BLOCK * width * 6 + N * width * 4 + BLOCK * N * 2,
        ),
    )(x, b.T, factors)


def head_columns(head_major):
    return jnp.repeat(head_major, P_SIZE, axis=-1)


def on_device(
    x_in,
    bc_in,
    dt_in,
    conv_x_weight,
    conv_x_bias,
    conv_bc_weight,
    conv_bc_bias,
    dt_bias,
    a_log,
    skip,
):
    n_tp = lax.axis_size("tp")
    tp_index = lax.axis_index("tp")
    n_ctx = lax.axis_size("ctx")
    ctx_index = lax.axis_index("ctx")
    rows = x_in.shape[0]
    local_heads = H // n_tp
    head_width = local_heads * P_SIZE
    per_group = H // G
    rim = CONV - 1

    prior_x, prior_bc = from_behind((x_in[rows - rim :], bc_in[rows - rim :]), ("ctx", "tp"), 1)
    x_part = conv_silu(x_in, prior_x, conv_x_weight, conv_x_bias)
    bc_part = conv_silu(bc_in, prior_bc, conv_bc_weight, conv_bc_bias)

    group_of = [(k * local_heads) // per_group for k in range(n_tp)]
    bc_groups = bc_part.reshape(rows, 2, G, N)
    if group_of != list(range(G)):
        bc_groups = jnp.take(bc_groups, np.array(group_of), axis=2)
    bc_groups = jnp.transpose(bc_groups, (2, 0, 1, 3))
    seg_bc = lax.all_to_all(bc_groups, "tp", split_axis=0, concat_axis=0, tiled=True)
    seg_bc = seg_bc.reshape(n_tp * rows, 2, N)
    seg_x = lax.all_to_all(x_part, "tp", split_axis=1, concat_axis=0, tiled=True)
    seg_dt = lax.all_to_all(dt_in, "tp", split_axis=1, concat_axis=0, tiled=True)
    seg_len = seg_x.shape[0]
    blocks = seg_len // BLOCK
    seg_b = seg_bc[:, 0].reshape(blocks, BLOCK, N)
    seg_c = seg_bc[:, 1].reshape(blocks, BLOCK, N)

    bias_local = lax.dynamic_slice_in_dim(dt_bias, tp_index * local_heads, local_heads, 0)
    rate_local = lax.dynamic_slice_in_dim(a_log, tp_index * local_heads, local_heads, 0)
    skip_local = lax.dynamic_slice_in_dim(skip, tp_index * local_heads, local_heads, 0)
    step_size = jax.nn.softplus(seg_dt.astype(jnp.float32) + bias_local[None, :])
    log_decay = -step_size * jnp.exp(rate_local)[None, :]

    dt_blk = step_size.reshape(blocks, BLOCK, local_heads)
    cum = jnp.cumsum(log_decay.reshape(blocks, BLOCK, local_heads), axis=1)
    last = cum[:, -1]
    x_blk = seg_x.reshape(blocks, BLOCK, head_width)

    fresh = [fresh_block(x_blk[b], seg_b[b], cum[b], dt_blk[b]) for b in range(blocks)]
    block_decay = jnp.exp(last)
    starts = [None]
    state = fresh[0]
    prefix = [jnp.ones((local_heads,), jnp.float32)]
    for b in range(1, blocks):
        starts.append(state)
        prefix.append(prefix[-1] * block_decay[b - 1])
        state = head_columns(block_decay[b])[None, :] * state + fresh[b]
    final = state
    segment_decay = prefix[-1] * block_decay[blocks - 1]

    core = ctx_index % 2
    chip = ctx_index // 2
    chips = n_ctx // 2
    half_width = head_width // 2
    half_heads = local_heads // 2
    decay_slab = jnp.pad(segment_decay[None, :], ((0, 7), (0, head_width - local_heads)))
    mate = lax.ppermute(
        jnp.concatenate([final, decay_slab], axis=0), "ctx", [(i, i ^ 1) for i in range(n_ctx)]
    )
    mate_final = mate[:N]
    even_final = jnp.where(core == 0, final, mate_final)
    odd_final = jnp.where(core == 0, mate_final, final)
    odd_decay = jnp.where(core == 0, mate[N, :local_heads], segment_decay)
    lo = core * half_width
    chip_half = head_columns(lax.dynamic_slice_in_dim(odd_decay, core * half_heads, half_heads, 0))[
        None, :
    ] * lax.dynamic_slice_in_dim(even_final, lo, half_width, 1) + lax.dynamic_slice_in_dim(
        odd_final, lo, half_width, 1
    )
    mate_decay = mate[N, :local_heads]
    chip_decay = head_columns(
        lax.dynamic_slice_in_dim(segment_decay * mate_decay, core * half_heads, half_heads, 0)
    )[None, :]
    pieces = 4 if N % 32 == 0 else 1
    piece_rows = N // pieces
    acc = [jnp.zeros((piece_rows, half_width), jnp.float32) for _ in range(pieces)]
    skip_cols = head_columns(skip_local)
    scores = [
        jnp.einsum("in,jn->ij", seg_c[b], seg_b[b], preferred_element_type=jnp.float32)
        for b in range(blocks)
    ]

    def intra_after(tie):
        parts, reach = [], []
        for b in range(blocks):
            operands = (x_blk[b], scores[b], cum[b], dt_blk[b])
            if tie is not None:
                operands = lax.optimization_barrier(operands + (tie,))[:4]
            part, spread = intra_block(*operands, skip_cols)
            parts.append(part)
            reach.append(spread)
        return parts, reach

    partials = None
    last_send = None
    for r in range(chips - 1):
        if r == chips - 2 and r >= 1:
            partials, reach = intra_after(last_send)
            acc = list(lax.optimization_barrier((tuple(acc), partials, reach))[0])
        pairs = [(2 * r + q, 2 * r + 2 + q) for q in range(2)]
        for k in range(pieces):
            send = chip_decay * acc[k] + chip_half[k * piece_rows : (k + 1) * piece_rows]
            acc[k] = acc[k] + lax.ppermute(send, "ctx", pairs)
            last_send = send
    if partials is None:
        partials, reach = intra_after(last_send)
    prefix_half = jnp.concatenate(acc, axis=0) if pieces > 1 else acc[0]
    mate_prefix = lax.ppermute(prefix_half, "ctx", [(i, i ^ 1) for i in range(n_ctx)])
    chip_prefix = jnp.concatenate(
        [jnp.where(core == 0, prefix_half, mate_prefix), jnp.where(core == 0, mate_prefix, prefix_half)],
        axis=1,
    )
    incoming = jnp.where(
        core == 1, head_columns(mate_decay)[None, :] * chip_prefix + mate_final, chip_prefix
    )

    results = []
    for b in range(blocks):
        carried_state = head_columns(prefix[b])[None, :] * incoming
        if starts[b] is not None:
            carried_state = starts[b] + carried_state
        state_hi = lax.reduce_precision(carried_state, exponent_bits=8, mantissa_bits=7)
        state_lo = (carried_state - state_hi).astype(jnp.bfloat16)
        projected = jnp.dot(
            seg_c[b], state_hi.astype(jnp.bfloat16), preferred_element_type=jnp.float32
        ) + jnp.dot(seg_c[b], state_lo, preferred_element_type=jnp.float32)
        inter = reach[b] * projected
        results.append((partials[b] + inter).astype(jnp.bfloat16))
    result = jnp.concatenate(results, axis=0) if blocks > 1 else results[0]
    return lax.all_to_all(result, "tp", split_axis=0, concat_axis=1, tiled=True)


def solution(mesh):
    return jax.shard_map(
        on_device,
        mesh=mesh,
        in_specs=(
            P(("ctx", "tp"), None),
            P(("ctx", "tp"), None),
            P(("ctx", "tp"), None),
            P(),
            P(),
            P(),
            P(),
            P(),
            P(),
            P(),
        ),
        out_specs=P(("ctx", "tp"), None),
        check_vma=False,
    )
```

```python
import numpy as np
import jax
import jax.numpy as jnp
from jax import lax
from jax.sharding import PartitionSpec as P
from jax.experimental import pallas as pl
from jax.experimental.pallas import tpu as pltpu

H = 128
P_SIZE = 64
N = 256
G = 4
CONV = 4
BLOCK = 512


def from_behind(value, axis, steps):
    count = lax.axis_size(axis)
    initial, last = (max(0, -steps), min(count, count - steps))
    return lax.ppermute(value, axis, [(source, source + steps) for source in range(initial, last)])


def conv_rows(full, rows, weight, bias):
    total = bias[None, :] + weight[0][None, :] * full[0:rows]
    for k in range(1, CONV):
        total = total + weight[k][None, :] * full[k : k + rows]
    return jax.nn.silu(total).astype(jnp.bfloat16)


def conv_silu(raw, prior, weight, bias):
    rows = raw.shape[0]
    rim = CONV - 1
    zero_prior = jnp.zeros((rim, raw.shape[1]), jnp.float32)
    body = conv_rows(jnp.concatenate([zero_prior, raw.astype(jnp.float32)], axis=0), rows, weight, bias)
    edge = jnp.concatenate([prior, raw[:rim]], axis=0).astype(jnp.float32)
    return lax.dynamic_update_slice_in_dim(body, conv_rows(edge, rim, weight, bias), 0, 0)


def intra_kernel(x_ref, s_ref, cum_ref, cumt_ref, dtt_ref, skip_ref, o_ref, reach_ref):
    tiles = BLOCK // 128
    lane_head = lax.broadcasted_iota(jnp.int32, cum_ref.shape, 1)
    row_head = lax.broadcasted_iota(jnp.int32, cumt_ref.shape, 0)
    lane = lax.broadcasted_iota(jnp.int32, (128, 128), 1)

    def pair(p, carry):
        off = pl.multiple_of(p * 128, 128)
        xp = x_ref[:, pl.ds(off, 128)]
        cum_all = cum_ref[...]
        cumt_all = cumt_ref[...]
        dtt_all = dtt_ref[...]
        cols, rows, dts = [], [], []
        for k in range(2):
            h = 2 * p + k
            cols.append(jnp.sum(jnp.where(lane_head == h, cum_all, 0.0), axis=1, keepdims=True))
            rows.append(jnp.sum(jnp.where(row_head == h, cumt_all, 0.0), axis=0, keepdims=True))
            dts.append(jnp.sum(jnp.where(row_head == h, dtt_all, 0.0), axis=0, keepdims=True))
        skip_p = skip_ref[:, pl.ds(off, 128)]
        pair_lane = lax.broadcasted_iota(jnp.int32, (BLOCK, 128), 1)
        reach_ref[:, pl.ds(off, 128)] = jnp.where(pair_lane < P_SIZE, jnp.exp(cols[0]), jnp.exp(cols[1]))
        for r in range(tiles):
            width = (r + 1) * 128
            s_tile = s_ref[r * 128 : width, 0:width]
            lower = lax.broadcasted_iota(jnp.int32, (128, width), 1) <= (
                lax.broadcasted_iota(jnp.int32, (128, width), 0) + r * 128
            )
            res = []
            for k in range(2):
                gap = cols[k][r * 128 : width] - rows[k][:, 0:width]
                decay = jnp.where(lower, jnp.exp(jnp.where(lower, gap, 0.0)), 0.0)
                w = (s_tile * decay * dts[k][:, 0:width]).astype(jnp.bfloat16)
                res.append(jnp.dot(w, xp[0:width], preferred_element_type=jnp.float32))
            out = jnp.where(lane < P_SIZE, res[0], res[1])
            o_ref[r * 128 : width, pl.ds(off, 128)] = out + skip_p * xp[r * 128 : width].astype(jnp.float32)
        return carry

    lax.fori_loop(0, x_ref.shape[1] // 128, pair, 0)


def intra_block(x, scores, cum, dt, skip_cols):
    heads = cum.shape[1]
    width = x.shape[1]
    cum_lanes = jnp.pad(cum, ((0, 0), (0, 128 - heads)))
    pad_rows = (-heads) % 8
    cum_rows = jnp.pad(cum.T, ((0, pad_rows), (0, 0)))
    dt_rows = jnp.pad(dt.T, ((0, pad_rows), (0, 0)))
    vmem = pl.BlockSpec(memory_space=pltpu.VMEM)
    return pl.pallas_call(
        intra_kernel,
        out_shape=(
            jax.ShapeDtypeStruct((BLOCK, width), jnp.float32),
            jax.ShapeDtypeStruct((BLOCK, width), jnp.float32),
        ),
        in_specs=[vmem] * 6,
        out_specs=(vmem, vmem),
        name="ssd_intra",
        cost_estimate=pl.CostEstimate(
            flops=2 * BLOCK * BLOCK * width * 2,
            transcendentals=heads * BLOCK * BLOCK,
            bytes_accessed=BLOCK * width * 6 + BLOCK * BLOCK * 4,
        ),
    )(x, scores, cum_lanes, cum_rows, dt_rows, skip_cols[None, :])


def fresh_kernel(x_ref, bt_ref, fac_ref, o_ref):
    def pair(p, carry):
        off = pl.multiple_of(p * 128, 128)
        xp = x_ref[:, pl.ds(off, 128)].astype(jnp.float32)
        wx = (fac_ref[:, pl.ds(off, 128)] * xp).astype(jnp.bfloat16)
        o_ref[:, pl.ds(off, 128)] = jnp.dot(bt_ref[...], wx, preferred_element_type=jnp.float32)
        return carry

    lax.fori_loop(0, x_ref.shape[1] // 128, pair, 0)


def fresh_block(x, b, cum, dt):
    heads = cum.shape[1]
    width = x.shape[1]
    factors = head_columns(jnp.exp(cum[BLOCK - 1 :] - cum) * dt)
    vmem = pl.BlockSpec(memory_space=pltpu.VMEM)
    return pl.pallas_call(
        fresh_kernel,
        out_shape=jax.ShapeDtypeStruct((N, width), jnp.float32),
        in_specs=[vmem] * 3,
        out_specs=vmem,
        name="ssd_fresh",
        cost_estimate=pl.CostEstimate(
            flops=2 * BLOCK * N * width,
            transcendentals=0,
            bytes_accessed=BLOCK * width * 6 + N * width * 4 + BLOCK * N * 2,
        ),
    )(x, b.T, factors)


def head_columns(head_major):
    return jnp.repeat(head_major, P_SIZE, axis=-1)


def on_device(
    x_in,
    bc_in,
    dt_in,
    conv_x_weight,
    conv_x_bias,
    conv_bc_weight,
    conv_bc_bias,
    dt_bias,
    a_log,
    skip,
):
    n_tp = lax.axis_size("tp")
    tp_index = lax.axis_index("tp")
    n_ctx = lax.axis_size("ctx")
    ctx_index = lax.axis_index("ctx")
    rows = x_in.shape[0]
    local_heads = H // n_tp
    head_width = local_heads * P_SIZE
    per_group = H // G
    rim = CONV - 1

    prior = from_behind(
        jnp.concatenate([x_in[rows - rim :], bc_in[rows - rim :]], axis=1), ("ctx", "tp"), 1
    )
    prior_x, prior_bc = prior[:, : x_in.shape[1]], prior[:, x_in.shape[1] :]
    x_part = conv_silu(x_in, prior_x, conv_x_weight, conv_x_bias)
    bc_part = conv_silu(bc_in, prior_bc, conv_bc_weight, conv_bc_bias)

    group_of = [(k * local_heads) // per_group for k in range(n_tp)]
    bc_groups = bc_part.reshape(rows, 2, G, N)
    if group_of != list(range(G)):
        bc_groups = jnp.take(bc_groups, np.array(group_of), axis=2)
    bc_groups = jnp.transpose(bc_groups, (2, 0, 1, 3))
    seg_bc = lax.all_to_all(bc_groups, "tp", split_axis=0, concat_axis=0, tiled=True)
    seg_bc = seg_bc.reshape(n_tp * rows, 2, N)
    seg_x = lax.all_to_all(x_part, "tp", split_axis=1, concat_axis=0, tiled=True)
    seg_dt = lax.all_to_all(dt_in, "tp", split_axis=1, concat_axis=0, tiled=True)
    seg_len = seg_x.shape[0]
    blocks = seg_len // BLOCK
    seg_b = seg_bc[:, 0].reshape(blocks, BLOCK, N)
    seg_c = seg_bc[:, 1].reshape(blocks, BLOCK, N)

    bias_local = lax.dynamic_slice_in_dim(dt_bias, tp_index * local_heads, local_heads, 0)
    rate_local = lax.dynamic_slice_in_dim(a_log, tp_index * local_heads, local_heads, 0)
    skip_local = lax.dynamic_slice_in_dim(skip, tp_index * local_heads, local_heads, 0)
    step_size = jax.nn.softplus(seg_dt.astype(jnp.float32) + bias_local[None, :])
    log_decay = -step_size * jnp.exp(rate_local)[None, :]

    dt_blk = step_size.reshape(blocks, BLOCK, local_heads)
    cum = jnp.cumsum(log_decay.reshape(blocks, BLOCK, local_heads), axis=1)
    last = cum[:, -1]
    x_blk = seg_x.reshape(blocks, BLOCK, head_width)

    fresh = [fresh_block(x_blk[b], seg_b[b], cum[b], dt_blk[b]) for b in range(blocks)]
    block_decay = jnp.exp(last)
    starts = [None]
    state = fresh[0]
    prefix = [jnp.ones((local_heads,), jnp.float32)]
    for b in range(1, blocks):
        starts.append(state)
        prefix.append(prefix[-1] * block_decay[b - 1])
        state = head_columns(block_decay[b])[None, :] * state + fresh[b]
    final = state
    segment_decay = prefix[-1] * block_decay[blocks - 1]

    core = ctx_index % 2
    chip = ctx_index // 2
    chips = n_ctx // 2
    half_width = head_width // 2
    half_heads = local_heads // 2
    decay_slab = jnp.pad(segment_decay[None, :], ((0, 7), (0, head_width - local_heads)))
    mate = lax.ppermute(
        jnp.concatenate([final, decay_slab], axis=0), "ctx", [(i, i ^ 1) for i in range(n_ctx)]
    )
    mate_final = mate[:N]
    even_final = jnp.where(core == 0, final, mate_final)
    odd_final = jnp.where(core == 0, mate_final, final)
    odd_decay = jnp.where(core == 0, mate[N, :local_heads], segment_decay)
    lo = core * half_width
    chip_half = head_columns(lax.dynamic_slice_in_dim(odd_decay, core * half_heads, half_heads, 0))[
        None, :
    ] * lax.dynamic_slice_in_dim(even_final, lo, half_width, 1) + lax.dynamic_slice_in_dim(
        odd_final, lo, half_width, 1
    )
    mate_decay = mate[N, :local_heads]
    chip_decay = head_columns(
        lax.dynamic_slice_in_dim(segment_decay * mate_decay, core * half_heads, half_heads, 0)
    )[None, :]
    pieces = 4 if N % 32 == 0 else 1
    piece_rows = N // pieces
    acc = [jnp.zeros((piece_rows, half_width), jnp.float32) for _ in range(pieces)]
    skip_cols = head_columns(skip_local)
    scores = [
        jnp.einsum("in,jn->ij", seg_c[b], seg_b[b], preferred_element_type=jnp.float32)
        for b in range(blocks)
    ]

    def intra_after(tie):
        parts, reach = [], []
        for b in range(blocks):
            operands = (x_blk[b], scores[b], cum[b], dt_blk[b])
            if tie is not None:
                operands = lax.optimization_barrier(operands + (tie,))[:4]
            part, spread = intra_block(*operands, skip_cols)
            parts.append(part)
            reach.append(spread)
        return parts, reach

    partials = None
    last_send = None
    for r in range(chips - 1):
        if r == chips - 2 and r >= 1:
            partials, reach = intra_after(last_send)
            acc = list(lax.optimization_barrier((tuple(acc), partials, reach))[0])
        pairs = [(2 * r + q, 2 * r + 2 + q) for q in range(2)]
        for k in range(pieces):
            send = chip_decay * acc[k] + chip_half[k * piece_rows : (k + 1) * piece_rows]
            acc[k] = acc[k] + lax.ppermute(send, "ctx", pairs)
            last_send = send
    if partials is None:
        partials, reach = intra_after(last_send)
    prefix_half = jnp.concatenate(acc, axis=0) if pieces > 1 else acc[0]
    mate_prefix = lax.ppermute(prefix_half, "ctx", [(i, i ^ 1) for i in range(n_ctx)])
    chip_prefix = jnp.concatenate(
        [jnp.where(core == 0, prefix_half, mate_prefix), jnp.where(core == 0, mate_prefix, prefix_half)],
        axis=1,
    )
    incoming = jnp.where(
        core == 1, head_columns(mate_decay)[None, :] * chip_prefix + mate_final, chip_prefix
    )

    results = []
    for b in range(blocks):
        carried_state = head_columns(prefix[b])[None, :] * incoming
        if starts[b] is not None:
            carried_state = starts[b] + carried_state
        state_hi = lax.reduce_precision(carried_state, exponent_bits=8, mantissa_bits=7)
        state_lo = (carried_state - state_hi).astype(jnp.bfloat16)
        projected = jnp.dot(
            seg_c[b], state_hi.astype(jnp.bfloat16), preferred_element_type=jnp.float32
        ) + jnp.dot(seg_c[b], state_lo, preferred_element_type=jnp.float32)
        inter = reach[b] * projected
        results.append((partials[b] + inter).astype(jnp.bfloat16))
    result = jnp.concatenate(results, axis=0) if blocks > 1 else results[0]
    return lax.all_to_all(result, "tp", split_axis=0, concat_axis=1, tiled=True)


def solution(mesh):
    return jax.shard_map(
        on_device,
        mesh=mesh,
        in_specs=(
            P(("ctx", "tp"), None),
            P(("ctx", "tp"), None),
            P(("ctx", "tp"), None),
            P(),
            P(),
            P(),
            P(),
            P(),
            P(),
            P(),
        ),
        out_specs=P(("ctx", "tp"), None),
        check_vma=False,
    )
```

```python
import numpy as np
import jax
import jax.numpy as jnp
from jax import lax
from jax.sharding import PartitionSpec as P
from jax.experimental import pallas as pl
from jax.experimental.pallas import tpu as pltpu

H = 128
P_SIZE = 64
N = 256
G = 4
CONV = 4
BLOCK = 512


def from_behind(value, axis, steps):
    count = lax.axis_size(axis)
    initial, last = (max(0, -steps), min(count, count - steps))
    return lax.ppermute(value, axis, [(source, source + steps) for source in range(initial, last)])


def conv_rows(full, rows, weight, bias):
    total = bias[None, :] + weight[0][None, :] * full[0:rows]
    for k in range(1, CONV):
        total = total + weight[k][None, :] * full[k : k + rows]
    return jax.nn.silu(total).astype(jnp.bfloat16)


def conv_silu(raw, prior, weight, bias):
    rows = raw.shape[0]
    rim = CONV - 1
    zero_prior = jnp.zeros((rim, raw.shape[1]), jnp.float32)
    body = conv_rows(jnp.concatenate([zero_prior, raw.astype(jnp.float32)], axis=0), rows, weight, bias)
    edge = jnp.concatenate([prior, raw[:rim]], axis=0).astype(jnp.float32)
    return lax.dynamic_update_slice_in_dim(body, conv_rows(edge, rim, weight, bias), 0, 0)


def intra_kernel(x_ref, s_ref, cum_ref, cumt_ref, dtt_ref, skip_ref, o_ref, reach_ref):
    tiles = BLOCK // 128
    lane_head = lax.broadcasted_iota(jnp.int32, cum_ref.shape, 1)
    row_head = lax.broadcasted_iota(jnp.int32, cumt_ref.shape, 0)
    lane = lax.broadcasted_iota(jnp.int32, (128, 128), 1)

    def pair(p, carry):
        off = pl.multiple_of(p * 128, 128)
        xp = x_ref[:, pl.ds(off, 128)]
        cum_all = cum_ref[...]
        cumt_all = cumt_ref[...]
        dtt_all = dtt_ref[...]
        cols, rows, dts = [], [], []
        for k in range(2):
            h = 2 * p + k
            cols.append(jnp.sum(jnp.where(lane_head == h, cum_all, 0.0), axis=1, keepdims=True))
            rows.append(jnp.sum(jnp.where(row_head == h, cumt_all, 0.0), axis=0, keepdims=True))
            dts.append(jnp.sum(jnp.where(row_head == h, dtt_all, 0.0), axis=0, keepdims=True))
        skip_p = skip_ref[:, pl.ds(off, 128)]
        pair_lane = lax.broadcasted_iota(jnp.int32, (BLOCK, 128), 1)
        reach_ref[:, pl.ds(off, 128)] = jnp.where(pair_lane < P_SIZE, jnp.exp(cols[0]), jnp.exp(cols[1]))
        for r in range(tiles):
            width = (r + 1) * 128
            s_tile = s_ref[r * 128 : width, 0:width]
            lower = lax.broadcasted_iota(jnp.int32, (128, width), 1) <= (
                lax.broadcasted_iota(jnp.int32, (128, width), 0) + r * 128
            )
            res = []
            for k in range(2):
                gap = cols[k][r * 128 : width] - rows[k][:, 0:width]
                decay = jnp.where(lower, jnp.exp(jnp.where(lower, gap, 0.0)), 0.0)
                w = (s_tile * decay * dts[k][:, 0:width]).astype(jnp.bfloat16)
                res.append(jnp.dot(w, xp[0:width], preferred_element_type=jnp.float32))
            out = jnp.where(lane < P_SIZE, res[0], res[1])
            o_ref[r * 128 : width, pl.ds(off, 128)] = out + skip_p * xp[r * 128 : width].astype(jnp.float32)
        return carry

    lax.fori_loop(0, x_ref.shape[1] // 128, pair, 0)


def intra_block(x, scores, cum, dt, skip_cols):
    heads = cum.shape[1]
    width = x.shape[1]
    cum_lanes = jnp.pad(cum, ((0, 0), (0, 128 - heads)))
    pad_rows = (-heads) % 8
    cum_rows = jnp.pad(cum.T, ((0, pad_rows), (0, 0)))
    dt_rows = jnp.pad(dt.T, ((0, pad_rows), (0, 0)))
    vmem = pl.BlockSpec(memory_space=pltpu.VMEM)
    return pl.pallas_call(
        intra_kernel,
        out_shape=(
            jax.ShapeDtypeStruct((BLOCK, width), jnp.float32),
            jax.ShapeDtypeStruct((BLOCK, width), jnp.float32),
        ),
        in_specs=[vmem] * 6,
        out_specs=(vmem, vmem),
        name="ssd_intra",
        cost_estimate=pl.CostEstimate(
            flops=2 * BLOCK * BLOCK * width * 2,
            transcendentals=heads * BLOCK * BLOCK,
            bytes_accessed=BLOCK * width * 6 + BLOCK * BLOCK * 4,
        ),
    )(x, scores, cum_lanes, cum_rows, dt_rows, skip_cols[None, :])


def fresh_kernel(x_ref, bt_ref, fac_ref, o_ref):
    def pair(p, carry):
        off = pl.multiple_of(p * 128, 128)
        xp = x_ref[:, pl.ds(off, 128)].astype(jnp.float32)
        wx = (fac_ref[:, pl.ds(off, 128)] * xp).astype(jnp.bfloat16)
        o_ref[:, pl.ds(off, 128)] = jnp.dot(bt_ref[...], wx, preferred_element_type=jnp.float32)
        return carry

    lax.fori_loop(0, x_ref.shape[1] // 128, pair, 0)


def fresh_block(x, b, cum, dt):
    heads = cum.shape[1]
    width = x.shape[1]
    factors = head_columns(jnp.exp(cum[BLOCK - 1 :] - cum) * dt)
    vmem = pl.BlockSpec(memory_space=pltpu.VMEM)
    return pl.pallas_call(
        fresh_kernel,
        out_shape=jax.ShapeDtypeStruct((N, width), jnp.float32),
        in_specs=[vmem] * 3,
        out_specs=vmem,
        name="ssd_fresh",
        cost_estimate=pl.CostEstimate(
            flops=2 * BLOCK * N * width,
            transcendentals=0,
            bytes_accessed=BLOCK * width * 6 + N * width * 4 + BLOCK * N * 2,
        ),
    )(x, b.T, factors)


def head_columns(head_major):
    return jnp.repeat(head_major, P_SIZE, axis=-1)


def on_device(
    x_in,
    bc_in,
    dt_in,
    conv_x_weight,
    conv_x_bias,
    conv_bc_weight,
    conv_bc_bias,
    dt_bias,
    a_log,
    skip,
):
    n_tp = lax.axis_size("tp")
    tp_index = lax.axis_index("tp")
    n_ctx = lax.axis_size("ctx")
    ctx_index = lax.axis_index("ctx")
    rows = x_in.shape[0]
    local_heads = H // n_tp
    head_width = local_heads * P_SIZE
    per_group = H // G
    rim = CONV - 1

    prior = from_behind(
        jnp.concatenate([x_in[rows - rim :], bc_in[rows - rim :]], axis=1), ("ctx", "tp"), 1
    )
    prior_x, prior_bc = prior[:, : x_in.shape[1]], prior[:, x_in.shape[1] :]
    x_part = conv_silu(x_in, prior_x, conv_x_weight, conv_x_bias)
    bc_part = conv_silu(bc_in, prior_bc, conv_bc_weight, conv_bc_bias)

    group_of = [(k * local_heads) // per_group for k in range(n_tp)]
    bc_groups = bc_part.reshape(rows, 2, G, N)
    if group_of != list(range(G)):
        bc_groups = jnp.take(bc_groups, np.array(group_of), axis=2)
    bc_groups = jnp.transpose(bc_groups, (2, 0, 1, 3)).reshape(n_tp, rows, 2 * N)
    packed = jnp.concatenate(
        [
            jnp.transpose(x_part.reshape(rows, n_tp, head_width), (1, 0, 2)),
            bc_groups,
            jnp.transpose(dt_in.reshape(rows, n_tp, local_heads), (1, 0, 2)),
        ],
        axis=2,
    )
    packed = lax.all_to_all(packed, "tp", split_axis=0, concat_axis=0, tiled=True)
    packed = packed.reshape(n_tp * rows, packed.shape[2])
    seg_x = packed[:, :head_width]
    seg_bc = packed[:, head_width : head_width + 2 * N].reshape(n_tp * rows, 2, N)
    seg_dt = packed[:, head_width + 2 * N :]
    seg_len = seg_x.shape[0]
    blocks = seg_len // BLOCK
    seg_b = seg_bc[:, 0].reshape(blocks, BLOCK, N)
    seg_c = seg_bc[:, 1].reshape(blocks, BLOCK, N)

    bias_local = lax.dynamic_slice_in_dim(dt_bias, tp_index * local_heads, local_heads, 0)
    rate_local = lax.dynamic_slice_in_dim(a_log, tp_index * local_heads, local_heads, 0)
    skip_local = lax.dynamic_slice_in_dim(skip, tp_index * local_heads, local_heads, 0)
    step_size = jax.nn.softplus(seg_dt.astype(jnp.float32) + bias_local[None, :])
    log_decay = -step_size * jnp.exp(rate_local)[None, :]

    dt_blk = step_size.reshape(blocks, BLOCK, local_heads)
    cum = jnp.cumsum(log_decay.reshape(blocks, BLOCK, local_heads), axis=1)
    last = cum[:, -1]
    x_blk = seg_x.reshape(blocks, BLOCK, head_width)

    fresh = [fresh_block(x_blk[b], seg_b[b], cum[b], dt_blk[b]) for b in range(blocks)]
    block_decay = jnp.exp(last)
    starts = [None]
    state = fresh[0]
    prefix = [jnp.ones((local_heads,), jnp.float32)]
    for b in range(1, blocks):
        starts.append(state)
        prefix.append(prefix[-1] * block_decay[b - 1])
        state = head_columns(block_decay[b])[None, :] * state + fresh[b]
    final = state
    segment_decay = prefix[-1] * block_decay[blocks - 1]

    core = ctx_index % 2
    chip = ctx_index // 2
    chips = n_ctx // 2
    half_width = head_width // 2
    half_heads = local_heads // 2
    decay_slab = jnp.pad(segment_decay[None, :], ((0, 7), (0, head_width - local_heads)))
    mate = lax.ppermute(
        jnp.concatenate([final, decay_slab], axis=0), "ctx", [(i, i ^ 1) for i in range(n_ctx)]
    )
    mate_final = mate[:N]
    even_final = jnp.where(core == 0, final, mate_final)
    odd_final = jnp.where(core == 0, mate_final, final)
    odd_decay = jnp.where(core == 0, mate[N, :local_heads], segment_decay)
    lo = core * half_width
    chip_half = head_columns(lax.dynamic_slice_in_dim(odd_decay, core * half_heads, half_heads, 0))[
        None, :
    ] * lax.dynamic_slice_in_dim(even_final, lo, half_width, 1) + lax.dynamic_slice_in_dim(
        odd_final, lo, half_width, 1
    )
    mate_decay = mate[N, :local_heads]
    chip_decay = head_columns(
        lax.dynamic_slice_in_dim(segment_decay * mate_decay, core * half_heads, half_heads, 0)
    )[None, :]
    pieces = 4 if N % 32 == 0 else 1
    piece_rows = N // pieces
    acc = [jnp.zeros((piece_rows, half_width), jnp.float32) for _ in range(pieces)]
    skip_cols = head_columns(skip_local)
    scores = [
        jnp.einsum("in,jn->ij", seg_c[b], seg_b[b], preferred_element_type=jnp.float32)
        for b in range(blocks)
    ]

    def intra_after(tie):
        parts, reach = [], []
        for b in range(blocks):
            operands = (x_blk[b], scores[b], cum[b], dt_blk[b])
            if tie is not None:
                operands = lax.optimization_barrier(operands + (tie,))[:4]
            part, spread = intra_block(*operands, skip_cols)
            parts.append(part)
            reach.append(spread)
        return parts, reach

    partials = None
    last_send = None
    for r in range(chips - 1):
        if r == chips - 2 and r >= 1:
            partials, reach = intra_after(last_send)
            acc = list(lax.optimization_barrier((tuple(acc), partials, reach))[0])
        pairs = [(2 * r + q, 2 * r + 2 + q) for q in range(2)]
        for k in range(pieces):
            send = chip_decay * acc[k] + chip_half[k * piece_rows : (k + 1) * piece_rows]
            acc[k] = acc[k] + lax.ppermute(send, "ctx", pairs)
            last_send = send
    if partials is None:
        partials, reach = intra_after(last_send)
    prefix_half = jnp.concatenate(acc, axis=0) if pieces > 1 else acc[0]
    mate_prefix = lax.ppermute(prefix_half, "ctx", [(i, i ^ 1) for i in range(n_ctx)])
    chip_prefix = jnp.concatenate(
        [jnp.where(core == 0, prefix_half, mate_prefix), jnp.where(core == 0, mate_prefix, prefix_half)],
        axis=1,
    )
    incoming = jnp.where(
        core == 1, head_columns(mate_decay)[None, :] * chip_prefix + mate_final, chip_prefix
    )

    results = []
    for b in range(blocks):
        carried_state = head_columns(prefix[b])[None, :] * incoming
        if starts[b] is not None:
            carried_state = starts[b] + carried_state
        state_hi = lax.reduce_precision(carried_state, exponent_bits=8, mantissa_bits=7)
        state_lo = (carried_state - state_hi).astype(jnp.bfloat16)
        projected = jnp.dot(
            seg_c[b], state_hi.astype(jnp.bfloat16), preferred_element_type=jnp.float32
        ) + jnp.dot(seg_c[b], state_lo, preferred_element_type=jnp.float32)
        inter = reach[b] * projected
        results.append((partials[b] + inter).astype(jnp.bfloat16))
    result = jnp.concatenate(results, axis=0) if blocks > 1 else results[0]
    return lax.all_to_all(result, "tp", split_axis=0, concat_axis=1, tiled=True)


def solution(mesh):
    return jax.shard_map(
        on_device,
        mesh=mesh,
        in_specs=(
            P(("ctx", "tp"), None),
            P(("ctx", "tp"), None),
            P(("ctx", "tp"), None),
            P(),
            P(),
            P(),
            P(),
            P(),
            P(),
            P(),
        ),
        out_specs=P(("ctx", "tp"), None),
        check_vma=False,
    )
```

```python
import numpy as np
import jax
import jax.numpy as jnp
from jax import lax
from jax.sharding import PartitionSpec as P
from jax.experimental import pallas as pl
from jax.experimental.pallas import tpu as pltpu

H = 128
P_SIZE = 64
N = 256
G = 4
CONV = 4
BLOCK = 512


def from_behind(value, axis, steps):
    count = lax.axis_size(axis)
    initial, last = (max(0, -steps), min(count, count - steps))
    return lax.ppermute(value, axis, [(source, source + steps) for source in range(initial, last)])


def conv_rows(full, rows, weight, bias):
    total = bias[None, :] + weight[0][None, :] * full[0:rows]
    for k in range(1, CONV):
        total = total + weight[k][None, :] * full[k : k + rows]
    return jax.nn.silu(total).astype(jnp.bfloat16)


def conv_silu(raw, prior, weight, bias):
    rows = raw.shape[0]
    rim = CONV - 1
    zero_prior = jnp.zeros((rim, raw.shape[1]), jnp.float32)
    body = conv_rows(jnp.concatenate([zero_prior, raw.astype(jnp.float32)], axis=0), rows, weight, bias)
    edge = jnp.concatenate([prior, raw[:rim]], axis=0).astype(jnp.float32)
    return lax.dynamic_update_slice_in_dim(body, conv_rows(edge, rim, weight, bias), 0, 0)


def intra_kernel(x_ref, s_ref, cum_ref, cumt_ref, dtt_ref, skip_ref, o_ref, reach_ref):
    tiles = BLOCK // 128
    lane_head = lax.broadcasted_iota(jnp.int32, cum_ref.shape, 1)
    row_head = lax.broadcasted_iota(jnp.int32, cumt_ref.shape, 0)
    lane = lax.broadcasted_iota(jnp.int32, (128, 128), 1)

    def pair(p, carry):
        off = pl.multiple_of(p * 128, 128)
        xp = x_ref[:, pl.ds(off, 128)]
        cum_all = cum_ref[...]
        cumt_all = cumt_ref[...]
        dtt_all = dtt_ref[...]
        cols, rows, dts = [], [], []
        for k in range(2):
            h = 2 * p + k
            cols.append(jnp.sum(jnp.where(lane_head == h, cum_all, 0.0), axis=1, keepdims=True))
            rows.append(jnp.sum(jnp.where(row_head == h, cumt_all, 0.0), axis=0, keepdims=True))
            dts.append(jnp.sum(jnp.where(row_head == h, dtt_all, 0.0), axis=0, keepdims=True))
        skip_p = skip_ref[:, pl.ds(off, 128)]
        pair_lane = lax.broadcasted_iota(jnp.int32, (BLOCK, 128), 1)
        reach_ref[:, pl.ds(off, 128)] = jnp.where(pair_lane < P_SIZE, jnp.exp(cols[0]), jnp.exp(cols[1]))
        for r in range(tiles):
            width = (r + 1) * 128
            s_tile = s_ref[r * 128 : width, 0:width]
            lower = lax.broadcasted_iota(jnp.int32, (128, width), 1) <= (
                lax.broadcasted_iota(jnp.int32, (128, width), 0) + r * 128
            )
            res = []
            for k in range(2):
                gap = cols[k][r * 128 : width] - rows[k][:, 0:width]
                decay = jnp.where(lower, jnp.exp(jnp.where(lower, gap, 0.0)), 0.0)
                w = (s_tile * decay * dts[k][:, 0:width]).astype(jnp.bfloat16)
                res.append(jnp.dot(w, xp[0:width], preferred_element_type=jnp.float32))
            out = jnp.where(lane < P_SIZE, res[0], res[1])
            o_ref[r * 128 : width, pl.ds(off, 128)] = out + skip_p * xp[r * 128 : width].astype(jnp.float32)
        return carry

    lax.fori_loop(0, x_ref.shape[1] // 128, pair, 0)


def intra_block(x, scores, cum, dt, skip_cols):
    heads = cum.shape[1]
    width = x.shape[1]
    cum_lanes = jnp.pad(cum, ((0, 0), (0, 128 - heads)))
    pad_rows = (-heads) % 8
    cum_rows = jnp.pad(cum.T, ((0, pad_rows), (0, 0)))
    dt_rows = jnp.pad(dt.T, ((0, pad_rows), (0, 0)))
    vmem = pl.BlockSpec(memory_space=pltpu.VMEM)
    return pl.pallas_call(
        intra_kernel,
        out_shape=(
            jax.ShapeDtypeStruct((BLOCK, width), jnp.float32),
            jax.ShapeDtypeStruct((BLOCK, width), jnp.float32),
        ),
        in_specs=[vmem] * 6,
        out_specs=(vmem, vmem),
        name="ssd_intra",
        cost_estimate=pl.CostEstimate(
            flops=2 * BLOCK * BLOCK * width * 2,
            transcendentals=heads * BLOCK * BLOCK,
            bytes_accessed=BLOCK * width * 6 + BLOCK * BLOCK * 4,
        ),
    )(x, scores, cum_lanes, cum_rows, dt_rows, skip_cols[None, :])


def fresh_kernel(x_ref, bt_ref, fac_ref, o_ref):
    def pair(p, carry):
        off = pl.multiple_of(p * 128, 128)
        xp = x_ref[:, pl.ds(off, 128)].astype(jnp.float32)
        wx = (fac_ref[:, pl.ds(off, 128)] * xp).astype(jnp.bfloat16)
        o_ref[:, pl.ds(off, 128)] = jnp.dot(bt_ref[...], wx, preferred_element_type=jnp.float32)
        return carry

    lax.fori_loop(0, x_ref.shape[1] // 128, pair, 0)


def fresh_block(x, b, cum, dt):
    heads = cum.shape[1]
    width = x.shape[1]
    factors = head_columns(jnp.exp(cum[BLOCK - 1 :] - cum) * dt)
    vmem = pl.BlockSpec(memory_space=pltpu.VMEM)
    return pl.pallas_call(
        fresh_kernel,
        out_shape=jax.ShapeDtypeStruct((N, width), jnp.float32),
        in_specs=[vmem] * 3,
        out_specs=vmem,
        name="ssd_fresh",
        cost_estimate=pl.CostEstimate(
            flops=2 * BLOCK * N * width,
            transcendentals=0,
            bytes_accessed=BLOCK * width * 6 + N * width * 4 + BLOCK * N * 2,
        ),
    )(x, b.T, factors)


def head_columns(head_major):
    return jnp.repeat(head_major, P_SIZE, axis=-1)


def on_device(
    x_in,
    bc_in,
    dt_in,
    conv_x_weight,
    conv_x_bias,
    conv_bc_weight,
    conv_bc_bias,
    dt_bias,
    a_log,
    skip,
):
    n_tp = lax.axis_size("tp")
    tp_index = lax.axis_index("tp")
    n_ctx = lax.axis_size("ctx")
    ctx_index = lax.axis_index("ctx")
    rows = x_in.shape[0]
    local_heads = H // n_tp
    head_width = local_heads * P_SIZE
    per_group = H // G
    rim = CONV - 1

    prior = from_behind(
        jnp.concatenate([x_in[rows - rim :], bc_in[rows - rim :]], axis=1), ("ctx", "tp"), 1
    )
    prior_x, prior_bc = prior[:, : x_in.shape[1]], prior[:, x_in.shape[1] :]
    x_part = conv_silu(x_in, prior_x, conv_x_weight, conv_x_bias)
    bc_part = conv_silu(bc_in, prior_bc, conv_bc_weight, conv_bc_bias)

    group_of = [(k * local_heads) // per_group for k in range(n_tp)]
    bc_groups = bc_part.reshape(rows, 2, G, N)
    if group_of != list(range(G)):
        bc_groups = jnp.take(bc_groups, np.array(group_of), axis=2)
    bc_groups = jnp.transpose(bc_groups, (2, 0, 1, 3))
    seg_bc = lax.all_to_all(bc_groups, "tp", split_axis=0, concat_axis=0, tiled=True)
    seg_bc = seg_bc.reshape(n_tp * rows, 2, N)
    seg_x = lax.all_to_all(x_part, "tp", split_axis=1, concat_axis=0, tiled=True)
    seg_dt = lax.all_to_all(dt_in, "tp", split_axis=1, concat_axis=0, tiled=True)
    seg_len = seg_x.shape[0]
    blocks = seg_len // BLOCK
    seg_b = seg_bc[:, 0].reshape(blocks, BLOCK, N)
    seg_c = seg_bc[:, 1].reshape(blocks, BLOCK, N)

    bias_local = lax.dynamic_slice_in_dim(dt_bias, tp_index * local_heads, local_heads, 0)
    rate_local = lax.dynamic_slice_in_dim(a_log, tp_index * local_heads, local_heads, 0)
    skip_local = lax.dynamic_slice_in_dim(skip, tp_index * local_heads, local_heads, 0)
    step_size = jax.nn.softplus(seg_dt.astype(jnp.float32) + bias_local[None, :])
    log_decay = -step_size * jnp.exp(rate_local)[None, :]

    dt_blk = step_size.reshape(blocks, BLOCK, local_heads)
    cum = jnp.cumsum(log_decay.reshape(blocks, BLOCK, local_heads), axis=1)
    last = cum[:, -1]
    x_blk = seg_x.reshape(blocks, BLOCK, head_width)

    fresh = [fresh_block(x_blk[b], seg_b[b], cum[b], dt_blk[b]) for b in range(blocks)]
    block_decay = jnp.exp(last)
    starts = [None]
    state = fresh[0]
    prefix = [jnp.ones((local_heads,), jnp.float32)]
    for b in range(1, blocks):
        starts.append(state)
        prefix.append(prefix[-1] * block_decay[b - 1])
        state = head_columns(block_decay[b])[None, :] * state + fresh[b]
    final = state
    segment_decay = prefix[-1] * block_decay[blocks - 1]

    core = ctx_index % 2
    chip = ctx_index // 2
    chips = n_ctx // 2
    half_width = head_width // 2
    half_heads = local_heads // 2
    decay_slab = jnp.pad(segment_decay[None, :], ((0, 7), (0, head_width - local_heads)))
    mate = lax.ppermute(
        jnp.concatenate([final, decay_slab], axis=0), "ctx", [(i, i ^ 1) for i in range(n_ctx)]
    )
    mate_final = mate[:N]
    even_final = jnp.where(core == 0, final, mate_final)
    odd_final = jnp.where(core == 0, mate_final, final)
    odd_decay = jnp.where(core == 0, mate[N, :local_heads], segment_decay)
    lo = core * half_width
    chip_half = head_columns(lax.dynamic_slice_in_dim(odd_decay, core * half_heads, half_heads, 0))[
        None, :
    ] * lax.dynamic_slice_in_dim(even_final, lo, half_width, 1) + lax.dynamic_slice_in_dim(
        odd_final, lo, half_width, 1
    )
    mate_decay = mate[N, :local_heads]
    chip_decay = head_columns(
        lax.dynamic_slice_in_dim(segment_decay * mate_decay, core * half_heads, half_heads, 0)
    )[None, :]
    pieces = 2 if N % 16 == 0 else 1
    piece_rows = N // pieces
    acc = [jnp.zeros((piece_rows, half_width), jnp.float32) for _ in range(pieces)]
    skip_cols = head_columns(skip_local)
    scores = [
        jnp.einsum("in,jn->ij", seg_c[b], seg_b[b], preferred_element_type=jnp.float32)
        for b in range(blocks)
    ]

    def intra_after(tie):
        parts, reach = [], []
        for b in range(blocks):
            operands = (x_blk[b], scores[b], cum[b], dt_blk[b])
            if tie is not None:
                operands = lax.optimization_barrier(operands + (tie,))[:4]
            part, spread = intra_block(*operands, skip_cols)
            parts.append(part)
            reach.append(spread)
        return parts, reach

    partials = None
    last_send = None
    for r in range(chips - 1):
        if r == chips - 2 and r >= 1:
            partials, reach = intra_after(last_send)
            acc = list(lax.optimization_barrier((tuple(acc), partials, reach))[0])
        pairs = [(2 * r + q, 2 * r + 2 + q) for q in range(2)]
        for k in range(pieces):
            send = chip_decay * acc[k] + chip_half[k * piece_rows : (k + 1) * piece_rows]
            acc[k] = acc[k] + lax.ppermute(send, "ctx", pairs)
            last_send = send
    if partials is None:
        partials, reach = intra_after(last_send)
    prefix_half = jnp.concatenate(acc, axis=0) if pieces > 1 else acc[0]
    mate_prefix = lax.ppermute(prefix_half, "ctx", [(i, i ^ 1) for i in range(n_ctx)])
    chip_prefix = jnp.concatenate(
        [jnp.where(core == 0, prefix_half, mate_prefix), jnp.where(core == 0, mate_prefix, prefix_half)],
        axis=1,
    )
    incoming = jnp.where(
        core == 1, head_columns(mate_decay)[None, :] * chip_prefix + mate_final, chip_prefix
    )

    results = []
    for b in range(blocks):
        carried_state = head_columns(prefix[b])[None, :] * incoming
        if starts[b] is not None:
            carried_state = starts[b] + carried_state
        state_hi = lax.reduce_precision(carried_state, exponent_bits=8, mantissa_bits=7)
        state_lo = (carried_state - state_hi).astype(jnp.bfloat16)
        projected = jnp.dot(
            seg_c[b], state_hi.astype(jnp.bfloat16), preferred_element_type=jnp.float32
        ) + jnp.dot(seg_c[b], state_lo, preferred_element_type=jnp.float32)
        inter = reach[b] * projected
        results.append((partials[b] + inter).astype(jnp.bfloat16))
    result = jnp.concatenate(results, axis=0) if blocks > 1 else results[0]
    return lax.all_to_all(result, "tp", split_axis=0, concat_axis=1, tiled=True)


def solution(mesh):
    return jax.shard_map(
        on_device,
        mesh=mesh,
        in_specs=(
            P(("ctx", "tp"), None),
            P(("ctx", "tp"), None),
            P(("ctx", "tp"), None),
            P(),
            P(),
            P(),
            P(),
            P(),
            P(),
            P(),
        ),
        out_specs=P(("ctx", "tp"), None),
        check_vma=False,
    )
```

```python
import numpy as np
import jax
import jax.numpy as jnp
from jax import lax
from jax.sharding import PartitionSpec as P
from jax.experimental import pallas as pl
from jax.experimental.pallas import tpu as pltpu

H = 128
P_SIZE = 64
N = 256
G = 4
CONV = 4
BLOCK = 512


def from_behind(value, axis, steps):
    count = lax.axis_size(axis)
    initial, last = (max(0, -steps), min(count, count - steps))
    return lax.ppermute(value, axis, [(source, source + steps) for source in range(initial, last)])


def conv_rows(full, rows, weight, bias):
    total = bias[None, :] + weight[0][None, :] * full[0:rows]
    for k in range(1, CONV):
        total = total + weight[k][None, :] * full[k : k + rows]
    return jax.nn.silu(total).astype(jnp.bfloat16)


def conv_silu(raw, prior, weight, bias):
    rows = raw.shape[0]
    rim = CONV - 1
    zero_prior = jnp.zeros((rim, raw.shape[1]), jnp.float32)
    body = conv_rows(jnp.concatenate([zero_prior, raw.astype(jnp.float32)], axis=0), rows, weight, bias)
    edge = jnp.concatenate([prior, raw[:rim]], axis=0).astype(jnp.float32)
    return lax.dynamic_update_slice_in_dim(body, conv_rows(edge, rim, weight, bias), 0, 0)


def intra_kernel(x_ref, s_ref, cum_ref, cumt_ref, dtt_ref, skip_ref, o_ref, reach_ref):
    tiles = BLOCK // 128
    lane_head = lax.broadcasted_iota(jnp.int32, cum_ref.shape, 1)
    row_head = lax.broadcasted_iota(jnp.int32, cumt_ref.shape, 0)
    lane = lax.broadcasted_iota(jnp.int32, (128, 128), 1)

    def pair(p, carry):
        off = pl.multiple_of(p * 128, 128)
        xp = x_ref[:, pl.ds(off, 128)]
        cum_all = cum_ref[...]
        cumt_all = cumt_ref[...]
        dtt_all = dtt_ref[...]
        cols, rows, dts = [], [], []
        for k in range(2):
            h = 2 * p + k
            cols.append(jnp.sum(jnp.where(lane_head == h, cum_all, 0.0), axis=1, keepdims=True))
            rows.append(jnp.sum(jnp.where(row_head == h, cumt_all, 0.0), axis=0, keepdims=True))
            dts.append(jnp.sum(jnp.where(row_head == h, dtt_all, 0.0), axis=0, keepdims=True))
        skip_p = skip_ref[:, pl.ds(off, 128)]
        pair_lane = lax.broadcasted_iota(jnp.int32, (BLOCK, 128), 1)
        reach_ref[:, pl.ds(off, 128)] = jnp.where(pair_lane < P_SIZE, jnp.exp(cols[0]), jnp.exp(cols[1]))
        for r in range(tiles):
            width = (r + 1) * 128
            s_tile = s_ref[r * 128 : width, 0:width]
            lower = lax.broadcasted_iota(jnp.int32, (128, width), 1) <= (
                lax.broadcasted_iota(jnp.int32, (128, width), 0) + r * 128
            )
            res = []
            for k in range(2):
                gap = cols[k][r * 128 : width] - rows[k][:, 0:width]
                decay = jnp.where(lower, jnp.exp(jnp.where(lower, gap, 0.0)), 0.0)
                w = (s_tile * decay * dts[k][:, 0:width]).astype(jnp.bfloat16)
                res.append(jnp.dot(w, xp[0:width], preferred_element_type=jnp.float32))
            out = jnp.where(lane < P_SIZE, res[0], res[1])
            o_ref[r * 128 : width, pl.ds(off, 128)] = out + skip_p * xp[r * 128 : width].astype(jnp.float32)
        return carry

    lax.fori_loop(0, x_ref.shape[1] // 128, pair, 0)


def intra_block(x, scores, cum, dt, skip_cols):
    heads = cum.shape[1]
    width = x.shape[1]
    cum_lanes = jnp.pad(cum, ((0, 0), (0, 128 - heads)))
    pad_rows = (-heads) % 8
    cum_rows = jnp.pad(cum.T, ((0, pad_rows), (0, 0)))
    dt_rows = jnp.pad(dt.T, ((0, pad_rows), (0, 0)))
    vmem = pl.BlockSpec(memory_space=pltpu.VMEM)
    return pl.pallas_call(
        intra_kernel,
        out_shape=(
            jax.ShapeDtypeStruct((BLOCK, width), jnp.float32),
            jax.ShapeDtypeStruct((BLOCK, width), jnp.float32),
        ),
        in_specs=[vmem] * 6,
        out_specs=(vmem, vmem),
        name="ssd_intra",
        cost_estimate=pl.CostEstimate(
            flops=2 * BLOCK * BLOCK * width * 2,
            transcendentals=heads * BLOCK * BLOCK,
            bytes_accessed=BLOCK * width * 6 + BLOCK * BLOCK * 4,
        ),
    )(x, scores, cum_lanes, cum_rows, dt_rows, skip_cols[None, :])


def fresh_kernel(x_ref, bt_ref, fac_ref, o_ref):
    def pair(p, carry):
        off = pl.multiple_of(p * 128, 128)
        xp = x_ref[:, pl.ds(off, 128)].astype(jnp.float32)
        wx = (fac_ref[:, pl.ds(off, 128)] * xp).astype(jnp.bfloat16)
        o_ref[:, pl.ds(off, 128)] = jnp.dot(bt_ref[...], wx, preferred_element_type=jnp.float32)
        return carry

    lax.fori_loop(0, x_ref.shape[1] // 128, pair, 0)


def fresh_block(x, b, cum, dt):
    heads = cum.shape[1]
    width = x.shape[1]
    factors = head_columns(jnp.exp(cum[BLOCK - 1 :] - cum) * dt)
    vmem = pl.BlockSpec(memory_space=pltpu.VMEM)
    return pl.pallas_call(
        fresh_kernel,
        out_shape=jax.ShapeDtypeStruct((N, width), jnp.float32),
        in_specs=[vmem] * 3,
        out_specs=vmem,
        name="ssd_fresh",
        cost_estimate=pl.CostEstimate(
            flops=2 * BLOCK * N * width,
            transcendentals=0,
            bytes_accessed=BLOCK * width * 6 + N * width * 4 + BLOCK * N * 2,
        ),
    )(x, b.T, factors)


def head_columns(head_major):
    return jnp.repeat(head_major, P_SIZE, axis=-1)


def on_device(
    x_in,
    bc_in,
    dt_in,
    conv_x_weight,
    conv_x_bias,
    conv_bc_weight,
    conv_bc_bias,
    dt_bias,
    a_log,
    skip,
):
    n_tp = lax.axis_size("tp")
    tp_index = lax.axis_index("tp")
    n_ctx = lax.axis_size("ctx")
    ctx_index = lax.axis_index("ctx")
    rows = x_in.shape[0]
    local_heads = H // n_tp
    head_width = local_heads * P_SIZE
    per_group = H // G
    rim = CONV - 1

    prior = from_behind(
        jnp.concatenate([x_in[rows - rim :], bc_in[rows - rim :]], axis=1), ("ctx", "tp"), 1
    )
    prior_x, prior_bc = prior[:, : x_in.shape[1]], prior[:, x_in.shape[1] :]
    x_part = conv_silu(x_in, prior_x, conv_x_weight, conv_x_bias)
    bc_part = conv_silu(bc_in, prior_bc, conv_bc_weight, conv_bc_bias)

    group_of = [(k * local_heads) // per_group for k in range(n_tp)]
    bc_groups = bc_part.reshape(rows, 2, G, N)
    if group_of != list(range(G)):
        bc_groups = jnp.take(bc_groups, np.array(group_of), axis=2)
    bc_groups = jnp.transpose(bc_groups, (2, 0, 1, 3))
    seg_bc = lax.all_to_all(bc_groups, "tp", split_axis=0, concat_axis=0, tiled=True)
    seg_bc = seg_bc.reshape(n_tp * rows, 2, N)
    seg_x = lax.all_to_all(x_part, "tp", split_axis=1, concat_axis=0, tiled=True)
    seg_dt = lax.all_to_all(dt_in, "tp", split_axis=1, concat_axis=0, tiled=True)
    seg_len = seg_x.shape[0]
    blocks = seg_len // BLOCK
    seg_b = seg_bc[:, 0].reshape(blocks, BLOCK, N)
    seg_c = seg_bc[:, 1].reshape(blocks, BLOCK, N)

    bias_local = lax.dynamic_slice_in_dim(dt_bias, tp_index * local_heads, local_heads, 0)
    rate_local = lax.dynamic_slice_in_dim(a_log, tp_index * local_heads, local_heads, 0)
    skip_local = lax.dynamic_slice_in_dim(skip, tp_index * local_heads, local_heads, 0)
    step_size = jax.nn.softplus(seg_dt.astype(jnp.float32) + bias_local[None, :])
    log_decay = -step_size * jnp.exp(rate_local)[None, :]

    dt_blk = step_size.reshape(blocks, BLOCK, local_heads)
    cum = jnp.cumsum(log_decay.reshape(blocks, BLOCK, local_heads), axis=1)
    last = cum[:, -1]
    x_blk = seg_x.reshape(blocks, BLOCK, head_width)

    fresh = [fresh_block(x_blk[b], seg_b[b], cum[b], dt_blk[b]) for b in range(blocks)]
    block_decay = jnp.exp(last)
    starts = [None]
    state = fresh[0]
    prefix = [jnp.ones((local_heads,), jnp.float32)]
    for b in range(1, blocks):
        starts.append(state)
        prefix.append(prefix[-1] * block_decay[b - 1])
        state = head_columns(block_decay[b])[None, :] * state + fresh[b]
    final = state
    segment_decay = prefix[-1] * block_decay[blocks - 1]

    core = ctx_index % 2
    chip = ctx_index // 2
    chips = n_ctx // 2
    half_width = head_width // 2
    half_heads = local_heads // 2
    decay_slab = jnp.pad(segment_decay[None, :], ((0, 7), (0, head_width - local_heads)))
    mate = lax.ppermute(
        jnp.concatenate([final, decay_slab], axis=0), "ctx", [(i, i ^ 1) for i in range(n_ctx)]
    )
    mate_final = mate[:N]
    even_final = jnp.where(core == 0, final, mate_final)
    odd_final = jnp.where(core == 0, mate_final, final)
    odd_decay = jnp.where(core == 0, mate[N, :local_heads], segment_decay)
    lo = core * half_width
    chip_half = head_columns(lax.dynamic_slice_in_dim(odd_decay, core * half_heads, half_heads, 0))[
        None, :
    ] * lax.dynamic_slice_in_dim(even_final, lo, half_width, 1) + lax.dynamic_slice_in_dim(
        odd_final, lo, half_width, 1
    )
    mate_decay = mate[N, :local_heads]
    chip_decay = head_columns(
        lax.dynamic_slice_in_dim(segment_decay * mate_decay, core * half_heads, half_heads, 0)
    )[None, :]
    pieces = 1
    piece_rows = N // pieces
    acc = [jnp.zeros((piece_rows, half_width), jnp.float32) for _ in range(pieces)]
    skip_cols = head_columns(skip_local)
    scores = [
        jnp.einsum("in,jn->ij", seg_c[b], seg_b[b], preferred_element_type=jnp.float32)
        for b in range(blocks)
    ]

    def intra_after(tie):
        parts, reach = [], []
        for b in range(blocks):
            operands = (x_blk[b], scores[b], cum[b], dt_blk[b])
            if tie is not None:
                operands = lax.optimization_barrier(operands + (tie,))[:4]
            part, spread = intra_block(*operands, skip_cols)
            parts.append(part)
            reach.append(spread)
        return parts, reach

    partials = None
    last_send = None
    for r in range(chips - 1):
        if r == chips - 2 and r >= 1:
            partials, reach = intra_after(last_send)
            acc = list(lax.optimization_barrier((tuple(acc), partials, reach))[0])
        pairs = [(2 * r + q, 2 * r + 2 + q) for q in range(2)]
        for k in range(pieces):
            send = chip_decay * acc[k] + chip_half[k * piece_rows : (k + 1) * piece_rows]
            acc[k] = acc[k] + lax.ppermute(send, "ctx", pairs)
            last_send = send
    if partials is None:
        partials, reach = intra_after(last_send)
    prefix_half = jnp.concatenate(acc, axis=0) if pieces > 1 else acc[0]
    mate_prefix = lax.ppermute(prefix_half, "ctx", [(i, i ^ 1) for i in range(n_ctx)])
    chip_prefix = jnp.concatenate(
        [jnp.where(core == 0, prefix_half, mate_prefix), jnp.where(core == 0, mate_prefix, prefix_half)],
        axis=1,
    )
    incoming = jnp.where(
        core == 1, head_columns(mate_decay)[None, :] * chip_prefix + mate_final, chip_prefix
    )

    results = []
    for b in range(blocks):
        carried_state = head_columns(prefix[b])[None, :] * incoming
        if starts[b] is not None:
            carried_state = starts[b] + carried_state
        state_hi = lax.reduce_precision(carried_state, exponent_bits=8, mantissa_bits=7)
        state_lo = (carried_state - state_hi).astype(jnp.bfloat16)
        projected = jnp.dot(
            seg_c[b], state_hi.astype(jnp.bfloat16), preferred_element_type=jnp.float32
        ) + jnp.dot(seg_c[b], state_lo, preferred_element_type=jnp.float32)
        inter = reach[b] * projected
        results.append((partials[b] + inter).astype(jnp.bfloat16))
    result = jnp.concatenate(results, axis=0) if blocks > 1 else results[0]
    return lax.all_to_all(result, "tp", split_axis=0, concat_axis=1, tiled=True)


def solution(mesh):
    return jax.shard_map(
        on_device,
        mesh=mesh,
        in_specs=(
            P(("ctx", "tp"), None),
            P(("ctx", "tp"), None),
            P(("ctx", "tp"), None),
            P(),
            P(),
            P(),
            P(),
            P(),
            P(),
            P(),
        ),
        out_specs=P(("ctx", "tp"), None),
        check_vma=False,
    )
```
